32 devices in a mesh: tile: 8 (over y, x, core), mem: 4 (over z).
Axes of the slice: x: 2, y: 2, z: 4, core: 2. Of those that a mesh axis runs over, the one named last changes fastest.
Arguments:
- control: bfloat16 [80, 1, 360, 720], P('mem', None, 'tile'), may hold values from -6 to 6
- perturb: bfloat16 [80, 1, 360, 720], P('mem', None, 'tile'), may hold values from -6 to 6
- lon_taps: bfloat16 [17], replicated, may hold values from 0.026367188 to 0.07910156
- lat_taps: bfloat16 [17], replicated, may hold values from 0.026367188 to 0.07910156
- innov: float32 [8, 8, 256], P('tile'), may hold values from -6 to 6
- inv_var: float32 [8, 8, 256], P('tile'), may hold values from 1 to 8
- cell_index: int32 [8, 8, 256], P('tile'), may hold values from 0 to 32399, as said below
- counts: int32 [8, 8], P('tile'), may hold values from 0 to 256, as said below
Outputs:
- gradient: float32 [80, 1, 360, 720], P('mem', None, 'tile')
The draws below stay inside these ranges and needn't reach their ends.
Inputs may be any that keep to these rules, and one draw needn't show every extreme that they name: `cell_index`: an observation's cell within its owning tile, level * 45 * 720 + longitude within the tile * 720 + latitude; both ends are taken. `counts`: live slots per pair of tiles; some pair fills all 256 slots in every draw, and some owning tiles receive far more than others.
All inputs are finite; a program needn't handle non-finite values.
Results may differ from the reference program's by a relative error of at most 0.00066.
Values may be sent and summed in bfloat16 or wider, within the bound.
No kernel may reach another device: no remote copies, remote signals or barrier semaphores. Data moves between devices by JAX's collectives and lax.ppermute only.
A program may use at most 64 MiB of HBM per device.

```python
import math
import jax
import jax.numpy as jnp
from jax import lax

LEV = 1
LON_DEV = 45
LAT = 720
RAD = 16
CAP = 256
TILES = 8
LON = 360
MEMBERS = 80
CELLS = 32400


def draw_cell_index(key, part):
    total_cells = LEV * LON_DEV * LAT
    drawn = jax.random.randint(key, (TILES, TILES, CAP), 0, total_cells, dtype=jnp.int32)
    drawn = drawn.at[0, 0, 0].set(0)
    return drawn.at[TILES - 1, TILES - 1, CAP - 1].set(total_cells - 1)


def draw_counts(key, part):
    raw_key = jax.random.fold_in(key, 11)
    level_key = jax.random.fold_in(key, 12)
    source_key = jax.random.fold_in(key, 13)
    target_key = jax.random.fold_in(key, 14)
    raw_counts = jax.random.randint(raw_key, (TILES, TILES), 0, CAP + 1, dtype=jnp.int32)
    levels_drawn = jax.random.randint(level_key, (TILES,), 0, 4, dtype=jnp.int32)
    density = jnp.array([1, 2, 4, 8], dtype=jnp.int32)[levels_drawn]
    scaled = jnp.minimum(raw_counts * density[None, :] // 4, CAP)
    heavy_source = jax.random.randint(source_key, (), 0, TILES, dtype=jnp.int32)
    heavy_target = jax.random.randint(target_key, (), 0, TILES, dtype=jnp.int32)
    return scaled.at[heavy_source, heavy_target].set(CAP)


def level_of(own_key, extent, shards, smallest, top_value):
    level, own = 1.0, jax.random.fold_in(own_key, 6)
    for dim, shards_of in shards:
        heights = jnp.exp(jax.random.uniform(jax.random.fold_in(own, dim), (shards_of,), jnp.float32, smallest / len(shards), top_value / len(shards)))
        level = level * jnp.repeat(heights, extent[dim] // shards_of).reshape([-1 if axis == dim else 1 for axis in range(len(extent))])
    return level


def gaussian(rng, extent, scale, reach, split=(), kind=jnp.bfloat16):
    values = jax.random.normal(rng, extent, jnp.float32) * scale
    if len(split) > 0:
        values = level_of(rng, extent, split, -0.22, 0.18) * values
    return jnp.clip(values, min=-reach, max=reach).astype(kind)


def setup_inputs(seed: int = 0) -> dict:
    key_of = jax.random.split(jax.random.key(seed), 9)
    control = gaussian(key_of[0], (MEMBERS, LEV, LON, LAT), 1.0, 6.0, ((0, 4), (2, 8)))
    perturb = gaussian(key_of[1], (MEMBERS, LEV, LON, LAT), 1.0, 6.0, ((0, 4), (2, 8)))
    lon_taps = jnp.clip(jax.random.uniform(key_of[2], (RAD + 1,), jnp.float32, 0.026367188, 0.07910156), 0.026367188, 0.07910156).astype(jnp.bfloat16)
    lat_taps = jnp.clip(jax.random.uniform(key_of[3], (RAD + 1,), jnp.float32, 0.026367188, 0.07910156), 0.026367188, 0.07910156).astype(jnp.bfloat16)
    innov = gaussian(key_of[4], (TILES, TILES, CAP), 1.0, 6.0, ((0, 8),), jnp.float32)
    inv_var = jnp.clip(jnp.exp(math.log(8.0) - 2.0794415 * jax.random.uniform(key_of[5], (TILES, TILES, CAP), jnp.float32) ** level_of(key_of[5], (TILES, TILES, CAP), ((0, 8),), -0.2, 0.2)), 1.0, 8.0)
    cell_index = draw_cell_index(jax.random.fold_in(key_of[8], 71), 0)
    counts = draw_counts(jax.random.fold_in(key_of[8], 71), 0)
    return dict(control=control, perturb=perturb, lon_taps=lon_taps, lat_taps=lat_taps, innov=innov, inv_var=inv_var, cell_index=cell_index, counts=counts)


def along_lon(grid_field, tap_weights):
    taps = tap_weights.astype(jnp.float32)
    field = grid_field.astype(jnp.float32)
    result = taps[0] * field
    for offset in range(1, RAD + 1):
        result = result + taps[offset] * (jnp.roll(field, offset, axis=-2) + jnp.roll(field, -offset, axis=-2))
    return result.astype(jnp.bfloat16)


def along_lat(grid_field, tap_weights):
    taps = tap_weights.astype(jnp.float32)
    field = grid_field.astype(jnp.float32)
    padded = jnp.pad(field, ((0, 0), (0, 0), (RAD, RAD)))
    result = taps[0] * field
    for offset in range(1, RAD + 1):
        result = result + taps[offset] * (padded[:, :, RAD + offset:RAD + offset + LAT] + padded[:, :, RAD - offset:RAD - offset + LAT])
    return result


def reference(control, perturb, lon_taps, lat_taps, innov, inv_var, cell_index, counts):
    def forward(running, member_pair):
        member, member_pert = member_pair
        smoothed = along_lat(along_lon(member, lon_taps), lat_taps)
        return running + member_pert.astype(jnp.float32) * smoothed, None

    increment, _ = lax.scan(forward, jnp.zeros((LEV, LON, LAT), jnp.float32), (control, perturb))
    by_tile = increment.reshape(LEV, TILES, LON_DEV, LAT).transpose(1, 0, 2, 3).reshape(TILES, CELLS)
    targets = cell_index.transpose(1, 0, 2).reshape(TILES, TILES * CAP).astype(jnp.int32)
    slot_ids = jnp.arange(CAP, dtype=jnp.int32)
    is_live = slot_ids[None, None, :] < counts[:, :, None]
    weights = jnp.where(is_live, inv_var, jnp.zeros_like(inv_var)).transpose(1, 0, 2).reshape(TILES, TILES * CAP)
    observed = innov.transpose(1, 0, 2).reshape(TILES, TILES * CAP)
    picked = jnp.take_along_axis(by_tile, targets, axis=1)
    misfit = weights * (picked - observed)

    def spread_tile(values, positions):
        return jnp.zeros((CELLS,), misfit.dtype).at[positions].add(values)

    spread = jax.vmap(spread_tile)(misfit, targets)
    spread = spread.reshape(TILES, LEV, LON_DEV, LAT).transpose(1, 0, 2, 3).reshape(LEV, LON, LAT)

    def backward(member_pair):
        member, member_pert = member_pair
        weighted = (member_pert.astype(jnp.float32) * spread).astype(jnp.bfloat16)
        return member.astype(jnp.float32) + along_lat(along_lon(weighted, lon_taps), lat_taps)

    return lax.map(backward, (control, perturb))
```

```python
import math

import jax
import jax.numpy as jnp
from jax import lax
from jax.experimental import pallas as pl
from jax.experimental.pallas import tpu as pltpu
from jax.sharding import PartitionSpec as P


def halos(block, axis, dim, width):
    count = lax.axis_size(axis)
    forward = [(i, (i + 1) % count) for i in range(count)]
    backward = [((i + 1) % count, i) for i in range(count)]
    low = lax.ppermute(
        lax.slice_in_dim(block, block.shape[dim] - width, None, axis=dim), axis, forward
    )
    high = lax.ppermute(lax.slice_in_dim(block, 0, width, axis=dim), axis, backward)
    return low, high


def extend(block, low, high, dim, padded):
    pad_shape = list(block.shape)
    pad_shape[dim] = padded - block.shape[dim]
    parts = [block]
    if pad_shape[dim] > 0:
        parts.append(jnp.zeros(pad_shape, block.dtype))
    return jnp.concatenate(parts + [low, high], axis=dim)


def lon_band(tap_weights, lon_cells, padded):
    radius = tap_weights.shape[0] - 1
    taps = tap_weights.astype(jnp.float32)
    ext_cells = padded + 2 * radius
    rows = lax.broadcasted_iota(jnp.int32, (padded, ext_cells), 0)
    cols = lax.broadcasted_iota(jnp.int32, (padded, ext_cells), 1)
    source = jnp.where(
        cols < padded,
        cols,
        jnp.where(cols < padded + radius, cols - padded - radius, cols - padded - radius + lon_cells),
    )
    valid = (rows < lon_cells) & ((cols < lon_cells) | (cols >= padded))
    dist = jnp.abs(source - rows)
    band = jnp.where(valid & (dist <= radius), taps[jnp.minimum(dist, radius)], 0.0)
    return band.astype(jnp.bfloat16)


def lat_band(tap_weights, lat_cells):
    radius = tap_weights.shape[0] - 1
    taps = tap_weights.astype(jnp.float32)
    rows = lax.broadcasted_iota(jnp.int32, (lat_cells, lat_cells), 0)
    cols = lax.broadcasted_iota(jnp.int32, (lat_cells, lat_cells), 1)
    dist = jnp.abs(rows - cols)
    band = jnp.where(dist <= radius, taps[jnp.minimum(dist, radius)], 0.0)
    return band.astype(jnp.bfloat16)


def member_chunk(members):
    for size in (5, 4, 3, 2, 1):
        if members % size == 0:
            return size
    return 1


def forward_sum(ext_control, perturb, band_lon, band_lat):
    members, levels, ext_cells, lat_cells = ext_control.shape
    lon_cells = perturb.shape[2]
    padded = band_lon.shape[0]
    chunk = member_chunk(members)

    def kernel(ext_ref, pert_ref, blon_ref, blat_ref, out_ref, along_ref):
        step = pl.program_id(1)
        blon = blon_ref[...]
        for m in range(chunk):
            along = jnp.dot(blon, ext_ref[m], preferred_element_type=jnp.float32)
            along_ref[m * padded:(m + 1) * padded, :] = along.astype(jnp.bfloat16)
        smoothed = jnp.dot(along_ref[...], blat_ref[...], preferred_element_type=jnp.float32)
        total = pert_ref[0].astype(jnp.float32) * smoothed[0:lon_cells]
        for m in range(1, chunk):
            total = total + pert_ref[m].astype(jnp.float32) * smoothed[
                m * padded:m * padded + lon_cells
            ]

        @pl.when(step == 0)
        def _():
            out_ref[...] = total

        @pl.when(step > 0)
        def _():
            out_ref[...] = out_ref[...] + total

    return pl.pallas_call(
        kernel,
        grid=(levels, members // chunk),
        in_specs=[
            pl.BlockSpec((chunk, None, ext_cells, lat_cells), lambda l, g: (g, l, 0, 0)),
            pl.BlockSpec((chunk, None, lon_cells, lat_cells), lambda l, g: (g, l, 0, 0)),
            pl.BlockSpec(band_lon.shape, lambda l, g: (0, 0)),
            pl.BlockSpec(band_lat.shape, lambda l, g: (0, 0)),
        ],
        out_specs=pl.BlockSpec((None, lon_cells, lat_cells), lambda l, g: (l, 0, 0)),
        out_shape=jax.ShapeDtypeStruct((levels, lon_cells, lat_cells), jnp.float32),
        scratch_shapes=[pltpu.VMEM((chunk * padded, lat_cells), jnp.bfloat16)],
        compiler_params=pltpu.CompilerParams(dimension_semantics=("arbitrary", "arbitrary")),
    )(ext_control, perturb, band_lon, band_lat)


def backward_grad(ext_perturb, ext_spread, control, band_lon, band_lat):
    members, levels, ext_cells, lat_cells = ext_perturb.shape
    lon_cells = control.shape[2]
    padded = band_lon.shape[0]
    chunk = member_chunk(members)

    def kernel(pext_ref, spread_ref, ctrl_ref, blon_ref, blat_ref, out_ref, along_ref):
        blon = blon_ref[...]
        spread = spread_ref[...]
        for m in range(chunk):
            weighted = (pext_ref[m].astype(jnp.float32) * spread).astype(jnp.bfloat16)
            along = jnp.dot(blon, weighted, preferred_element_type=jnp.float32)
            along_ref[m * padded:(m + 1) * padded, :] = along.astype(jnp.bfloat16)
        smoothed = jnp.dot(along_ref[...], blat_ref[...], preferred_element_type=jnp.float32)
        for m in range(chunk):
            out_ref[m] = ctrl_ref[m].astype(jnp.float32) + smoothed[
                m * padded:m * padded + lon_cells
            ]

    return pl.pallas_call(
        kernel,
        grid=(levels, members // chunk),
        in_specs=[
            pl.BlockSpec((chunk, None, ext_cells, lat_cells), lambda l, g: (g, l, 0, 0)),
            pl.BlockSpec((None, ext_cells, lat_cells), lambda l, g: (l, 0, 0)),
            pl.BlockSpec((chunk, None, lon_cells, lat_cells), lambda l, g: (g, l, 0, 0)),
            pl.BlockSpec(band_lon.shape, lambda l, g: (0, 0)),
            pl.BlockSpec(band_lat.shape, lambda l, g: (0, 0)),
        ],
        out_specs=pl.BlockSpec((chunk, None, lon_cells, lat_cells), lambda l, g: (g, l, 0, 0)),
        out_shape=jax.ShapeDtypeStruct(control.shape, jnp.float32),
        scratch_shapes=[pltpu.VMEM((chunk * padded, lat_cells), jnp.bfloat16)],
        compiler_params=pltpu.CompilerParams(dimension_semantics=("parallel", "parallel")),
    )(ext_perturb, ext_spread, control, band_lon, band_lat)


def pick_cells(field_rows, row_index, col_index, block_rows):
    row_count, col_count = field_rows.shape
    field_cols = field_rows.T

    def pick_one_block(indices):
        rows_here, cols_here = indices
        onehot_rows = (
            rows_here[:, None] == jnp.arange(row_count, dtype=jnp.int32)[None, :]
        ).astype(jnp.float32)
        onehot_cols = (
            cols_here[:, None] == jnp.arange(col_count, dtype=jnp.int32)[None, :]
        ).astype(jnp.float32)
        picked = jnp.dot(
            onehot_cols,
            field_cols,
            precision=lax.Precision.HIGHEST,
            preferred_element_type=jnp.float32,
        )
        return jnp.sum(picked * onehot_rows, axis=1)

    values = lax.map(
        pick_one_block, (row_index.reshape(-1, block_rows), col_index.reshape(-1, block_rows))
    )
    return values.reshape(-1)


def spread_cells(misfit, row_index, col_index, row_count, col_count, block_rows):

    def spread_one_block(total, items):
        rows_here, cols_here, values = items
        onehot_rows = (
            rows_here[:, None] == jnp.arange(row_count, dtype=jnp.int32)[None, :]
        ).astype(jnp.float32)
        onehot_cols = (
            cols_here[:, None] == jnp.arange(col_count, dtype=jnp.int32)[None, :]
        ).astype(jnp.float32)
        weighted = onehot_rows * values[:, None]
        return (
            total
            + jnp.dot(
                weighted.T,
                onehot_cols,
                precision=lax.Precision.HIGHEST,
                preferred_element_type=jnp.float32,
            ),
            None,
        )

    start = jnp.zeros((row_count, col_count), jnp.float32)
    items = (
        row_index.reshape(-1, block_rows),
        col_index.reshape(-1, block_rows),
        misfit.reshape(-1, block_rows),
    )
    total, _ = lax.scan(spread_one_block, start, items)
    return total


def local(control, perturb, lon_taps, lat_taps, innov, inv_var, cell_index, counts):
    members_here, levels, lon_cells, lat_cells = control.shape
    radius = lon_taps.shape[0] - 1
    padded = -(-lon_cells // 16) * 16
    band_lon = lon_band(lon_taps, lon_cells, padded)
    band_lat = lat_band(lat_taps, lat_cells)

    slot_ids = lax.broadcasted_iota(jnp.int32, innov.shape, 2)
    weights = jnp.where(slot_ids < counts[:, :, None], inv_var, 0.0)
    lists = jnp.stack([innov, weights, cell_index.astype(jnp.float32)])
    received = lax.all_to_all(lists, "tile", split_axis=2, concat_axis=1, tiled=True)
    observed = received[0].reshape(-1)
    weight_recv = received[1].reshape(-1)
    cells_hit = received[2].reshape(-1).astype(jnp.int32)
    row_index = cells_hit // lat_cells
    col_index = cells_hit % lat_cells
    row_count = levels * lon_cells
    block_rows = math.gcd(observed.shape[0], 1024)

    c_low, c_high = halos(control, "tile", 2, radius)
    p_low, p_high = halos(perturb, "tile", 2, radius)
    ext_control = extend(control, c_low, c_high, 2, padded)
    member_sum = forward_sum(ext_control, perturb, band_lon, band_lat)
    partial = pick_cells(member_sum.reshape(row_count, lat_cells), row_index, col_index, block_rows)
    at_cells = lax.psum(partial, "mem")
    misfit = weight_recv * (at_cells - observed)
    spread = spread_cells(misfit, row_index, col_index, row_count, lat_cells, block_rows)
    spread = spread.reshape(levels, lon_cells, lat_cells)
    s_low, s_high = halos(spread, "tile", 1, radius)
    ext_spread = extend(spread, s_low, s_high, 1, padded)
    ext_perturb = extend(perturb, p_low, p_high, 2, padded)
    return backward_grad(ext_perturb, ext_spread, control, band_lon, band_lat)


def solution(mesh):
    return jax.shard_map(
        local,
        mesh=mesh,
        in_specs=(
            P("mem", None, "tile", None),
            P("mem", None, "tile", None),
            P(),
            P(),
            P("tile", None, None),
            P("tile", None, None),
            P("tile", None, None),
            P("tile", None),
        ),
        out_specs=P("mem", None, "tile", None),
        check_vma=False,
    )
```

```python
import math

import jax
import jax.numpy as jnp
from jax import lax
from jax.experimental import pallas as pl
from jax.experimental.pallas import tpu as pltpu
from jax.sharding import PartitionSpec as P


def halos(block, axis, dim, width):
    count = lax.axis_size(axis)
    forward = [(i, (i + 1) % count) for i in range(count)]
    backward = [((i + 1) % count, i) for i in range(count)]
    low = lax.ppermute(
        lax.slice_in_dim(block, block.shape[dim] - width, None, axis=dim), axis, forward
    )
    high = lax.ppermute(lax.slice_in_dim(block, 0, width, axis=dim), axis, backward)
    return low, high


def lon_band(tap_weights, lon_cells, padded):
    radius = tap_weights.shape[0] - 1
    taps = tap_weights.astype(jnp.float32)
    ext_cells = padded + 2 * radius
    rows = lax.broadcasted_iota(jnp.int32, (padded, ext_cells), 0)
    cols = lax.broadcasted_iota(jnp.int32, (padded, ext_cells), 1)
    source = jnp.where(
        cols < padded,
        cols,
        jnp.where(cols < padded + radius, cols - padded - radius, cols - padded - radius + lon_cells),
    )
    valid = (rows < lon_cells) & ((cols < lon_cells) | (cols >= padded))
    dist = jnp.abs(source - rows)
    dist = jnp.where(valid, dist, radius + 1)
    return band_from(dist, taps)


def band_from(dist, taps):
    band = jnp.zeros(dist.shape, jnp.float32)
    for offset in range(taps.shape[0]):
        band = jnp.where(dist == offset, taps[offset], band)
    return band.astype(jnp.bfloat16)


def lat_band(tap_weights, lat_cells):
    radius = tap_weights.shape[0] - 1
    taps = tap_weights.astype(jnp.float32)
    rows = lax.broadcasted_iota(jnp.int32, (lat_cells, lat_cells), 0)
    cols = lax.broadcasted_iota(jnp.int32, (lat_cells, lat_cells), 1)
    return band_from(jnp.abs(rows - cols), taps)


def member_chunk(members):
    for size in (5, 4, 3, 2, 1):
        if members % size == 0:
            return size
    return 1


def fill_ext(ext_ref, local, low, high, lon_cells, padded):
    radius = low.shape[0]
    base = (lon_cells // 16) * 16
    ext_ref[base:padded, :] = jnp.zeros((padded - base, ext_ref.shape[1]), ext_ref.dtype)
    ext_ref[0:lon_cells, :] = local
    ext_ref[padded:padded + radius, :] = low
    ext_ref[padded + radius:padded + 2 * radius, :] = high


def forward_sum(control, c_low, c_high, perturb, band_lon, band_lat):
    members, levels, lon_cells, lat_cells = control.shape
    radius = c_low.shape[2]
    padded, ext_cells = band_lon.shape
    chunk = member_chunk(members)

    def kernel(ctrl_ref, low_ref, high_ref, pert_ref, blon_ref, blat_ref, out_ref, ext_ref, along_ref):
        step = pl.program_id(1)
        blon = blon_ref[...]
        for m in range(chunk):
            fill_ext(ext_ref, ctrl_ref[m], low_ref[m], high_ref[m], lon_cells, padded)
            along = jnp.dot(blon, ext_ref[...], preferred_element_type=jnp.float32)
            along_ref[m * padded:(m + 1) * padded, :] = along.astype(jnp.bfloat16)
        smoothed = jnp.dot(along_ref[...], blat_ref[...], preferred_element_type=jnp.float32)
        total = pert_ref[0].astype(jnp.float32) * smoothed[0:lon_cells]
        for m in range(1, chunk):
            total = total + pert_ref[m].astype(jnp.float32) * smoothed[
                m * padded:m * padded + lon_cells
            ]

        @pl.when(step == 0)
        def _():
            out_ref[...] = total

        @pl.when(step > 0)
        def _():
            out_ref[...] = out_ref[...] + total

    field = pl.BlockSpec((chunk, None, lon_cells, lat_cells), lambda l, g: (g, l, 0, 0))
    halo = pl.BlockSpec((chunk, None, radius, lat_cells), lambda l, g: (g, l, 0, 0))
    return pl.pallas_call(
        kernel,
        grid=(levels, members // chunk),
        in_specs=[
            field,
            halo,
            halo,
            field,
            pl.BlockSpec(band_lon.shape, lambda l, g: (0, 0)),
            pl.BlockSpec(band_lat.shape, lambda l, g: (0, 0)),
        ],
        out_specs=pl.BlockSpec((None, lon_cells, lat_cells), lambda l, g: (l, 0, 0)),
        out_shape=jax.ShapeDtypeStruct((levels, lon_cells, lat_cells), jnp.float32),
        scratch_shapes=[
            pltpu.VMEM((ext_cells, lat_cells), jnp.bfloat16),
            pltpu.VMEM((chunk * padded, lat_cells), jnp.bfloat16),
        ],
        compiler_params=pltpu.CompilerParams(dimension_semantics=("arbitrary", "arbitrary")),
    )(control, c_low, c_high, perturb, band_lon, band_lat)


def backward_grad(perturb, p_low, p_high, spread, s_low, s_high, control, band_lon, band_lat):
    members, levels, lon_cells, lat_cells = control.shape
    radius = p_low.shape[2]
    padded, ext_cells = band_lon.shape
    chunk = member_chunk(members)

    def kernel(pert_ref, plow_ref, phigh_ref, spread_ref, slow_ref, shigh_ref, ctrl_ref,
               blon_ref, blat_ref, out_ref, ext_ref, along_ref):
        blon = blon_ref[...]
        spread = spread_ref[...]
        s_lo = slow_ref[...]
        s_hi = shigh_ref[...]
        for m in range(chunk):
            fill_ext(
                ext_ref,
                (pert_ref[m].astype(jnp.float32) * spread).astype(jnp.bfloat16),
                (plow_ref[m].astype(jnp.float32) * s_lo).astype(jnp.bfloat16),
                (phigh_ref[m].astype(jnp.float32) * s_hi).astype(jnp.bfloat16),
                lon_cells,
                padded,
            )
            along = jnp.dot(blon, ext_ref[...], preferred_element_type=jnp.float32)
            along_ref[m * padded:(m + 1) * padded, :] = along.astype(jnp.bfloat16)
        smoothed = jnp.dot(along_ref[...], blat_ref[...], preferred_element_type=jnp.float32)
        for m in range(chunk):
            out_ref[m] = ctrl_ref[m].astype(jnp.float32) + smoothed[
                m * padded:m * padded + lon_cells
            ]

    field = pl.BlockSpec((chunk, None, lon_cells, lat_cells), lambda l, g: (g, l, 0, 0))
    halo = pl.BlockSpec((chunk, None, radius, lat_cells), lambda l, g: (g, l, 0, 0))
    level_field = pl.BlockSpec((None, lon_cells, lat_cells), lambda l, g: (l, 0, 0))
    level_halo = pl.BlockSpec((None, radius, lat_cells), lambda l, g: (l, 0, 0))
    out = pl.pallas_call(
        kernel,
        grid=(levels, members // chunk),
        in_specs=[
            field,
            halo,
            halo,
            level_field,
            level_halo,
            level_halo,
            field,
            pl.BlockSpec(band_lon.shape, lambda l, g: (0, 0)),
            pl.BlockSpec(band_lat.shape, lambda l, g: (0, 0)),
        ],
        out_specs=pl.BlockSpec((chunk, lon_cells, None, lat_cells), lambda l, g: (g, 0, l, 0)),
        out_shape=jax.ShapeDtypeStruct((members, lon_cells, levels, lat_cells), jnp.float32),
        scratch_shapes=[
            pltpu.VMEM((ext_cells, lat_cells), jnp.bfloat16),
            pltpu.VMEM((chunk * padded, lat_cells), jnp.bfloat16),
        ],
        compiler_params=pltpu.CompilerParams(dimension_semantics=("arbitrary", "arbitrary")),
    )(perturb, p_low, p_high, spread, s_low, s_high, control, band_lon, band_lat)
    return jnp.transpose(out, (0, 2, 1, 3))


def pick_cells(field_rows, row_index, col_index, block_rows):
    row_count, col_count = field_rows.shape
    field_cols = field_rows.T

    def pick_one_block(indices):
        rows_here, cols_here = indices
        onehot_rows = (
            rows_here[:, None] == jnp.arange(row_count, dtype=jnp.int32)[None, :]
        ).astype(jnp.float32)
        onehot_cols = (
            cols_here[:, None] == jnp.arange(col_count, dtype=jnp.int32)[None, :]
        ).astype(jnp.float32)
        picked = jnp.dot(
            onehot_cols,
            field_cols,
            precision=lax.Precision.HIGHEST,
            preferred_element_type=jnp.float32,
        )
        return jnp.sum(picked * onehot_rows, axis=1)

    values = lax.map(
        pick_one_block, (row_index.reshape(-1, block_rows), col_index.reshape(-1, block_rows))
    )
    return values.reshape(-1)


def spread_cells(misfit, row_index, col_index, row_count, col_count, block_rows):

    def spread_one_block(total, items):
        rows_here, cols_here, values = items
        onehot_rows = (
            rows_here[:, None] == jnp.arange(row_count, dtype=jnp.int32)[None, :]
        ).astype(jnp.float32)
        onehot_cols = (
            cols_here[:, None] == jnp.arange(col_count, dtype=jnp.int32)[None, :]
        ).astype(jnp.float32)
        weighted = onehot_rows * values[:, None]
        return (
            total
            + jnp.dot(
                weighted.T,
                onehot_cols,
                precision=lax.Precision.HIGHEST,
                preferred_element_type=jnp.float32,
            ),
            None,
        )

    start = jnp.zeros((row_count, col_count), jnp.float32)
    items = (
        row_index.reshape(-1, block_rows),
        col_index.reshape(-1, block_rows),
        misfit.reshape(-1, block_rows),
    )
    total, _ = lax.scan(spread_one_block, start, items)
    return total


def local(control, perturb, lon_taps, lat_taps, innov, inv_var, cell_index, counts):
    members_here, levels, lon_cells, lat_cells = control.shape
    radius = lon_taps.shape[0] - 1
    padded = -(-lon_cells // 16) * 16
    band_lon = lon_band(lon_taps, lon_cells, padded)
    band_lat = lat_band(lat_taps, lat_cells)

    slot_ids = lax.broadcasted_iota(jnp.int32, innov.shape, 2)
    weights = jnp.where(slot_ids < counts[:, :, None], inv_var, 0.0)
    lists = jnp.stack([innov, weights, cell_index.astype(jnp.float32)])
    received = lax.all_to_all(lists, "tile", split_axis=2, concat_axis=1, tiled=True)
    observed = received[0].reshape(-1)
    weight_recv = received[1].reshape(-1)
    cells_hit = received[2].reshape(-1).astype(jnp.int32)
    row_index = cells_hit // lat_cells
    col_index = cells_hit % lat_cells
    row_count = levels * lon_cells
    block_rows = math.gcd(observed.shape[0], 1024)

    c_low, c_high = halos(control, "tile", 2, radius)
    p_low, p_high = halos(perturb, "tile", 2, radius)
    member_sum = forward_sum(control, c_low, c_high, perturb, band_lon, band_lat)
    partial = pick_cells(member_sum.reshape(row_count, lat_cells), row_index, col_index, block_rows)
    at_cells = lax.psum(partial, "mem")
    misfit = weight_recv * (at_cells - observed)
    spread = spread_cells(misfit, row_index, col_index, row_count, lat_cells, block_rows)
    spread = spread.reshape(levels, lon_cells, lat_cells)
    s_low, s_high = halos(spread, "tile", 1, radius)
    return backward_grad(
        perturb, p_low, p_high, spread, s_low, s_high, control, band_lon, band_lat
    )


def solution(mesh):
    return jax.shard_map(
        local,
        mesh=mesh,
        in_specs=(
            P("mem", None, "tile", None),
            P("mem", None, "tile", None),
            P(),
            P(),
            P("tile", None, None),
            P("tile", None, None),
            P("tile", None, None),
            P("tile", None),
        ),
        out_specs=P("mem", None, "tile", None),
        check_vma=False,
    )
```

```python
import math

import jax
import jax.numpy as jnp
from jax import lax
from jax.experimental import pallas as pl
from jax.experimental.pallas import tpu as pltpu
from jax.sharding import PartitionSpec as P


def halos(block, axis, dim, width):
    count = lax.axis_size(axis)
    forward = [(i, (i + 1) % count) for i in range(count)]
    backward = [((i + 1) % count, i) for i in range(count)]
    low = lax.ppermute(
        lax.slice_in_dim(block, block.shape[dim] - width, None, axis=dim), axis, forward
    )
    high = lax.ppermute(lax.slice_in_dim(block, 0, width, axis=dim), axis, backward)
    return low, high


def select_chain(dist, taps_ref):
    band = jnp.zeros(dist.shape, jnp.float32)
    for offset in range(taps_ref.shape[0]):
        band = jnp.where(dist == offset, taps_ref[offset], band)
    return band.astype(jnp.bfloat16)


def build_bands(lon_taps, lat_taps, lon_cells, padded, lat_cells):
    radius = lon_taps.shape[0] - 1
    ext_cells = padded + 2 * radius
    tile = 128
    tiles = -(-lat_cells // tile)

    def kernel(lon_ref, lat_ref, blon_ref, blat_ref):
        rows = lax.broadcasted_iota(jnp.int32, (padded, ext_cells), 0)
        cols = lax.broadcasted_iota(jnp.int32, (padded, ext_cells), 1)
        source = jnp.where(
            cols < padded,
            cols,
            jnp.where(
                cols < padded + radius,
                cols - padded - radius,
                cols - padded - radius + lon_cells,
            ),
        )
        valid = (rows < lon_cells) & ((cols < lon_cells) | (cols >= padded))
        dist = jnp.where(valid, jnp.abs(source - rows), radius + 1)
        blon_ref[...] = select_chain(dist, lon_ref)

        t_rows = lax.broadcasted_iota(jnp.int32, (tile, tile), 0)
        t_cols = lax.broadcasted_iota(jnp.int32, (tile, tile), 1)
        blocks = {
            shift: select_chain(jnp.abs(t_rows - t_cols + shift * tile), lat_ref)
            for shift in (-1, 0, 1)
        }
        blat_ref[...] = jnp.zeros(blat_ref.shape, blat_ref.dtype)
        for a in range(tiles):
            for b in (a - 1, a, a + 1):
                if b < 0 or b >= tiles:
                    continue
                height = min(tile, lat_cells - a * tile)
                width = min(tile, lat_cells - b * tile)
                blat_ref[a * tile:a * tile + height, b * tile:b * tile + width] = blocks[a - b][
                    :height, :width
                ]

    smem = pl.BlockSpec(memory_space=pltpu.SMEM)
    return pl.pallas_call(
        kernel,
        in_specs=[smem, smem],
        out_shape=(
            jax.ShapeDtypeStruct((padded, ext_cells), jnp.bfloat16),
            jax.ShapeDtypeStruct((lat_cells, lat_cells), jnp.bfloat16),
        ),
    )(lon_taps.astype(jnp.float32), lat_taps.astype(jnp.float32))


def member_chunk(members):
    for size in (5, 4, 3, 2, 1):
        if members % size == 0:
            return size
    return 1


def fill_ext(ext_ref, local, low, high, lon_cells, padded):
    radius = low.shape[0]
    base = (lon_cells // 16) * 16
    ext_ref[base:padded, :] = jnp.zeros((padded - base, ext_ref.shape[1]), ext_ref.dtype)
    ext_ref[0:lon_cells, :] = local
    ext_ref[padded:padded + radius, :] = low
    ext_ref[padded + radius:padded + 2 * radius, :] = high


def forward_sum(control, c_low, c_high, perturb, band_lon, band_lat):
    members, levels, lon_cells, lat_cells = control.shape
    radius = c_low.shape[2]
    padded, ext_cells = band_lon.shape
    chunk = member_chunk(members)

    def kernel(ctrl_ref, low_ref, high_ref, pert_ref, blon_ref, blat_ref, out_ref, ext_ref, along_ref):
        step = pl.program_id(1)
        blon = blon_ref[...]
        for m in range(chunk):
            fill_ext(ext_ref, ctrl_ref[m], low_ref[m], high_ref[m], lon_cells, padded)
            along = jnp.dot(blon, ext_ref[...], preferred_element_type=jnp.float32)
            along_ref[m * padded:(m + 1) * padded, :] = along.astype(jnp.bfloat16)
        smoothed = jnp.dot(along_ref[...], blat_ref[...], preferred_element_type=jnp.float32)
        total = pert_ref[0].astype(jnp.float32) * smoothed[0:lon_cells]
        for m in range(1, chunk):
            total = total + pert_ref[m].astype(jnp.float32) * smoothed[
                m * padded:m * padded + lon_cells
            ]

        @pl.when(step == 0)
        def _():
            out_ref[...] = total

        @pl.when(step > 0)
        def _():
            out_ref[...] = out_ref[...] + total

    field = pl.BlockSpec((chunk, None, lon_cells, lat_cells), lambda l, g: (g, l, 0, 0))
    halo = pl.BlockSpec((chunk, None, radius, lat_cells), lambda l, g: (g, l, 0, 0))
    return pl.pallas_call(
        kernel,
        grid=(levels, members // chunk),
        in_specs=[
            field,
            halo,
            halo,
            field,
            pl.BlockSpec(band_lon.shape, lambda l, g: (0, 0)),
            pl.BlockSpec(band_lat.shape, lambda l, g: (0, 0)),
        ],
        out_specs=pl.BlockSpec((None, lon_cells, lat_cells), lambda l, g: (l, 0, 0)),
        out_shape=jax.ShapeDtypeStruct((levels, lon_cells, lat_cells), jnp.float32),
        scratch_shapes=[
            pltpu.VMEM((ext_cells, lat_cells), jnp.bfloat16),
            pltpu.VMEM((chunk * padded, lat_cells), jnp.bfloat16),
        ],
        compiler_params=pltpu.CompilerParams(dimension_semantics=("arbitrary", "arbitrary")),
    )(control, c_low, c_high, perturb, band_lon, band_lat)


def backward_grad(perturb, p_low, p_high, spread, s_low, s_high, control, band_lon, band_lat):
    members, levels, lon_cells, lat_cells = control.shape
    radius = p_low.shape[2]
    padded, ext_cells = band_lon.shape
    chunk = member_chunk(members)

    def kernel(pert_ref, plow_ref, phigh_ref, spread_ref, slow_ref, shigh_ref, ctrl_ref,
               blon_ref, blat_ref, out_ref, ext_ref, along_ref):
        blon = blon_ref[...]
        spread = spread_ref[...]
        s_lo = slow_ref[...]
        s_hi = shigh_ref[...]
        for m in range(chunk):
            fill_ext(
                ext_ref,
                (pert_ref[m].astype(jnp.float32) * spread).astype(jnp.bfloat16),
                (plow_ref[m].astype(jnp.float32) * s_lo).astype(jnp.bfloat16),
                (phigh_ref[m].astype(jnp.float32) * s_hi).astype(jnp.bfloat16),
                lon_cells,
                padded,
            )
            along = jnp.dot(blon, ext_ref[...], preferred_element_type=jnp.float32)
            along_ref[m * padded:(m + 1) * padded, :] = along.astype(jnp.bfloat16)
        smoothed = jnp.dot(along_ref[...], blat_ref[...], preferred_element_type=jnp.float32)
        for m in range(chunk):
            out_ref[m] = ctrl_ref[m].astype(jnp.float32) + smoothed[
                m * padded:m * padded + lon_cells
            ]

    field = pl.BlockSpec((chunk, None, lon_cells, lat_cells), lambda l, g: (g, l, 0, 0))
    halo = pl.BlockSpec((chunk, None, radius, lat_cells), lambda l, g: (g, l, 0, 0))
    level_field = pl.BlockSpec((None, lon_cells, lat_cells), lambda l, g: (l, 0, 0))
    level_halo = pl.BlockSpec((None, radius, lat_cells), lambda l, g: (l, 0, 0))
    out = pl.pallas_call(
        kernel,
        grid=(levels, members // chunk),
        in_specs=[
            field,
            halo,
            halo,
            level_field,
            level_halo,
            level_halo,
            field,
            pl.BlockSpec(band_lon.shape, lambda l, g: (0, 0)),
            pl.BlockSpec(band_lat.shape, lambda l, g: (0, 0)),
        ],
        out_specs=pl.BlockSpec((chunk, lon_cells, None, lat_cells), lambda l, g: (g, 0, l, 0)),
        out_shape=jax.ShapeDtypeStruct((members, lon_cells, levels, lat_cells), jnp.float32),
        scratch_shapes=[
            pltpu.VMEM((ext_cells, lat_cells), jnp.bfloat16),
            pltpu.VMEM((chunk * padded, lat_cells), jnp.bfloat16),
        ],
        compiler_params=pltpu.CompilerParams(dimension_semantics=("arbitrary", "arbitrary")),
    )(perturb, p_low, p_high, spread, s_low, s_high, control, band_lon, band_lat)
    return jnp.transpose(out, (0, 2, 1, 3))


def pick_cells(field_rows, row_index, col_index, block_rows):
    row_count, col_count = field_rows.shape
    field_cols = field_rows.T

    def pick_one_block(indices):
        rows_here, cols_here = indices
        onehot_rows = (
            rows_here[:, None] == jnp.arange(row_count, dtype=jnp.int32)[None, :]
        ).astype(jnp.float32)
        onehot_cols = (
            cols_here[:, None] == jnp.arange(col_count, dtype=jnp.int32)[None, :]
        ).astype(jnp.float32)
        picked = jnp.dot(
            onehot_cols,
            field_cols,
            precision=lax.Precision.HIGHEST,
            preferred_element_type=jnp.float32,
        )
        return jnp.sum(picked * onehot_rows, axis=1)

    values = lax.map(
        pick_one_block, (row_index.reshape(-1, block_rows), col_index.reshape(-1, block_rows))
    )
    return values.reshape(-1)


def spread_cells(misfit, row_index, col_index, row_count, col_count, block_rows):

    def spread_one_block(total, items):
        rows_here, cols_here, values = items
        onehot_rows = (
            rows_here[:, None] == jnp.arange(row_count, dtype=jnp.int32)[None, :]
        ).astype(jnp.float32)
        onehot_cols = (
            cols_here[:, None] == jnp.arange(col_count, dtype=jnp.int32)[None, :]
        ).astype(jnp.float32)
        weighted = onehot_rows * values[:, None]
        return (
            total
            + jnp.dot(
                weighted.T,
                onehot_cols,
                precision=lax.Precision.HIGHEST,
                preferred_element_type=jnp.float32,
            ),
            None,
        )

    start = jnp.zeros((row_count, col_count), jnp.float32)
    items = (
        row_index.reshape(-1, block_rows),
        col_index.reshape(-1, block_rows),
        misfit.reshape(-1, block_rows),
    )
    total, _ = lax.scan(spread_one_block, start, items)
    return total


def local(control, perturb, lon_taps, lat_taps, innov, inv_var, cell_index, counts):
    members_here, levels, lon_cells, lat_cells = control.shape
    radius = lon_taps.shape[0] - 1
    padded = -(-lon_cells // 16) * 16
    band_lon, band_lat = build_bands(lon_taps, lat_taps, lon_cells, padded, lat_cells)

    slot_ids = lax.broadcasted_iota(jnp.int32, innov.shape, 2)
    weights = jnp.where(slot_ids < counts[:, :, None], inv_var, 0.0)
    lists = jnp.stack([innov, weights, cell_index.astype(jnp.float32)])
    received = lax.all_to_all(lists, "tile", split_axis=2, concat_axis=1, tiled=True)
    observed = received[0].reshape(-1)
    weight_recv = received[1].reshape(-1)
    cells_hit = received[2].reshape(-1).astype(jnp.int32)
    row_index = cells_hit // lat_cells
    col_index = cells_hit % lat_cells
    row_count = levels * lon_cells
    block_rows = math.gcd(observed.shape[0], 1024)

    c_low, c_high = halos(control, "tile", 2, radius)
    p_low, p_high = halos(perturb, "tile", 2, radius)
    member_sum = forward_sum(control, c_low, c_high, perturb, band_lon, band_lat)
    partial = pick_cells(member_sum.reshape(row_count, lat_cells), row_index, col_index, block_rows)
    at_cells = lax.psum(partial, "mem")
    misfit = weight_recv * (at_cells - observed)
    spread = spread_cells(misfit, row_index, col_index, row_count, lat_cells, block_rows)
    spread = spread.reshape(levels, lon_cells, lat_cells)
    s_low, s_high = halos(spread, "tile", 1, radius)
    return backward_grad(
        perturb, p_low, p_high, spread, s_low, s_high, control, band_lon, band_lat
    )


def solution(mesh):
    return jax.shard_map(
        local,
        mesh=mesh,
        in_specs=(
            P("mem", None, "tile", None),
            P("mem", None, "tile", None),
            P(),
            P(),
            P("tile", None, None),
            P("tile", None, None),
            P("tile", None, None),
            P("tile", None),
        ),
        out_specs=P("mem", None, "tile", None),
        check_vma=False,
    )
```

```python
import math

import jax
import jax.numpy as jnp
from jax import lax
from jax.experimental import pallas as pl
from jax.experimental.pallas import tpu as pltpu
from jax.sharding import PartitionSpec as P


def halos(block, axis, dim, width):
    count = lax.axis_size(axis)
    forward = [(i, (i + 1) % count) for i in range(count)]
    backward = [((i + 1) % count, i) for i in range(count)]
    low = lax.ppermute(
        lax.slice_in_dim(block, block.shape[dim] - width, None, axis=dim), axis, forward
    )
    high = lax.ppermute(lax.slice_in_dim(block, 0, width, axis=dim), axis, backward)
    return low, high


def sum_over(values, axis):
    count = lax.axis_size(axis)
    total = values
    for shift in range(1, count):
        total = total + lax.ppermute(
            values, axis, [(i, (i + shift) % count) for i in range(count)]
        )
    return total


def select_chain(dist, taps_ref):
    band = jnp.zeros(dist.shape, jnp.float32)
    for offset in range(taps_ref.shape[0]):
        band = jnp.where(dist == offset, taps_ref[offset], band)
    return band.astype(jnp.bfloat16)


def build_bands(lon_taps, lat_taps, lon_cells, padded, lat_cells):
    radius = lon_taps.shape[0] - 1
    ext_cells = padded + 2 * radius
    tile = 128
    tiles = -(-lat_cells // tile)

    def kernel(lon_ref, lat_ref, blon_ref, blat_ref):
        rows = lax.broadcasted_iota(jnp.int32, (padded, ext_cells), 0)
        cols = lax.broadcasted_iota(jnp.int32, (padded, ext_cells), 1)
        source = jnp.where(
            cols < padded,
            cols,
            jnp.where(
                cols < padded + radius,
                cols - padded - radius,
                cols - padded - radius + lon_cells,
            ),
        )
        valid = (rows < lon_cells) & ((cols < lon_cells) | (cols >= padded))
        dist = jnp.where(valid, jnp.abs(source - rows), radius + 1)
        blon_ref[...] = select_chain(dist, lon_ref)

        t_rows = lax.broadcasted_iota(jnp.int32, (tile, tile), 0)
        t_cols = lax.broadcasted_iota(jnp.int32, (tile, tile), 1)
        blocks = {
            shift: select_chain(jnp.abs(t_rows - t_cols + shift * tile), lat_ref)
            for shift in (-1, 0, 1)
        }
        blat_ref[...] = jnp.zeros(blat_ref.shape, blat_ref.dtype)
        for a in range(tiles):
            for b in (a - 1, a, a + 1):
                if b < 0 or b >= tiles:
                    continue
                height = min(tile, lat_cells - a * tile)
                width = min(tile, lat_cells - b * tile)
                blat_ref[a * tile:a * tile + height, b * tile:b * tile + width] = blocks[a - b][
                    :height, :width
                ]

    smem = pl.BlockSpec(memory_space=pltpu.SMEM)
    return pl.pallas_call(
        kernel,
        in_specs=[smem, smem],
        out_shape=(
            jax.ShapeDtypeStruct((padded, ext_cells), jnp.bfloat16),
            jax.ShapeDtypeStruct((lat_cells, lat_cells), jnp.bfloat16),
        ),
    )(lon_taps.astype(jnp.float32), lat_taps.astype(jnp.float32))


def member_chunk(members):
    for size in (5, 4, 3, 2, 1):
        if members % size == 0:
            return size
    return 1


def fill_ext(ext_ref, local, low, high, lon_cells, padded):
    radius = low.shape[0]
    base = (lon_cells // 16) * 16
    ext_ref[base:padded, :] = jnp.zeros((padded - base, ext_ref.shape[1]), ext_ref.dtype)
    ext_ref[0:lon_cells, :] = local
    ext_ref[padded:padded + radius, :] = low
    ext_ref[padded + radius:padded + 2 * radius, :] = high


def forward_sum(control, c_low, c_high, perturb, band_lon, band_lat):
    members, levels, lon_cells, lat_cells = control.shape
    radius = c_low.shape[2]
    padded, ext_cells = band_lon.shape
    chunk = member_chunk(members)

    def kernel(ctrl_ref, low_ref, high_ref, pert_ref, blon_ref, blat_ref, out_ref, ext_ref, along_ref):
        step = pl.program_id(1)
        blon = blon_ref[...]
        for m in range(chunk):
            fill_ext(ext_ref, ctrl_ref[m], low_ref[m], high_ref[m], lon_cells, padded)
            along = jnp.dot(blon, ext_ref[...], preferred_element_type=jnp.float32)
            along_ref[m * padded:(m + 1) * padded, :] = along.astype(jnp.bfloat16)
        smoothed = jnp.dot(along_ref[...], blat_ref[...], preferred_element_type=jnp.float32)
        total = pert_ref[0].astype(jnp.float32) * smoothed[0:lon_cells]
        for m in range(1, chunk):
            total = total + pert_ref[m].astype(jnp.float32) * smoothed[
                m * padded:m * padded + lon_cells
            ]

        @pl.when(step == 0)
        def _():
            out_ref[...] = total

        @pl.when(step > 0)
        def _():
            out_ref[...] = out_ref[...] + total

    field = pl.BlockSpec((chunk, None, lon_cells, lat_cells), lambda l, g: (g, l, 0, 0))
    halo = pl.BlockSpec((chunk, None, radius, lat_cells), lambda l, g: (g, l, 0, 0))
    return pl.pallas_call(
        kernel,
        grid=(levels, members // chunk),
        in_specs=[
            field,
            halo,
            halo,
            field,
            pl.BlockSpec(band_lon.shape, lambda l, g: (0, 0)),
            pl.BlockSpec(band_lat.shape, lambda l, g: (0, 0)),
        ],
        out_specs=pl.BlockSpec((None, lon_cells, lat_cells), lambda l, g: (l, 0, 0)),
        out_shape=jax.ShapeDtypeStruct((levels, lon_cells, lat_cells), jnp.float32),
        scratch_shapes=[
            pltpu.VMEM((ext_cells, lat_cells), jnp.bfloat16),
            pltpu.VMEM((chunk * padded, lat_cells), jnp.bfloat16),
        ],
        compiler_params=pltpu.CompilerParams(dimension_semantics=("arbitrary", "arbitrary")),
    )(control, c_low, c_high, perturb, band_lon, band_lat)


def backward_grad(perturb, p_low, p_high, spread, s_low, s_high, control, band_lon, band_lat):
    members, levels, lon_cells, lat_cells = control.shape
    radius = p_low.shape[2]
    padded, ext_cells = band_lon.shape
    chunk = member_chunk(members)

    def kernel(pert_ref, plow_ref, phigh_ref, spread_ref, slow_ref, shigh_ref, ctrl_ref,
               blon_ref, blat_ref, out_ref, ext_ref, along_ref):
        blon = blon_ref[...]
        spread = spread_ref[...]
        s_lo = slow_ref[...]
        s_hi = shigh_ref[...]
        for m in range(chunk):
            fill_ext(
                ext_ref,
                (pert_ref[m].astype(jnp.float32) * spread).astype(jnp.bfloat16),
                (plow_ref[m].astype(jnp.float32) * s_lo).astype(jnp.bfloat16),
                (phigh_ref[m].astype(jnp.float32) * s_hi).astype(jnp.bfloat16),
                lon_cells,
                padded,
            )
            along = jnp.dot(blon, ext_ref[...], preferred_element_type=jnp.float32)
            along_ref[m * padded:(m + 1) * padded, :] = along.astype(jnp.bfloat16)
        smoothed = jnp.dot(along_ref[...], blat_ref[...], preferred_element_type=jnp.float32)
        for m in range(chunk):
            out_ref[m] = ctrl_ref[m].astype(jnp.float32) + smoothed[
                m * padded:m * padded + lon_cells
            ]

    field = pl.BlockSpec((chunk, None, lon_cells, lat_cells), lambda l, g: (g, l, 0, 0))
    halo = pl.BlockSpec((chunk, None, radius, lat_cells), lambda l, g: (g, l, 0, 0))
    level_field = pl.BlockSpec((None, lon_cells, lat_cells), lambda l, g: (l, 0, 0))
    level_halo = pl.BlockSpec((None, radius, lat_cells), lambda l, g: (l, 0, 0))
    out = pl.pallas_call(
        kernel,
        grid=(levels, members // chunk),
        in_specs=[
            field,
            halo,
            halo,
            level_field,
            level_halo,
            level_halo,
            field,
            pl.BlockSpec(band_lon.shape, lambda l, g: (0, 0)),
            pl.BlockSpec(band_lat.shape, lambda l, g: (0, 0)),
        ],
        out_specs=pl.BlockSpec((chunk, lon_cells, None, lat_cells), lambda l, g: (g, 0, l, 0)),
        out_shape=jax.ShapeDtypeStruct((members, lon_cells, levels, lat_cells), jnp.float32),
        scratch_shapes=[
            pltpu.VMEM((ext_cells, lat_cells), jnp.bfloat16),
            pltpu.VMEM((chunk * padded, lat_cells), jnp.bfloat16),
        ],
        compiler_params=pltpu.CompilerParams(dimension_semantics=("arbitrary", "arbitrary")),
    )(perturb, p_low, p_high, spread, s_low, s_high, control, band_lon, band_lat)
    return jnp.transpose(out, (0, 2, 1, 3))


def pick_cells(field_rows, row_index, col_index, block_rows):
    row_count, col_count = field_rows.shape
    field_cols = field_rows.T

    def pick_one_block(indices):
        rows_here, cols_here = indices
        onehot_rows = (
            rows_here[:, None] == jnp.arange(row_count, dtype=jnp.int32)[None, :]
        ).astype(jnp.float32)
        onehot_cols = (
            cols_here[:, None] == jnp.arange(col_count, dtype=jnp.int32)[None, :]
        ).astype(jnp.float32)
        picked = jnp.dot(
            onehot_cols,
            field_cols,
            precision=lax.Precision.HIGHEST,
            preferred_element_type=jnp.float32,
        )
        return jnp.sum(picked * onehot_rows, axis=1)

    values = lax.map(
        pick_one_block, (row_index.reshape(-1, block_rows), col_index.reshape(-1, block_rows))
    )
    return values.reshape(-1)


def spread_cells(misfit, row_index, col_index, row_count, col_count, block_rows):

    def spread_one_block(total, items):
        rows_here, cols_here, values = items
        onehot_rows = (
            rows_here[:, None] == jnp.arange(row_count, dtype=jnp.int32)[None, :]
        ).astype(jnp.float32)
        onehot_cols = (
            cols_here[:, None] == jnp.arange(col_count, dtype=jnp.int32)[None, :]
        ).astype(jnp.float32)
        weighted = onehot_rows * values[:, None]
        return (
            total
            + jnp.dot(
                weighted.T,
                onehot_cols,
                precision=lax.Precision.HIGHEST,
                preferred_element_type=jnp.float32,
            ),
            None,
        )

    start = jnp.zeros((row_count, col_count), jnp.float32)
    items = (
        row_index.reshape(-1, block_rows),
        col_index.reshape(-1, block_rows),
        misfit.reshape(-1, block_rows),
    )
    total, _ = lax.scan(spread_one_block, start, items)
    return total


def local(control, perturb, lon_taps, lat_taps, innov, inv_var, cell_index, counts):
    members_here, levels, lon_cells, lat_cells = control.shape
    radius = lon_taps.shape[0] - 1
    padded = -(-lon_cells // 16) * 16
    band_lon, band_lat = build_bands(lon_taps, lat_taps, lon_cells, padded, lat_cells)

    slot_ids = lax.broadcasted_iota(jnp.int32, innov.shape, 2)
    weights = jnp.where(slot_ids < counts[:, :, None], inv_var, 0.0)
    lists = jnp.stack([innov, weights, cell_index.astype(jnp.float32)])
    received = lax.all_to_all(lists, "tile", split_axis=2, concat_axis=1, tiled=True)
    observed = received[0].reshape(-1)
    weight_recv = received[1].reshape(-1)
    cells_hit = received[2].reshape(-1).astype(jnp.int32)
    row_index = cells_hit // lat_cells
    col_index = cells_hit % lat_cells
    row_count = levels * lon_cells
    block_rows = math.gcd(observed.shape[0], 1024)

    c_low, c_high = halos(control, "tile", 2, radius)
    late_perturb = lax.optimization_barrier((perturb, c_low, c_high))[0]
    p_low, p_high = halos(late_perturb, "tile", 2, radius)
    member_sum = forward_sum(control, c_low, c_high, perturb, band_lon, band_lat)
    partial = pick_cells(member_sum.reshape(row_count, lat_cells), row_index, col_index, block_rows)
    at_cells = sum_over(partial, "mem")
    misfit = weight_recv * (at_cells - observed)
    spread = spread_cells(misfit, row_index, col_index, row_count, lat_cells, block_rows)
    spread = spread.reshape(levels, lon_cells, lat_cells)
    s_low, s_high = halos(spread, "tile", 1, radius)
    return backward_grad(
        perturb, p_low, p_high, spread, s_low, s_high, control, band_lon, band_lat
    )


def solution(mesh):
    return jax.shard_map(
        local,
        mesh=mesh,
        in_specs=(
            P("mem", None, "tile", None),
            P("mem", None, "tile", None),
            P(),
            P(),
            P("tile", None, None),
            P("tile", None, None),
            P("tile", None, None),
            P("tile", None),
        ),
        out_specs=P("mem", None, "tile", None),
        check_vma=False,
    )
```

```python
import math

import jax
import jax.numpy as jnp
from jax import lax
from jax.experimental import pallas as pl
from jax.experimental.pallas import tpu as pltpu
from jax.sharding import PartitionSpec as P


def halos(block, axis, dim, width):
    count = lax.axis_size(axis)
    forward = [(i, (i + 1) % count) for i in range(count)]
    backward = [((i + 1) % count, i) for i in range(count)]
    low = lax.ppermute(
        lax.slice_in_dim(block, block.shape[dim] - width, None, axis=dim), axis, forward
    )
    high = lax.ppermute(lax.slice_in_dim(block, 0, width, axis=dim), axis, backward)
    return low, high


def sum_over(values, axis):
    count = lax.axis_size(axis)
    total = values
    for shift in range(1, count):
        total = total + lax.ppermute(
            values, axis, [(i, (i + shift) % count) for i in range(count)]
        )
    return total


def select_chain(dist, taps_ref):
    band = jnp.zeros(dist.shape, jnp.float32)
    for offset in range(taps_ref.shape[0]):
        band = jnp.where(dist == offset, taps_ref[offset], band)
    return band.astype(jnp.bfloat16)


def build_bands(lon_taps, lat_taps, lon_cells, padded, lat_cells):
    radius = lon_taps.shape[0] - 1
    ext_cells = padded + 2 * radius
    tile = 128
    tiles = -(-lat_cells // tile)

    def kernel(lon_ref, lat_ref, blon_ref, blat_ref):
        rows = lax.broadcasted_iota(jnp.int32, (padded, ext_cells), 0)
        cols = lax.broadcasted_iota(jnp.int32, (padded, ext_cells), 1)
        source = jnp.where(
            cols < padded,
            cols,
            jnp.where(
                cols < padded + radius,
                cols - padded - radius,
                cols - padded - radius + lon_cells,
            ),
        )
        valid = (rows < lon_cells) & ((cols < lon_cells) | (cols >= padded))
        dist = jnp.where(valid, jnp.abs(source - rows), radius + 1)
        blon_ref[...] = select_chain(dist, lon_ref)

        t_rows = lax.broadcasted_iota(jnp.int32, (tile, tile), 0)
        t_cols = lax.broadcasted_iota(jnp.int32, (tile, tile), 1)
        blocks = {
            shift: select_chain(jnp.abs(t_rows - t_cols + shift * tile), lat_ref)
            for shift in (-1, 0, 1)
        }
        blat_ref[...] = jnp.zeros(blat_ref.shape, blat_ref.dtype)
        for a in range(tiles):
            for b in (a - 1, a, a + 1):
                if b < 0 or b >= tiles:
                    continue
                height = min(tile, lat_cells - a * tile)
                width = min(tile, lat_cells - b * tile)
                blat_ref[a * tile:a * tile + height, b * tile:b * tile + width] = blocks[a - b][
                    :height, :width
                ]

    smem = pl.BlockSpec(memory_space=pltpu.SMEM)
    return pl.pallas_call(
        kernel,
        in_specs=[smem, smem],
        out_shape=(
            jax.ShapeDtypeStruct((padded, ext_cells), jnp.bfloat16),
            jax.ShapeDtypeStruct((lat_cells, lat_cells), jnp.bfloat16),
        ),
    )(lon_taps.astype(jnp.float32), lat_taps.astype(jnp.float32))


def member_chunk(members):
    for size in (5, 4, 3, 2, 1):
        if members % size == 0:
            return size
    return 1


def fill_ext(ext_ref, local, low, high, lon_cells, padded):
    radius = low.shape[0]
    base = (lon_cells // 16) * 16
    ext_ref[base:padded, :] = jnp.zeros((padded - base, ext_ref.shape[1]), ext_ref.dtype)
    ext_ref[0:lon_cells, :] = local
    ext_ref[padded:padded + radius, :] = low
    ext_ref[padded + radius:padded + 2 * radius, :] = high


def split3(values):
    hi = values.astype(jnp.bfloat16)
    rest = values - hi.astype(jnp.float32)
    mid = rest.astype(jnp.bfloat16)
    lo = (rest - mid.astype(jnp.float32)).astype(jnp.bfloat16)
    return hi, mid, lo


def cell_onehots(cells, row_count, lat_cells):
    rows = jnp.floor((cells + 0.5) / lat_cells)
    cols = (cells - rows * lat_cells).astype(jnp.int32)
    col_ids = lax.broadcasted_iota(jnp.int32, (lat_cells, cells.shape[1]), 0)
    onehot_cols = jnp.where(col_ids == cols, 1.0, 0.0).astype(jnp.bfloat16)
    row_ids = lax.broadcasted_iota(jnp.int32, (row_count, cells.shape[1]), 0)
    return row_ids == rows.astype(jnp.int32), onehot_cols


def obs_chunk(count):
    for size in (2048, 1024, 512, 256, 128):
        if count % size == 0:
            return size
    return count


def forward_pick(control, c_low, c_high, perturb, band_lon, band_lat, cells):
    members, levels, lon_cells, lat_cells = control.shape
    radius = c_low.shape[2]
    padded, ext_cells = band_lon.shape
    chunk = member_chunk(members)
    steps = members // chunk
    count = cells.shape[1]
    block = obs_chunk(count)

    def kernel(ctrl_ref, low_ref, high_ref, pert_ref, blon_ref, blat_ref, cells_ref, out_ref,
               ext_ref, along_ref, acc_ref):
        step = pl.program_id(0)
        blon = blon_ref[...]
        for m in range(chunk):
            fill_ext(ext_ref, ctrl_ref[m], low_ref[m], high_ref[m], lon_cells, padded)
            along = jnp.dot(blon, ext_ref[...], preferred_element_type=jnp.float32)
            along_ref[m * padded:(m + 1) * padded, :] = along.astype(jnp.bfloat16)
        smoothed = jnp.dot(along_ref[...], blat_ref[...], preferred_element_type=jnp.float32)
        total = pert_ref[0].astype(jnp.float32) * smoothed[0:lon_cells]
        for m in range(1, chunk):
            total = total + pert_ref[m].astype(jnp.float32) * smoothed[
                m * padded:m * padded + lon_cells
            ]

        @pl.when(step == 0)
        def _():
            acc_ref[...] = jnp.zeros(acc_ref.shape, acc_ref.dtype)

        acc_ref[0:lon_cells, :] = acc_ref[0:lon_cells, :] + total

        @pl.when(step == steps - 1)
        def _():
            pieces = split3(acc_ref[...])
            for start in range(0, count, block):
                onehot_rows, onehot_cols = cell_onehots(
                    cells_ref[:, start:start + block], padded, lat_cells
                )
                at_rows = jnp.dot(pieces[0], onehot_cols, preferred_element_type=jnp.float32)
                at_rows = at_rows + jnp.dot(
                    pieces[1], onehot_cols, preferred_element_type=jnp.float32
                )
                at_rows = at_rows + jnp.dot(
                    pieces[2], onehot_cols, preferred_element_type=jnp.float32
                )
                out_ref[:, start:start + block] = jnp.sum(
                    jnp.where(onehot_rows, at_rows, 0.0), axis=0, keepdims=True
                )

    field = pl.BlockSpec((chunk, None, lon_cells, lat_cells), lambda g: (g, 0, 0, 0))
    halo = pl.BlockSpec((chunk, None, radius, lat_cells), lambda g: (g, 0, 0, 0))
    whole = lambda shape: pl.BlockSpec(shape, lambda g: (0,) * len(shape))
    return pl.pallas_call(
        kernel,
        grid=(steps,),
        in_specs=[
            field,
            halo,
            halo,
            field,
            whole(band_lon.shape),
            whole(band_lat.shape),
            whole(cells.shape),
        ],
        out_specs=whole((1, count)),
        out_shape=jax.ShapeDtypeStruct((1, count), jnp.float32),
        scratch_shapes=[
            pltpu.VMEM((ext_cells, lat_cells), jnp.bfloat16),
            pltpu.VMEM((chunk * padded, lat_cells), jnp.bfloat16),
            pltpu.VMEM((padded, lat_cells), jnp.float32),
        ],
        compiler_params=pltpu.CompilerParams(dimension_semantics=("arbitrary",)),
    )(control, c_low, c_high, perturb, band_lon, band_lat, cells)


def spread_misfits(at_cells, lists, lon_cells, lat_cells, radius, padded):
    count = lists.shape[1]
    block = obs_chunk(count)

    def kernel(at_ref, lists_ref, spread_ref, low_ref, high_ref):
        misfit = lists_ref[1:2, :] * (at_ref[...] - lists_ref[0:1, :])
        total = jnp.zeros((padded, lat_cells), jnp.float32)
        for start in range(0, count, block):
            onehot_rows, onehot_cols = cell_onehots(
                lists_ref[2:3, start:start + block], padded, lat_cells
            )
            weighted = jnp.where(onehot_rows, misfit[:, start:start + block], 0.0)
            for piece in split3(weighted):
                total = total + lax.dot_general(
                    piece,
                    onehot_cols,
                    (((1,), (1,)), ((), ())),
                    preferred_element_type=jnp.float32,
                )
        spread_ref[...] = total[0:lon_cells]
        low_ref[...] = total[lon_cells - radius:lon_cells]
        high_ref[...] = total[0:radius]

    return pl.pallas_call(
        kernel,
        out_shape=(
            jax.ShapeDtypeStruct((lon_cells, lat_cells), jnp.float32),
            jax.ShapeDtypeStruct((radius, lat_cells), jnp.float32),
            jax.ShapeDtypeStruct((radius, lat_cells), jnp.float32),
        ),
    )(at_cells, lists)


def backward_grad(perturb, p_low, p_high, spread, s_low, s_high, control, band_lon, band_lat):
    members, levels, lon_cells, lat_cells = control.shape
    radius = p_low.shape[2]
    padded, ext_cells = band_lon.shape
    chunk = member_chunk(members)

    def kernel(pert_ref, plow_ref, phigh_ref, spread_ref, slow_ref, shigh_ref, ctrl_ref,
               blon_ref, blat_ref, out_ref, ext_ref, along_ref):
        blon = blon_ref[...]
        spread = spread_ref[...]
        s_lo = slow_ref[...]
        s_hi = shigh_ref[...]
        for m in range(chunk):
            fill_ext(
                ext_ref,
                (pert_ref[m].astype(jnp.float32) * spread).astype(jnp.bfloat16),
                (plow_ref[m].astype(jnp.float32) * s_lo).astype(jnp.bfloat16),
                (phigh_ref[m].astype(jnp.float32) * s_hi).astype(jnp.bfloat16),
                lon_cells,
                padded,
            )
            along = jnp.dot(blon, ext_ref[...], preferred_element_type=jnp.float32)
            along_ref[m * padded:(m + 1) * padded, :] = along.astype(jnp.bfloat16)
        smoothed = jnp.dot(along_ref[...], blat_ref[...], preferred_element_type=jnp.float32)
        for m in range(chunk):
            out_ref[m] = ctrl_ref[m].astype(jnp.float32) + smoothed[
                m * padded:m * padded + lon_cells
            ]

    field = pl.BlockSpec((chunk, None, lon_cells, lat_cells), lambda l, g: (g, l, 0, 0))
    halo = pl.BlockSpec((chunk, None, radius, lat_cells), lambda l, g: (g, l, 0, 0))
    level_field = pl.BlockSpec((None, lon_cells, lat_cells), lambda l, g: (l, 0, 0))
    level_halo = pl.BlockSpec((None, radius, lat_cells), lambda l, g: (l, 0, 0))
    out = pl.pallas_call(
        kernel,
        grid=(levels, members // chunk),
        in_specs=[
            field,
            halo,
            halo,
            level_field,
            level_halo,
            level_halo,
            field,
            pl.BlockSpec(band_lon.shape, lambda l, g: (0, 0)),
            pl.BlockSpec(band_lat.shape, lambda l, g: (0, 0)),
        ],
        out_specs=pl.BlockSpec((chunk, lon_cells, None, lat_cells), lambda l, g: (g, 0, l, 0)),
        out_shape=jax.ShapeDtypeStruct((members, lon_cells, levels, lat_cells), jnp.float32),
        scratch_shapes=[
            pltpu.VMEM((ext_cells, lat_cells), jnp.bfloat16),
            pltpu.VMEM((chunk * padded, lat_cells), jnp.bfloat16),
        ],
        compiler_params=pltpu.CompilerParams(dimension_semantics=("arbitrary", "arbitrary")),
    )(perturb, p_low, p_high, spread, s_low, s_high, control, band_lon, band_lat)
    return jnp.transpose(out, (0, 2, 1, 3))


def local(control, perturb, lon_taps, lat_taps, innov, inv_var, cell_index, counts):
    members_here, levels, lon_cells, lat_cells = control.shape
    radius = lon_taps.shape[0] - 1
    padded = -(-lon_cells // 16) * 16
    band_lon, band_lat = build_bands(lon_taps, lat_taps, lon_cells, padded, lat_cells)

    slot_ids = lax.broadcasted_iota(jnp.int32, innov.shape, 2)
    weights = jnp.where(slot_ids < counts[:, :, None], inv_var, 0.0)
    lists = jnp.stack([innov, weights, cell_index.astype(jnp.float32)])
    received = lax.all_to_all(lists, "tile", split_axis=2, concat_axis=1, tiled=True)
    received = received.reshape(3, -1)

    c_low, c_high = halos(control, "tile", 2, radius)
    late_perturb = lax.optimization_barrier((perturb, c_low, c_high))[0]
    p_low, p_high = halos(late_perturb, "tile", 2, radius)
    partial = forward_pick(
        control, c_low, c_high, perturb, band_lon, band_lat, received[2:3]
    )
    at_cells = sum_over(partial, "mem")
    spread, low_send, high_send = spread_misfits(
        at_cells, received, lon_cells, lat_cells, radius, padded
    )
    count = lax.axis_size("tile")
    s_low = lax.ppermute(low_send, "tile", [(i, (i + 1) % count) for i in range(count)])
    s_high = lax.ppermute(high_send, "tile", [((i + 1) % count, i) for i in range(count)])
    return backward_grad(
        perturb,
        p_low,
        p_high,
        spread[None],
        s_low[None],
        s_high[None],
        control,
        band_lon,
        band_lat,
    )


def solution(mesh):
    return jax.shard_map(
        local,
        mesh=mesh,
        in_specs=(
            P("mem", None, "tile", None),
            P("mem", None, "tile", None),
            P(),
            P(),
            P("tile", None, None),
            P("tile", None, None),
            P("tile", None, None),
            P("tile", None),
        ),
        out_specs=P("mem", None, "tile", None),
        check_vma=False,
    )
```

```python
import math

import jax
import jax.numpy as jnp
from jax import lax
from jax.experimental import pallas as pl
from jax.experimental.pallas import tpu as pltpu
from jax.sharding import PartitionSpec as P


def halos(block, axis, dim, width):
    count = lax.axis_size(axis)
    forward = [(i, (i + 1) % count) for i in range(count)]
    backward = [((i + 1) % count, i) for i in range(count)]
    low = lax.ppermute(
        lax.slice_in_dim(block, block.shape[dim] - width, None, axis=dim), axis, forward
    )
    high = lax.ppermute(lax.slice_in_dim(block, 0, width, axis=dim), axis, backward)
    return low, high


def sum_over(values, axis):
    count = lax.axis_size(axis)
    total = values
    for shift in range(1, count):
        total = total + lax.ppermute(
            values, axis, [(i, (i + shift) % count) for i in range(count)]
        )
    return total


def select_chain(dist, taps_ref):
    band = jnp.zeros(dist.shape, jnp.float32)
    for offset in range(taps_ref.shape[0]):
        band = jnp.where(dist == offset, taps_ref[offset], band)
    return band.astype(jnp.bfloat16)


def build_bands(lon_taps, lat_taps, lon_cells, padded, lat_cells):
    radius = lon_taps.shape[0] - 1
    ext_cells = padded + 2 * radius
    tile = 128
    tiles = -(-lat_cells // tile)

    def kernel(lon_ref, lat_ref, blon_ref, blat_ref):
        rows = lax.broadcasted_iota(jnp.int32, (padded, ext_cells), 0)
        cols = lax.broadcasted_iota(jnp.int32, (padded, ext_cells), 1)
        source = jnp.where(
            cols < padded,
            cols,
            jnp.where(
                cols < padded + radius,
                cols - padded - radius,
                cols - padded - radius + lon_cells,
            ),
        )
        valid = (rows < lon_cells) & ((cols < lon_cells) | (cols >= padded))
        dist = jnp.where(valid, jnp.abs(source - rows), radius + 1)
        blon_ref[...] = select_chain(dist, lon_ref)

        t_rows = lax.broadcasted_iota(jnp.int32, (tile, tile), 0)
        t_cols = lax.broadcasted_iota(jnp.int32, (tile, tile), 1)
        blocks = {
            shift: select_chain(jnp.abs(t_rows - t_cols + shift * tile), lat_ref)
            for shift in (-1, 0, 1)
        }
        blat_ref[...] = jnp.zeros(blat_ref.shape, blat_ref.dtype)
        for a in range(tiles):
            for b in (a - 1, a, a + 1):
                if b < 0 or b >= tiles:
                    continue
                height = min(tile, lat_cells - a * tile)
                width = min(tile, lat_cells - b * tile)
                blat_ref[a * tile:a * tile + height, b * tile:b * tile + width] = blocks[a - b][
                    :height, :width
                ]

    smem = pl.BlockSpec(memory_space=pltpu.SMEM)
    return pl.pallas_call(
        kernel,
        in_specs=[smem, smem],
        out_shape=(
            jax.ShapeDtypeStruct((padded, ext_cells), jnp.bfloat16),
            jax.ShapeDtypeStruct((lat_cells, lat_cells), jnp.bfloat16),
        ),
    )(lon_taps.astype(jnp.float32), lat_taps.astype(jnp.float32))


def member_chunk(members):
    for size in (5, 4, 3, 2, 1):
        if members % size == 0:
            return size
    return 1


def fill_ext(ext_ref, local, low, high, lon_cells, padded):
    radius = low.shape[0]
    base = (lon_cells // 16) * 16
    ext_ref[base:padded, :] = jnp.zeros((padded - base, ext_ref.shape[1]), ext_ref.dtype)
    ext_ref[0:lon_cells, :] = local
    ext_ref[padded:padded + radius, :] = low
    ext_ref[padded + radius:padded + 2 * radius, :] = high


def split3(values):
    hi = values.astype(jnp.bfloat16)
    rest = values - hi.astype(jnp.float32)
    mid = rest.astype(jnp.bfloat16)
    lo = (rest - mid.astype(jnp.float32)).astype(jnp.bfloat16)
    return hi, mid, lo


def cell_onehots(cells, row_count, lat_cells):
    rows = jnp.floor((cells + 0.5) / lat_cells)
    cols = (cells - rows * lat_cells).astype(jnp.int32)
    col_ids = lax.broadcasted_iota(jnp.int32, (lat_cells, cells.shape[1]), 0)
    onehot_cols = jnp.where(col_ids == cols, 1.0, 0.0).astype(jnp.bfloat16)
    row_ids = lax.broadcasted_iota(jnp.int32, (row_count, cells.shape[1]), 0)
    return row_ids == rows.astype(jnp.int32), onehot_cols


def obs_chunk(count):
    for size in (2048, 1024, 512, 256, 128):
        if count % size == 0:
            return size
    return count


def forward_sum(control, c_low, c_high, perturb, band_lon, band_lat):
    members, levels, lon_cells, lat_cells = control.shape
    radius = c_low.shape[2]
    padded, ext_cells = band_lon.shape
    chunk = member_chunk(members)
    steps = members // chunk

    def kernel(ctrl_ref, low_ref, high_ref, pert_ref, blon_ref, blat_ref, out_ref,
               ext_ref, along_ref, acc_ref):
        step = pl.program_id(0)
        blon = blon_ref[...]
        for m in range(chunk):
            fill_ext(ext_ref, ctrl_ref[m], low_ref[m], high_ref[m], lon_cells, padded)
            along = jnp.dot(blon, ext_ref[...], preferred_element_type=jnp.float32)
            along_ref[m * padded:(m + 1) * padded, :] = along.astype(jnp.bfloat16)
        smoothed = jnp.dot(along_ref[...], blat_ref[...], preferred_element_type=jnp.float32)
        total = pert_ref[0].astype(jnp.float32) * smoothed[0:lon_cells]
        for m in range(1, chunk):
            total = total + pert_ref[m].astype(jnp.float32) * smoothed[
                m * padded:m * padded + lon_cells
            ]

        @pl.when(step == 0)
        def _():
            acc_ref[...] = jnp.zeros(acc_ref.shape, acc_ref.dtype)

        acc_ref[0:lon_cells, :] = acc_ref[0:lon_cells, :] + total

        @pl.when(step == steps - 1)
        def _():
            out_ref[...] = acc_ref[...]

    field = pl.BlockSpec((chunk, None, lon_cells, lat_cells), lambda g: (g, 0, 0, 0))
    halo = pl.BlockSpec((chunk, None, radius, lat_cells), lambda g: (g, 0, 0, 0))
    whole = lambda shape: pl.BlockSpec(shape, lambda g: (0,) * len(shape))
    return pl.pallas_call(
        kernel,
        grid=(steps,),
        in_specs=[
            field,
            halo,
            halo,
            field,
            whole(band_lon.shape),
            whole(band_lat.shape),
        ],
        out_specs=whole((padded, lat_cells)),
        out_shape=jax.ShapeDtypeStruct((padded, lat_cells), jnp.float32),
        scratch_shapes=[
            pltpu.VMEM((ext_cells, lat_cells), jnp.bfloat16),
            pltpu.VMEM((chunk * padded, lat_cells), jnp.bfloat16),
            pltpu.VMEM((padded, lat_cells), jnp.float32),
        ],
        compiler_params=pltpu.CompilerParams(dimension_semantics=("arbitrary",)),
    )(control, c_low, c_high, perturb, band_lon, band_lat)


def pick_partials(field, cells):
    padded, lat_cells = field.shape
    count = cells.shape[1]
    block = obs_chunk(count)

    def kernel(field_ref, cells_ref, out_ref):
        pieces = split3(field_ref[...])
        for start in range(0, count, block):
            onehot_rows, onehot_cols = cell_onehots(
                cells_ref[:, start:start + block], padded, lat_cells
            )
            at_rows = jnp.dot(pieces[0], onehot_cols, preferred_element_type=jnp.float32)
            at_rows = at_rows + jnp.dot(pieces[1], onehot_cols, preferred_element_type=jnp.float32)
            at_rows = at_rows + jnp.dot(pieces[2], onehot_cols, preferred_element_type=jnp.float32)
            out_ref[:, start:start + block] = jnp.sum(
                jnp.where(onehot_rows, at_rows, 0.0), axis=0, keepdims=True
            )

    return pl.pallas_call(kernel, out_shape=jax.ShapeDtypeStruct((1, count), jnp.float32))(
        field, cells
    )


def spread_misfits(at_cells, lists, cells_col, lon_cells, lat_cells, radius, padded):
    count = lists.shape[1]
    block = obs_chunk(count)

    def kernel(at_ref, lists_ref, col_ref, spread_ref, low_ref, high_ref):
        misfit = lists_ref[1:2, :] * (at_ref[...] - lists_ref[0:1, :])
        cells = lists_ref[2:3, :]
        rows = jnp.floor((cells + 0.5) / lat_cells).astype(jnp.int32)
        total = jnp.zeros((padded, lat_cells), jnp.float32)
        for start in range(0, count, block):
            row_ids = lax.broadcasted_iota(jnp.int32, (padded, block), 0)
            weighted = jnp.where(
                row_ids == rows[:, start:start + block], misfit[:, start:start + block], 0.0
            )
            col_ids = lax.broadcasted_iota(jnp.int32, (block, lat_cells), 1)
            onehot_cols = jnp.where(
                col_ids == col_ref[start:start + block, :], 1.0, 0.0
            ).astype(jnp.bfloat16)
            for piece in split3(weighted):
                total = total + jnp.dot(piece, onehot_cols, preferred_element_type=jnp.float32)
        spread_ref[...] = total[0:lon_cells]
        low_ref[...] = total[lon_cells - radius:lon_cells]
        high_ref[...] = total[0:radius]

    return pl.pallas_call(
        kernel,
        out_shape=(
            jax.ShapeDtypeStruct((lon_cells, lat_cells), jnp.float32),
            jax.ShapeDtypeStruct((radius, lat_cells), jnp.float32),
            jax.ShapeDtypeStruct((radius, lat_cells), jnp.float32),
        ),
    )(at_cells, lists, cells_col)


def backward_grad(perturb, p_low, p_high, spread, s_low, s_high, control, band_lon, band_lat):
    members, levels, lon_cells, lat_cells = control.shape
    radius = p_low.shape[2]
    padded, ext_cells = band_lon.shape
    chunk = member_chunk(members)

    def kernel(pert_ref, plow_ref, phigh_ref, spread_ref, slow_ref, shigh_ref, ctrl_ref,
               blon_ref, blat_ref, out_ref, ext_ref, along_ref):
        blon = blon_ref[...]
        spread = spread_ref[...]
        s_lo = slow_ref[...]
        s_hi = shigh_ref[...]
        for m in range(chunk):
            fill_ext(
                ext_ref,
                (pert_ref[m].astype(jnp.float32) * spread).astype(jnp.bfloat16),
                (plow_ref[m].astype(jnp.float32) * s_lo).astype(jnp.bfloat16),
                (phigh_ref[m].astype(jnp.float32) * s_hi).astype(jnp.bfloat16),
                lon_cells,
                padded,
            )
            along = jnp.dot(blon, ext_ref[...], preferred_element_type=jnp.float32)
            along_ref[m * padded:(m + 1) * padded, :] = along.astype(jnp.bfloat16)
        smoothed = jnp.dot(along_ref[...], blat_ref[...], preferred_element_type=jnp.float32)
        for m in range(chunk):
            out_ref[m] = ctrl_ref[m].astype(jnp.float32) + smoothed[
                m * padded:m * padded + lon_cells
            ]

    field = pl.BlockSpec((chunk, None, lon_cells, lat_cells), lambda l, g: (g, l, 0, 0))
    halo = pl.BlockSpec((chunk, None, radius, lat_cells), lambda l, g: (g, l, 0, 0))
    level_field = pl.BlockSpec((None, lon_cells, lat_cells), lambda l, g: (l, 0, 0))
    level_halo = pl.BlockSpec((None, radius, lat_cells), lambda l, g: (l, 0, 0))
    out = pl.pallas_call(
        kernel,
        grid=(levels, members // chunk),
        in_specs=[
            field,
            halo,
            halo,
            level_field,
            level_halo,
            level_halo,
            field,
            pl.BlockSpec(band_lon.shape, lambda l, g: (0, 0)),
            pl.BlockSpec(band_lat.shape, lambda l, g: (0, 0)),
        ],
        out_specs=pl.BlockSpec((chunk, lon_cells, None, lat_cells), lambda l, g: (g, 0, l, 0)),
        out_shape=jax.ShapeDtypeStruct((members, lon_cells, levels, lat_cells), jnp.float32),
        scratch_shapes=[
            pltpu.VMEM((ext_cells, lat_cells), jnp.bfloat16),
            pltpu.VMEM((chunk * padded, lat_cells), jnp.bfloat16),
        ],
        compiler_params=pltpu.CompilerParams(dimension_semantics=("arbitrary", "arbitrary")),
    )(perturb, p_low, p_high, spread, s_low, s_high, control, band_lon, band_lat)
    return jnp.transpose(out, (0, 2, 1, 3))


def local(control, perturb, lon_taps, lat_taps, innov, inv_var, cell_index, counts):
    members_here, levels, lon_cells, lat_cells = control.shape
    radius = lon_taps.shape[0] - 1
    padded = -(-lon_cells // 16) * 16
    band_lon, band_lat = build_bands(lon_taps, lat_taps, lon_cells, padded, lat_cells)

    slot_ids = lax.broadcasted_iota(jnp.int32, innov.shape, 2)
    weights = jnp.where(slot_ids < counts[:, :, None], inv_var, 0.0)
    lists = jnp.stack([innov, weights, cell_index.astype(jnp.float32)])
    received = lax.all_to_all(lists, "tile", split_axis=2, concat_axis=1, tiled=True)
    received = received.reshape(3, -1)

    c_low, c_high = halos(control, "tile", 2, radius)
    late_perturb = lax.optimization_barrier((perturb, c_low, c_high))[0]
    p_low, p_high = halos(late_perturb, "tile", 2, radius)
    field = forward_sum(control, c_low, c_high, perturb, band_lon, band_lat)
    partial = pick_partials(field, received[2:3])
    at_cells = sum_over(partial, "mem")
    cells_hit = received[2].astype(jnp.int32)
    cells_col = (cells_hit % lat_cells)[:, None]
    spread, low_send, high_send = spread_misfits(
        at_cells, received, cells_col, lon_cells, lat_cells, radius, padded
    )
    count = lax.axis_size("tile")
    s_low = lax.ppermute(low_send, "tile", [(i, (i + 1) % count) for i in range(count)])
    s_high = lax.ppermute(high_send, "tile", [((i + 1) % count, i) for i in range(count)])
    return backward_grad(
        perturb,
        p_low,
        p_high,
        spread[None],
        s_low[None],
        s_high[None],
        control,
        band_lon,
        band_lat,
    )


def solution(mesh):
    return jax.shard_map(
        local,
        mesh=mesh,
        in_specs=(
            P("mem", None, "tile", None),
            P("mem", None, "tile", None),
            P(),
            P(),
            P("tile", None, None),
            P("tile", None, None),
            P("tile", None, None),
            P("tile", None),
        ),
        out_specs=P("mem", None, "tile", None),
        check_vma=False,
    )
```

```python
import math

import jax
import jax.numpy as jnp
from jax import lax
from jax.experimental import pallas as pl
from jax.experimental.pallas import tpu as pltpu
from jax.sharding import PartitionSpec as P


def halos(block, axis, dim, width):
    count = lax.axis_size(axis)
    forward = [(i, (i + 1) % count) for i in range(count)]
    backward = [((i + 1) % count, i) for i in range(count)]
    low = lax.ppermute(
        lax.slice_in_dim(block, block.shape[dim] - width, None, axis=dim), axis, forward
    )
    high = lax.ppermute(lax.slice_in_dim(block, 0, width, axis=dim), axis, backward)
    return low, high


def sum_over(values, axis):
    count = lax.axis_size(axis)
    total = values
    for shift in range(1, count):
        total = total + lax.ppermute(
            values, axis, [(i, (i + shift) % count) for i in range(count)]
        )
    return total


def select_chain(dist, taps_ref):
    band = jnp.zeros(dist.shape, jnp.float32)
    for offset in range(taps_ref.shape[0]):
        band = jnp.where(dist == offset, taps_ref[offset], band)
    return band.astype(jnp.bfloat16)


def build_bands(lon_taps, lat_taps, lon_cells, padded, lat_cells):
    radius = lon_taps.shape[0] - 1
    ext_cells = padded + 2 * radius
    tile = 128
    tiles = -(-lat_cells // tile)

    def kernel(lon_ref, lat_ref, blon_ref, blat_ref):
        rows = lax.broadcasted_iota(jnp.int32, (padded, ext_cells), 0)
        cols = lax.broadcasted_iota(jnp.int32, (padded, ext_cells), 1)
        source = jnp.where(
            cols < padded,
            cols,
            jnp.where(
                cols < padded + radius,
                cols - padded - radius,
                cols - padded - radius + lon_cells,
            ),
        )
        valid = (rows < lon_cells) & ((cols < lon_cells) | (cols >= padded))
        dist = jnp.where(valid, jnp.abs(source - rows), radius + 1)
        blon_ref[...] = select_chain(dist, lon_ref)

        t_rows = lax.broadcasted_iota(jnp.int32, (tile, tile), 0)
        t_cols = lax.broadcasted_iota(jnp.int32, (tile, tile), 1)
        blocks = {
            shift: select_chain(jnp.abs(t_rows - t_cols + shift * tile), lat_ref)
            for shift in (-1, 0, 1)
        }
        blat_ref[...] = jnp.zeros(blat_ref.shape, blat_ref.dtype)
        for a in range(tiles):
            for b in (a - 1, a, a + 1):
                if b < 0 or b >= tiles:
                    continue
                height = min(tile, lat_cells - a * tile)
                width = min(tile, lat_cells - b * tile)
                blat_ref[a * tile:a * tile + height, b * tile:b * tile + width] = blocks[a - b][
                    :height, :width
                ]

    smem = pl.BlockSpec(memory_space=pltpu.SMEM)
    return pl.pallas_call(
        kernel,
        in_specs=[smem, smem],
        out_shape=(
            jax.ShapeDtypeStruct((padded, ext_cells), jnp.bfloat16),
            jax.ShapeDtypeStruct((lat_cells, lat_cells), jnp.bfloat16),
        ),
    )(lon_taps.astype(jnp.float32), lat_taps.astype(jnp.float32))


def member_chunk(members):
    for size in (5, 4, 3, 2, 1):
        if members % size == 0:
            return size
    return 1


def fill_ext(ext_ref, local, low, high, lon_cells, padded):
    radius = low.shape[0]
    base = (lon_cells // 16) * 16
    ext_ref[base:padded, :] = jnp.zeros((padded - base, ext_ref.shape[1]), ext_ref.dtype)
    ext_ref[0:lon_cells, :] = local
    ext_ref[padded:padded + radius, :] = low
    ext_ref[padded + radius:padded + 2 * radius, :] = high


def split3(values):
    hi = values.astype(jnp.bfloat16)
    rest = values - hi.astype(jnp.float32)
    mid = rest.astype(jnp.bfloat16)
    lo = (rest - mid.astype(jnp.float32)).astype(jnp.bfloat16)
    return hi, mid, lo


def cell_keys(cells, padded, lat_cells):
    rows = jnp.floor((cells + 0.5) / lat_cells)
    cols = (cells - rows * lat_cells).astype(jnp.int32)
    keys = (cols // 128) * padded + rows.astype(jnp.int32)
    lane_ids = lax.broadcasted_iota(jnp.int32, (128, cells.shape[1]), 0)
    onehot = jnp.where(lane_ids == cols % 128, 1.0, 0.0).astype(jnp.bfloat16)
    return keys, onehot


def forward_pick(control, c_low, c_high, perturb, band_lon, band_lat, cells):
    members, levels, lon_cells, lat_cells = control.shape
    radius = c_low.shape[2]
    padded, ext_cells = band_lon.shape
    chunk = member_chunk(members)
    steps = members // chunk
    _, sources, slots = cells.shape
    parts = -(-lat_cells // 128)

    def kernel(ctrl_ref, low_ref, high_ref, pert_ref, blon_ref, blat_ref, cells_ref, out_ref,
               ext_ref, along_ref, acc_ref, fold_ref):
        step = pl.program_id(0)
        blon = blon_ref[...]
        for m in range(chunk):
            fill_ext(ext_ref, ctrl_ref[m], low_ref[m], high_ref[m], lon_cells, padded)
            along = jnp.dot(blon, ext_ref[...], preferred_element_type=jnp.float32)
            along_ref[m * padded:(m + 1) * padded, :] = along.astype(jnp.bfloat16)
        smoothed = jnp.dot(along_ref[...], blat_ref[...], preferred_element_type=jnp.float32)
        total = pert_ref[0].astype(jnp.float32) * smoothed[0:lon_cells]
        for m in range(1, chunk):
            total = total + pert_ref[m].astype(jnp.float32) * smoothed[
                m * padded:m * padded + lon_cells
            ]

        @pl.when(step == 0)
        def _():
            acc_ref[...] = jnp.zeros(acc_ref.shape, acc_ref.dtype)

        acc_ref[0:lon_cells, :] = acc_ref[0:lon_cells, :] + total

        @pl.when(step == steps - 1)
        def _():
            fold_ref[...] = jnp.zeros(fold_ref.shape, fold_ref.dtype)
            for part in range(parts):
                width = min(128, lat_cells - part * 128)
                fold_ref[part * padded:(part + 1) * padded, 0:width] = acc_ref[
                    :, part * 128:part * 128 + width
                ]
            pieces = split3(fold_ref[...])
            key_ids = lax.broadcasted_iota(jnp.int32, (parts * padded, slots), 0)
            for row in range(sources):
                keys, onehot = cell_keys(cells_ref[2, row:row + 1, :], padded, lat_cells)
                at_keys = jnp.dot(pieces[0], onehot, preferred_element_type=jnp.float32)
                at_keys = at_keys + jnp.dot(pieces[1], onehot, preferred_element_type=jnp.float32)
                at_keys = at_keys + jnp.dot(pieces[2], onehot, preferred_element_type=jnp.float32)
                out_ref[row:row + 1, :] = jnp.sum(
                    jnp.where(key_ids == keys, at_keys, 0.0), axis=0, keepdims=True
                )

    field = pl.BlockSpec((chunk, None, lon_cells, lat_cells), lambda g: (g, 0, 0, 0))
    halo = pl.BlockSpec((chunk, None, radius, lat_cells), lambda g: (g, 0, 0, 0))
    whole = lambda shape: pl.BlockSpec(shape, lambda g: (0,) * len(shape))
    return pl.pallas_call(
        kernel,
        grid=(steps,),
        in_specs=[
            field,
            halo,
            halo,
            field,
            whole(band_lon.shape),
            whole(band_lat.shape),
            whole(cells.shape),
        ],
        out_specs=whole((sources, slots)),
        out_shape=jax.ShapeDtypeStruct((sources, slots), jnp.float32),
        scratch_shapes=[
            pltpu.VMEM((ext_cells, lat_cells), jnp.bfloat16),
            pltpu.VMEM((chunk * padded, lat_cells), jnp.bfloat16),
            pltpu.VMEM((padded, lat_cells), jnp.float32),
            pltpu.VMEM((parts * padded, 128), jnp.float32),
        ],
        compiler_params=pltpu.CompilerParams(dimension_semantics=("arbitrary",)),
    )(control, c_low, c_high, perturb, band_lon, band_lat, cells)


def spread_misfits(at_cells, lists, lon_cells, lat_cells, radius, padded):
    _, sources, slots = lists.shape
    parts = -(-lat_cells // 128)

    def kernel(at_ref, lists_ref, spread_ref, low_ref, high_ref, fold_ref):
        key_ids = lax.broadcasted_iota(jnp.int32, (parts * padded, slots), 0)
        folded = jnp.zeros((parts * padded, 128), jnp.float32)
        for row in range(sources):
            misfit = lists_ref[1, row:row + 1, :] * (
                at_ref[row:row + 1, :] - lists_ref[0, row:row + 1, :]
            )
            keys, onehot = cell_keys(lists_ref[2, row:row + 1, :], padded, lat_cells)
            for piece in split3(misfit):
                weighted = jnp.where(key_ids == keys, piece.astype(jnp.float32), 0.0)
                folded = folded + lax.dot_general(
                    weighted.astype(jnp.bfloat16),
                    onehot,
                    (((1,), (1,)), ((), ())),
                    preferred_element_type=jnp.float32,
                )
        for part in range(parts):
            width = min(128, lat_cells - part * 128)
            fold_ref[:, part * 128:part * 128 + width] = folded[
                part * padded:(part + 1) * padded, 0:width
            ]
        spread_ref[...] = fold_ref[0:lon_cells, :]
        low_ref[...] = fold_ref[lon_cells - radius:lon_cells, :]
        high_ref[...] = fold_ref[0:radius, :]

    return pl.pallas_call(
        kernel,
        out_shape=(
            jax.ShapeDtypeStruct((lon_cells, lat_cells), jnp.float32),
            jax.ShapeDtypeStruct((radius, lat_cells), jnp.float32),
            jax.ShapeDtypeStruct((radius, lat_cells), jnp.float32),
        ),
        scratch_shapes=[pltpu.VMEM((padded, lat_cells), jnp.float32)],
    )(at_cells, lists)


def backward_grad(perturb, p_low, p_high, spread, s_low, s_high, control, band_lon, band_lat):
    members, levels, lon_cells, lat_cells = control.shape
    radius = p_low.shape[2]
    padded, ext_cells = band_lon.shape
    chunk = member_chunk(members)

    def kernel(pert_ref, plow_ref, phigh_ref, spread_ref, slow_ref, shigh_ref, ctrl_ref,
               blon_ref, blat_ref, out_ref, ext_ref, along_ref):
        blon = blon_ref[...]
        spread = spread_ref[...]
        s_lo = slow_ref[...]
        s_hi = shigh_ref[...]
        for m in range(chunk):
            fill_ext(
                ext_ref,
                (pert_ref[m].astype(jnp.float32) * spread).astype(jnp.bfloat16),
                (plow_ref[m].astype(jnp.float32) * s_lo).astype(jnp.bfloat16),
                (phigh_ref[m].astype(jnp.float32) * s_hi).astype(jnp.bfloat16),
                lon_cells,
                padded,
            )
            along = jnp.dot(blon, ext_ref[...], preferred_element_type=jnp.float32)
            along_ref[m * padded:(m + 1) * padded, :] = along.astype(jnp.bfloat16)
        smoothed = jnp.dot(along_ref[...], blat_ref[...], preferred_element_type=jnp.float32)
        for m in range(chunk):
            out_ref[m] = ctrl_ref[m].astype(jnp.float32) + smoothed[
                m * padded:m * padded + lon_cells
            ]

    field = pl.BlockSpec((chunk, None, lon_cells, lat_cells), lambda l, g: (g, l, 0, 0))
    halo = pl.BlockSpec((chunk, None, radius, lat_cells), lambda l, g: (g, l, 0, 0))
    level_field = pl.BlockSpec((None, lon_cells, lat_cells), lambda l, g: (l, 0, 0))
    level_halo = pl.BlockSpec((None, radius, lat_cells), lambda l, g: (l, 0, 0))
    out = pl.pallas_call(
        kernel,
        grid=(levels, members // chunk),
        in_specs=[
            field,
            halo,
            halo,
            level_field,
            level_halo,
            level_halo,
            field,
            pl.BlockSpec(band_lon.shape, lambda l, g: (0, 0)),
            pl.BlockSpec(band_lat.shape, lambda l, g: (0, 0)),
        ],
        out_specs=pl.BlockSpec((chunk, lon_cells, None, lat_cells), lambda l, g: (g, 0, l, 0)),
        out_shape=jax.ShapeDtypeStruct((members, lon_cells, levels, lat_cells), jnp.float32),
        scratch_shapes=[
            pltpu.VMEM((ext_cells, lat_cells), jnp.bfloat16),
            pltpu.VMEM((chunk * padded, lat_cells), jnp.bfloat16),
        ],
        compiler_params=pltpu.CompilerParams(dimension_semantics=("arbitrary", "arbitrary")),
    )(perturb, p_low, p_high, spread, s_low, s_high, control, band_lon, band_lat)
    return jnp.transpose(out, (0, 2, 1, 3))


def local(control, perturb, lon_taps, lat_taps, innov, inv_var, cell_index, counts):
    members_here, levels, lon_cells, lat_cells = control.shape
    radius = lon_taps.shape[0] - 1
    padded = -(-lon_cells // 16) * 16
    band_lon, band_lat = build_bands(lon_taps, lat_taps, lon_cells, padded, lat_cells)

    slot_ids = lax.broadcasted_iota(jnp.int32, innov.shape, 2)
    weights = jnp.where(slot_ids < counts[:, :, None], inv_var, 0.0)
    lists = jnp.concatenate([innov, weights, cell_index.astype(jnp.float32)])
    received = lax.all_to_all(lists, "tile", split_axis=1, concat_axis=1, tiled=True)

    c_low, c_high = halos(control, "tile", 2, radius)
    late_perturb = lax.optimization_barrier((perturb, c_low, c_high))[0]
    p_low, p_high = halos(late_perturb, "tile", 2, radius)
    partial = forward_pick(
        control, c_low, c_high, perturb, band_lon, band_lat, received
    )
    at_cells = sum_over(partial, "mem")
    spread, low_send, high_send = spread_misfits(
        at_cells, received, lon_cells, lat_cells, radius, padded
    )
    count = lax.axis_size("tile")
    s_low = lax.ppermute(low_send, "tile", [(i, (i + 1) % count) for i in range(count)])
    s_high = lax.ppermute(high_send, "tile", [((i + 1) % count, i) for i in range(count)])
    return backward_grad(
        perturb,
        p_low,
        p_high,
        spread[None],
        s_low[None],
        s_high[None],
        control,
        band_lon,
        band_lat,
    )


def solution(mesh):
    return jax.shard_map(
        local,
        mesh=mesh,
        in_specs=(
            P("mem", None, "tile", None),
            P("mem", None, "tile", None),
            P(),
            P(),
            P("tile", None, None),
            P("tile", None, None),
            P("tile", None, None),
            P("tile", None),
        ),
        out_specs=P("mem", None, "tile", None),
        check_vma=False,
    )
```

```python
import math

import jax
import jax.numpy as jnp
from jax import lax
from jax.experimental import pallas as pl
from jax.experimental.pallas import tpu as pltpu
from jax.sharding import PartitionSpec as P


def halos(block, axis, dim, width):
    count = lax.axis_size(axis)
    forward = [(i, (i + 1) % count) for i in range(count)]
    backward = [((i + 1) % count, i) for i in range(count)]
    low = lax.ppermute(
        lax.slice_in_dim(block, block.shape[dim] - width, None, axis=dim), axis, forward
    )
    high = lax.ppermute(lax.slice_in_dim(block, 0, width, axis=dim), axis, backward)
    return low, high


def sum_over(values, axis):
    count = lax.axis_size(axis)
    total = values
    for shift in range(1, count):
        total = total + lax.ppermute(
            values, axis, [(i, (i + shift) % count) for i in range(count)]
        )
    return total


def select_chain(dist, taps_ref):
    band = jnp.zeros(dist.shape, jnp.float32)
    for offset in range(taps_ref.shape[0]):
        band = jnp.where(dist == offset, taps_ref[offset], band)
    return band.astype(jnp.bfloat16)


def build_bands(lon_taps, lat_taps, lon_cells, padded, lat_cells):
    radius = lon_taps.shape[0] - 1
    ext_cells = padded + 2 * radius
    tile = 128
    tiles = -(-lat_cells // tile)

    def kernel(lon_ref, lat_ref, blon_ref, blat_ref):
        rows = lax.broadcasted_iota(jnp.int32, (padded, ext_cells), 0)
        cols = lax.broadcasted_iota(jnp.int32, (padded, ext_cells), 1)
        source = jnp.where(
            cols < padded,
            cols,
            jnp.where(
                cols < padded + radius,
                cols - padded - radius,
                cols - padded - radius + lon_cells,
            ),
        )
        valid = (rows < lon_cells) & ((cols < lon_cells) | (cols >= padded))
        dist = jnp.where(valid, jnp.abs(source - rows), radius + 1)
        blon_ref[...] = select_chain(dist, lon_ref)

        t_rows = lax.broadcasted_iota(jnp.int32, (tile, tile), 0)
        t_cols = lax.broadcasted_iota(jnp.int32, (tile, tile), 1)
        blocks = {
            shift: select_chain(jnp.abs(t_rows - t_cols + shift * tile), lat_ref)
            for shift in (-1, 0, 1)
        }
        blat_ref[...] = jnp.zeros(blat_ref.shape, blat_ref.dtype)
        for a in range(tiles):
            for b in (a - 1, a, a + 1):
                if b < 0 or b >= tiles:
                    continue
                height = min(tile, lat_cells - a * tile)
                width = min(tile, lat_cells - b * tile)
                blat_ref[a * tile:a * tile + height, b * tile:b * tile + width] = blocks[a - b][
                    :height, :width
                ]

    smem = pl.BlockSpec(memory_space=pltpu.SMEM)
    return pl.pallas_call(
        kernel,
        in_specs=[smem, smem],
        out_shape=(
            jax.ShapeDtypeStruct((padded, ext_cells), jnp.bfloat16),
            jax.ShapeDtypeStruct((lat_cells, lat_cells), jnp.bfloat16),
        ),
    )(lon_taps.astype(jnp.float32), lat_taps.astype(jnp.float32))


def member_chunk(members):
    for size in (5, 4, 3, 2, 1):
        if members % size == 0:
            return size
    return 1


def fill_ext(ext_ref, local, low, high, lon_cells, padded):
    radius = low.shape[0]
    base = (lon_cells // 16) * 16
    ext_ref[base:padded, :] = jnp.zeros((padded - base, ext_ref.shape[1]), ext_ref.dtype)
    ext_ref[0:lon_cells, :] = local
    ext_ref[padded:padded + radius, :] = low
    ext_ref[padded + radius:padded + 2 * radius, :] = high


def split3(values):
    hi = values.astype(jnp.bfloat16)
    rest = values - hi.astype(jnp.float32)
    mid = rest.astype(jnp.bfloat16)
    lo = (rest - mid.astype(jnp.float32)).astype(jnp.bfloat16)
    return hi, mid, lo


def cell_keys(cells, padded, lat_cells):
    rows = jnp.floor((cells + 0.5) / lat_cells)
    cols = (cells - rows * lat_cells).astype(jnp.int32)
    keys = (cols // 128) * padded + rows.astype(jnp.int32)
    lane_ids = lax.broadcasted_iota(jnp.int32, (128, cells.shape[1]), 0)
    onehot = jnp.where(lane_ids == cols % 128, 1.0, 0.0).astype(jnp.bfloat16)
    return keys, onehot


def forward_pick(control, c_low, c_high, perturb, band_lon, band_lat, cells):
    members, levels, lon_cells, lat_cells = control.shape
    radius = c_low.shape[2]
    padded, ext_cells = band_lon.shape
    chunk = member_chunk(members)
    steps = members // chunk
    _, sources, slots = cells.shape
    parts = -(-lat_cells // 128)

    def kernel(ctrl_ref, low_ref, high_ref, pert_ref, blon_ref, blat_ref, cells_ref, out_ref,
               ext_ref, along_ref, acc_ref, fold_ref):
        step = pl.program_id(0)
        blon = blon_ref[...]
        for m in range(chunk):
            fill_ext(ext_ref, ctrl_ref[m], low_ref[m], high_ref[m], lon_cells, padded)
            along = jnp.dot(blon, ext_ref[...], preferred_element_type=jnp.float32)
            along_ref[m * padded:(m + 1) * padded, :] = along.astype(jnp.bfloat16)
        smoothed = jnp.dot(along_ref[...], blat_ref[...], preferred_element_type=jnp.float32)
        total = pert_ref[0].astype(jnp.float32) * smoothed[0:lon_cells]
        for m in range(1, chunk):
            total = total + pert_ref[m].astype(jnp.float32) * smoothed[
                m * padded:m * padded + lon_cells
            ]

        @pl.when(step == 0)
        def _():
            acc_ref[...] = jnp.zeros(acc_ref.shape, acc_ref.dtype)

        acc_ref[0:lon_cells, :] = acc_ref[0:lon_cells, :] + total

        @pl.when(step == steps - 1)
        def _():
            fold_ref[...] = jnp.zeros(fold_ref.shape, fold_ref.dtype)
            for part in range(parts):
                width = min(128, lat_cells - part * 128)
                fold_ref[part * padded:(part + 1) * padded, 0:width] = acc_ref[
                    :, part * 128:part * 128 + width
                ]
            pieces = split3(fold_ref[...])
            key_ids = lax.broadcasted_iota(jnp.int32, (parts * padded, slots), 0)
            for row in range(sources):
                keys, onehot = cell_keys(cells_ref[2, row:row + 1, :], padded, lat_cells)
                at_keys = jnp.dot(pieces[0], onehot, preferred_element_type=jnp.float32)
                at_keys = at_keys + jnp.dot(pieces[1], onehot, preferred_element_type=jnp.float32)
                at_keys = at_keys + jnp.dot(pieces[2], onehot, preferred_element_type=jnp.float32)
                out_ref[row:row + 1, :] = jnp.sum(
                    jnp.where(key_ids == keys, at_keys, 0.0), axis=0, keepdims=True
                )

    field = pl.BlockSpec((chunk, None, lon_cells, lat_cells), lambda g: (g, 0, 0, 0))
    halo = pl.BlockSpec((chunk, None, radius, lat_cells), lambda g: (g, 0, 0, 0))
    whole = lambda shape: pl.BlockSpec(shape, lambda g: (0,) * len(shape))
    return pl.pallas_call(
        kernel,
        grid=(steps,),
        in_specs=[
            field,
            halo,
            halo,
            field,
            whole(band_lon.shape),
            whole(band_lat.shape),
            whole(cells.shape),
        ],
        out_specs=whole((sources, slots)),
        out_shape=jax.ShapeDtypeStruct((sources, slots), jnp.float32),
        scratch_shapes=[
            pltpu.VMEM((ext_cells, lat_cells), jnp.bfloat16),
            pltpu.VMEM((chunk * padded, lat_cells), jnp.bfloat16),
            pltpu.VMEM((padded, lat_cells), jnp.float32),
            pltpu.VMEM((parts * padded, 128), jnp.float32),
        ],
        compiler_params=pltpu.CompilerParams(dimension_semantics=("arbitrary",)),
    )(control, c_low, c_high, perturb, band_lon, band_lat, cells)


def spread_misfits(at_cells, lists, lon_cells, lat_cells, radius, padded):
    _, sources, slots = lists.shape
    parts = -(-lat_cells // 128)

    def kernel(at_ref, lists_ref, spread_ref, low_ref, high_ref, fold_ref):
        key_ids = lax.broadcasted_iota(jnp.int32, (parts * padded, slots), 0)
        folded = jnp.zeros((parts * padded, 128), jnp.float32)
        for row in range(sources):
            misfit = lists_ref[1, row:row + 1, :] * (
                at_ref[row:row + 1, :] - lists_ref[0, row:row + 1, :]
            )
            keys, onehot = cell_keys(lists_ref[2, row:row + 1, :], padded, lat_cells)
            for piece in split3(misfit):
                weighted = jnp.where(key_ids == keys, piece.astype(jnp.float32), 0.0)
                folded = folded + lax.dot_general(
                    weighted.astype(jnp.bfloat16),
                    onehot,
                    (((1,), (1,)), ((), ())),
                    preferred_element_type=jnp.float32,
                )
        for part in range(parts):
            width = min(128, lat_cells - part * 128)
            fold_ref[:, part * 128:part * 128 + width] = folded[
                part * padded:(part + 1) * padded, 0:width
            ]
        spread_ref[...] = fold_ref[0:lon_cells, :]
        low_ref[...] = fold_ref[lon_cells - radius:lon_cells, :]
        high_ref[...] = fold_ref[0:radius, :]

    return pl.pallas_call(
        kernel,
        out_shape=(
            jax.ShapeDtypeStruct((lon_cells, lat_cells), jnp.float32),
            jax.ShapeDtypeStruct((radius, lat_cells), jnp.float32),
            jax.ShapeDtypeStruct((radius, lat_cells), jnp.float32),
        ),
        scratch_shapes=[pltpu.VMEM((padded, lat_cells), jnp.float32)],
    )(at_cells, lists)


def backward_grad(perturb, p_low, p_high, spread, s_low, s_high, control, band_lon, band_lat):
    members, levels, lon_cells, lat_cells = control.shape
    radius = p_low.shape[2]
    padded, ext_cells = band_lon.shape
    chunk = member_chunk(members)

    def kernel(pert_ref, plow_ref, phigh_ref, spread_ref, slow_ref, shigh_ref, ctrl_ref,
               blon_ref, blat_ref, out_ref, ext_ref, along_ref):
        blon = blon_ref[...]
        spread = spread_ref[...]
        s_lo = slow_ref[...]
        s_hi = shigh_ref[...]
        for m in range(chunk):
            fill_ext(
                ext_ref,
                (pert_ref[m].astype(jnp.float32) * spread).astype(jnp.bfloat16),
                (plow_ref[m].astype(jnp.float32) * s_lo).astype(jnp.bfloat16),
                (phigh_ref[m].astype(jnp.float32) * s_hi).astype(jnp.bfloat16),
                lon_cells,
                padded,
            )
            along = jnp.dot(blon, ext_ref[...], preferred_element_type=jnp.float32)
            along_ref[m * padded:(m + 1) * padded, :] = along.astype(jnp.bfloat16)
        smoothed = jnp.dot(along_ref[...], blat_ref[...], preferred_element_type=jnp.float32)
        for m in range(chunk):
            out_ref[m] = ctrl_ref[m].astype(jnp.float32) + smoothed[
                m * padded:m * padded + lon_cells
            ]

    field = pl.BlockSpec((chunk, None, lon_cells, lat_cells), lambda l, g: (g, l, 0, 0))
    halo = pl.BlockSpec((chunk, None, radius, lat_cells), lambda l, g: (g, l, 0, 0))
    level_field = pl.BlockSpec((None, lon_cells, lat_cells), lambda l, g: (l, 0, 0))
    level_halo = pl.BlockSpec((None, radius, lat_cells), lambda l, g: (l, 0, 0))
    out = pl.pallas_call(
        kernel,
        grid=(levels, members // chunk),
        in_specs=[
            field,
            halo,
            halo,
            level_field,
            level_halo,
            level_halo,
            field,
            pl.BlockSpec(band_lon.shape, lambda l, g: (0, 0)),
            pl.BlockSpec(band_lat.shape, lambda l, g: (0, 0)),
        ],
        out_specs=pl.BlockSpec((chunk, lon_cells, None, lat_cells), lambda l, g: (g, 0, l, 0)),
        out_shape=jax.ShapeDtypeStruct((members, lon_cells, levels, lat_cells), jnp.float32),
        scratch_shapes=[
            pltpu.VMEM((ext_cells, lat_cells), jnp.bfloat16),
            pltpu.VMEM((chunk * padded, lat_cells), jnp.bfloat16),
        ],
        compiler_params=pltpu.CompilerParams(dimension_semantics=("arbitrary", "arbitrary")),
    )(perturb, p_low, p_high, spread, s_low, s_high, control, band_lon, band_lat)
    return jnp.transpose(out, (0, 2, 1, 3))


def local(control, perturb, lon_taps, lat_taps, innov, inv_var, cell_index, counts):
    members_here, levels, lon_cells, lat_cells = control.shape
    radius = lon_taps.shape[0] - 1
    padded = -(-lon_cells // 16) * 16
    band_lon, band_lat = build_bands(lon_taps, lat_taps, lon_cells, padded, lat_cells)

    slot_ids = lax.broadcasted_iota(jnp.int32, innov.shape, 2)
    weights = jnp.where(slot_ids < counts[:, :, None], inv_var, 0.0)
    lists = jnp.concatenate([innov, weights, cell_index.astype(jnp.float32)])
    received = lax.all_to_all(lists, "tile", split_axis=1, concat_axis=1, tiled=True)

    c_low, c_high = halos(control, "tile", 2, radius)
    c_low, c_high, received = lax.optimization_barrier((c_low, c_high, received))
    late_perturb = lax.optimization_barrier((perturb, c_low, c_high))[0]
    p_low, p_high = halos(late_perturb, "tile", 2, radius)
    partial = forward_pick(
        control, c_low, c_high, perturb, band_lon, band_lat, received
    )
    at_cells = sum_over(partial, "mem")
    spread, low_send, high_send = spread_misfits(
        at_cells, received, lon_cells, lat_cells, radius, padded
    )
    count = lax.axis_size("tile")
    s_low = lax.ppermute(low_send, "tile", [(i, (i + 1) % count) for i in range(count)])
    s_high = lax.ppermute(high_send, "tile", [((i + 1) % count, i) for i in range(count)])
    return backward_grad(
        perturb,
        p_low,
        p_high,
        spread[None],
        s_low[None],
        s_high[None],
        control,
        band_lon,
        band_lat,
    )


def solution(mesh):
    return jax.shard_map(
        local,
        mesh=mesh,
        in_specs=(
            P("mem", None, "tile", None),
            P("mem", None, "tile", None),
            P(),
            P(),
            P("tile", None, None),
            P("tile", None, None),
            P("tile", None, None),
            P("tile", None),
        ),
        out_specs=P("mem", None, "tile", None),
        check_vma=False,
    )
```

```python
import math

import jax
import jax.numpy as jnp
from jax import lax
from jax.experimental import pallas as pl
from jax.experimental.pallas import tpu as pltpu
from jax.sharding import PartitionSpec as P


def halos(block, axis, dim, width):
    count = lax.axis_size(axis)
    forward = [(i, (i + 1) % count) for i in range(count)]
    backward = [((i + 1) % count, i) for i in range(count)]
    low = lax.ppermute(
        lax.slice_in_dim(block, block.shape[dim] - width, None, axis=dim), axis, forward
    )
    high = lax.ppermute(lax.slice_in_dim(block, 0, width, axis=dim), axis, backward)
    return low, high


def sum_over(values, axis):
    count = lax.axis_size(axis)
    total = values
    for shift in range(1, count):
        total = total + lax.ppermute(
            values, axis, [(i, (i + shift) % count) for i in range(count)]
        )
    return total


def select_chain(dist, taps_ref):
    band = jnp.zeros(dist.shape, jnp.float32)
    for offset in range(taps_ref.shape[0]):
        band = jnp.where(dist == offset, taps_ref[offset], band)
    return band.astype(jnp.bfloat16)


def build_bands(lon_taps, lat_taps, lon_cells, padded, lat_cells):
    radius = lon_taps.shape[0] - 1
    ext_cells = padded + 2 * radius
    tile = 128
    tiles = -(-lat_cells // tile)

    def kernel(lon_ref, lat_ref, blon_ref, blat_ref):
        rows = lax.broadcasted_iota(jnp.int32, (padded, ext_cells), 0)
        cols = lax.broadcasted_iota(jnp.int32, (padded, ext_cells), 1)
        source = jnp.where(
            cols < padded,
            cols,
            jnp.where(
                cols < padded + radius,
                cols - padded - radius,
                cols - padded - radius + lon_cells,
            ),
        )
        valid = (rows < lon_cells) & ((cols < lon_cells) | (cols >= padded))
        dist = jnp.where(valid, jnp.abs(source - rows), radius + 1)
        blon_ref[...] = select_chain(dist, lon_ref)

        t_rows = lax.broadcasted_iota(jnp.int32, (tile, tile), 0)
        t_cols = lax.broadcasted_iota(jnp.int32, (tile, tile), 1)
        blocks = {
            shift: select_chain(jnp.abs(t_rows - t_cols + shift * tile), lat_ref)
            for shift in (-1, 0, 1)
        }
        blat_ref[...] = jnp.zeros(blat_ref.shape, blat_ref.dtype)
        for a in range(tiles):
            for b in (a - 1, a, a + 1):
                if b < 0 or b >= tiles:
                    continue
                height = min(tile, lat_cells - a * tile)
                width = min(tile, lat_cells - b * tile)
                blat_ref[a * tile:a * tile + height, b * tile:b * tile + width] = blocks[a - b][
                    :height, :width
                ]

    smem = pl.BlockSpec(memory_space=pltpu.SMEM)
    return pl.pallas_call(
        kernel,
        in_specs=[smem, smem],
        out_shape=(
            jax.ShapeDtypeStruct((padded, ext_cells), jnp.bfloat16),
            jax.ShapeDtypeStruct((lat_cells, lat_cells), jnp.bfloat16),
        ),
    )(lon_taps.astype(jnp.float32), lat_taps.astype(jnp.float32))


def member_chunk(members):
    for size in (5, 4, 3, 2, 1):
        if members % size == 0:
            return size
    return 1


def fill_ext(ext_ref, local, low, high, lon_cells, padded):
    radius = low.shape[0]
    base = (lon_cells // 16) * 16
    ext_ref[base:padded, :] = jnp.zeros((padded - base, ext_ref.shape[1]), ext_ref.dtype)
    ext_ref[0:lon_cells, :] = local
    ext_ref[padded:padded + radius, :] = low
    ext_ref[padded + radius:padded + 2 * radius, :] = high


def split3(values):
    hi = values.astype(jnp.bfloat16)
    rest = values - hi.astype(jnp.float32)
    mid = rest.astype(jnp.bfloat16)
    lo = (rest - mid.astype(jnp.float32)).astype(jnp.bfloat16)
    return hi, mid, lo


def cell_keys(cells, padded, lat_cells):
    rows = jnp.floor((cells + 0.5) / lat_cells)
    cols = (cells - rows * lat_cells).astype(jnp.int32)
    keys = (cols // 128) * padded + rows.astype(jnp.int32)
    lane_ids = lax.broadcasted_iota(jnp.int32, (128, cells.shape[1]), 0)
    onehot = jnp.where(lane_ids == cols % 128, 1.0, 0.0).astype(jnp.bfloat16)
    return keys, onehot


def forward_pick(control, c_low, c_high, perturb, band_lon, band_lat, cells):
    members, levels, lon_cells, lat_cells = control.shape
    radius = c_low.shape[2]
    padded, ext_cells = band_lon.shape
    chunk = member_chunk(members)
    steps = members // chunk
    _, sources, slots = cells.shape
    parts = -(-lat_cells // 128)

    def kernel(ctrl_ref, low_ref, high_ref, pert_ref, blon_ref, blat_ref, cells_ref, out_ref,
               ext_ref, along_ref, acc_ref, fold_ref):
        step = pl.program_id(0)
        blon = blon_ref[...]
        for m in range(chunk):
            fill_ext(ext_ref, ctrl_ref[m], low_ref[m], high_ref[m], lon_cells, padded)
            along = jnp.dot(blon, ext_ref[...], preferred_element_type=jnp.float32)
            along_ref[m * padded:(m + 1) * padded, :] = along.astype(jnp.bfloat16)
        smoothed = jnp.dot(along_ref[...], blat_ref[...], preferred_element_type=jnp.float32)
        total = pert_ref[0].astype(jnp.float32) * smoothed[0:lon_cells]
        for m in range(1, chunk):
            total = total + pert_ref[m].astype(jnp.float32) * smoothed[
                m * padded:m * padded + lon_cells
            ]

        @pl.when(step == 0)
        def _():
            acc_ref[...] = jnp.zeros(acc_ref.shape, acc_ref.dtype)

        acc_ref[0:lon_cells, :] = acc_ref[0:lon_cells, :] + total

        @pl.when(step == steps - 1)
        def _():
            fold_ref[...] = jnp.zeros(fold_ref.shape, fold_ref.dtype)
            for part in range(parts):
                width = min(128, lat_cells - part * 128)
                fold_ref[part * padded:(part + 1) * padded, 0:width] = acc_ref[
                    :, part * 128:part * 128 + width
                ]
            pieces = split3(fold_ref[...])
            key_ids = lax.broadcasted_iota(jnp.int32, (parts * padded, slots), 0)
            for row in range(sources):
                keys, onehot = cell_keys(cells_ref[2, row:row + 1, :], padded, lat_cells)
                at_keys = jnp.dot(pieces[0], onehot, preferred_element_type=jnp.float32)
                at_keys = at_keys + jnp.dot(pieces[1], onehot, preferred_element_type=jnp.float32)
                at_keys = at_keys + jnp.dot(pieces[2], onehot, preferred_element_type=jnp.float32)
                out_ref[row:row + 1, :] = jnp.sum(
                    jnp.where(key_ids == keys, at_keys, 0.0), axis=0, keepdims=True
                )

    field = pl.BlockSpec((chunk, None, lon_cells, lat_cells), lambda g: (g, 0, 0, 0))
    halo = pl.BlockSpec((chunk, None, radius, lat_cells), lambda g: (g, 0, 0, 0))
    whole = lambda shape: pl.BlockSpec(shape, lambda g: (0,) * len(shape))
    return pl.pallas_call(
        kernel,
        grid=(steps,),
        in_specs=[
            field,
            halo,
            halo,
            field,
            whole(band_lon.shape),
            whole(band_lat.shape),
            whole(cells.shape),
        ],
        out_specs=whole((sources, slots)),
        out_shape=jax.ShapeDtypeStruct((sources, slots), jnp.float32),
        scratch_shapes=[
            pltpu.VMEM((ext_cells, lat_cells), jnp.bfloat16),
            pltpu.VMEM((chunk * padded, lat_cells), jnp.bfloat16),
            pltpu.VMEM((padded, lat_cells), jnp.float32),
            pltpu.VMEM((parts * padded, 128), jnp.float32),
        ],
        compiler_params=pltpu.CompilerParams(dimension_semantics=("arbitrary",)),
    )(control, c_low, c_high, perturb, band_lon, band_lat, cells)


def spread_misfits(at_cells, lists, lon_cells, lat_cells, radius, padded):
    _, sources, slots = lists.shape
    parts = -(-lat_cells // 128)

    def kernel(at_ref, lists_ref, spread_ref, low_ref, high_ref, fold_ref):
        key_ids = lax.broadcasted_iota(jnp.int32, (parts * padded, slots), 0)
        folded = jnp.zeros((parts * padded, 128), jnp.float32)
        for row in range(sources):
            misfit = lists_ref[1, row:row + 1, :] * (
                at_ref[row:row + 1, :] - lists_ref[0, row:row + 1, :]
            )
            keys, onehot = cell_keys(lists_ref[2, row:row + 1, :], padded, lat_cells)
            for piece in split3(misfit):
                weighted = jnp.where(key_ids == keys, piece.astype(jnp.float32), 0.0)
                folded = folded + lax.dot_general(
                    weighted.astype(jnp.bfloat16),
                    onehot,
                    (((1,), (1,)), ((), ())),
                    preferred_element_type=jnp.float32,
                )
        for part in range(parts):
            width = min(128, lat_cells - part * 128)
            fold_ref[:, part * 128:part * 128 + width] = folded[
                part * padded:(part + 1) * padded, 0:width
            ]
        spread_ref[...] = fold_ref[0:lon_cells, :]
        low_ref[...] = fold_ref[lon_cells - radius:lon_cells, :]
        high_ref[...] = fold_ref[0:radius, :]

    return pl.pallas_call(
        kernel,
        out_shape=(
            jax.ShapeDtypeStruct((lon_cells, lat_cells), jnp.float32),
            jax.ShapeDtypeStruct((radius, lat_cells), jnp.float32),
            jax.ShapeDtypeStruct((radius, lat_cells), jnp.float32),
        ),
        scratch_shapes=[pltpu.VMEM((padded, lat_cells), jnp.float32)],
    )(at_cells, lists)


def backward_grad(perturb, p_low, p_high, spread, s_low, s_high, control, band_lon, band_lat):
    members, levels, lon_cells, lat_cells = control.shape
    radius = p_low.shape[2]
    padded, ext_cells = band_lon.shape
    chunk = member_chunk(members)

    def kernel(pert_ref, plow_ref, phigh_ref, spread_ref, slow_ref, shigh_ref, ctrl_ref,
               blon_ref, blat_ref, out_ref, ext_ref, along_ref):
        blon = blon_ref[...]
        spread = spread_ref[...]
        s_lo = slow_ref[...]
        s_hi = shigh_ref[...]
        for m in range(chunk):
            fill_ext(
                ext_ref,
                (pert_ref[m].astype(jnp.float32) * spread).astype(jnp.bfloat16),
                (plow_ref[m].astype(jnp.float32) * s_lo).astype(jnp.bfloat16),
                (phigh_ref[m].astype(jnp.float32) * s_hi).astype(jnp.bfloat16),
                lon_cells,
                padded,
            )
            along = jnp.dot(blon, ext_ref[...], preferred_element_type=jnp.float32)
            along_ref[m * padded:(m + 1) * padded, :] = along.astype(jnp.bfloat16)
        smoothed = jnp.dot(along_ref[...], blat_ref[...], preferred_element_type=jnp.float32)
        for m in range(chunk):
            out_ref[m] = ctrl_ref[m].astype(jnp.float32) + smoothed[
                m * padded:m * padded + lon_cells
            ]

    field = pl.BlockSpec((chunk, None, lon_cells, lat_cells), lambda l, g: (g, l, 0, 0))
    halo = pl.BlockSpec((chunk, None, radius, lat_cells), lambda l, g: (g, l, 0, 0))
    level_field = pl.BlockSpec((None, lon_cells, lat_cells), lambda l, g: (l, 0, 0))
    level_halo = pl.BlockSpec((None, radius, lat_cells), lambda l, g: (l, 0, 0))
    out = pl.pallas_call(
        kernel,
        grid=(levels, members // chunk),
        in_specs=[
            field,
            halo,
            halo,
            level_field,
            level_halo,
            level_halo,
            field,
            pl.BlockSpec(band_lon.shape, lambda l, g: (0, 0)),
            pl.BlockSpec(band_lat.shape, lambda l, g: (0, 0)),
        ],
        out_specs=pl.BlockSpec((chunk, lon_cells, None, lat_cells), lambda l, g: (g, 0, l, 0)),
        out_shape=jax.ShapeDtypeStruct((members, lon_cells, levels, lat_cells), jnp.float32),
        scratch_shapes=[
            pltpu.VMEM((ext_cells, lat_cells), jnp.bfloat16),
            pltpu.VMEM((chunk * padded, lat_cells), jnp.bfloat16),
        ],
        compiler_params=pltpu.CompilerParams(dimension_semantics=("arbitrary", "arbitrary")),
    )(perturb, p_low, p_high, spread, s_low, s_high, control, band_lon, band_lat)
    return jnp.transpose(out, (0, 2, 1, 3))


def local(control, perturb, lon_taps, lat_taps, innov, inv_var, cell_index, counts):
    members_here, levels, lon_cells, lat_cells = control.shape
    radius = lon_taps.shape[0] - 1
    padded = -(-lon_cells // 16) * 16
    band_lon, band_lat = build_bands(lon_taps, lat_taps, lon_cells, padded, lat_cells)

    slot_ids = lax.broadcasted_iota(jnp.int32, innov.shape, 2)
    weights = jnp.where(slot_ids < counts[:, :, None], inv_var, 0.0)
    lists = jnp.concatenate([innov, weights, cell_index.astype(jnp.float32)])
    lists = lax.optimization_barrier((lists, band_lon, band_lat))[0]
    received = lax.all_to_all(lists, "tile", split_axis=1, concat_axis=1, tiled=True)

    c_low, c_high = halos(control, "tile", 2, radius)
    c_low, c_high, received = lax.optimization_barrier((c_low, c_high, received))
    late_perturb = lax.optimization_barrier((perturb, c_low, c_high))[0]
    p_low, p_high = halos(late_perturb, "tile", 2, radius)
    partial = forward_pick(
        control, c_low, c_high, perturb, band_lon, band_lat, received
    )
    at_cells = sum_over(partial, "mem")
    spread, low_send, high_send = spread_misfits(
        at_cells, received, lon_cells, lat_cells, radius, padded
    )
    count = lax.axis_size("tile")
    s_low = lax.ppermute(low_send, "tile", [(i, (i + 1) % count) for i in range(count)])
    s_high = lax.ppermute(high_send, "tile", [((i + 1) % count, i) for i in range(count)])
    return backward_grad(
        perturb,
        p_low,
        p_high,
        spread[None],
        s_low[None],
        s_high[None],
        control,
        band_lon,
        band_lat,
    )


def solution(mesh):
    return jax.shard_map(
        local,
        mesh=mesh,
        in_specs=(
            P("mem", None, "tile", None),
            P("mem", None, "tile", None),
            P(),
            P(),
            P("tile", None, None),
            P("tile", None, None),
            P("tile", None, None),
            P("tile", None),
        ),
        out_specs=P("mem", None, "tile", None),
        check_vma=False,
    )
```

```python
import math

import jax
import jax.numpy as jnp
from jax import lax
from jax.experimental import pallas as pl
from jax.experimental.pallas import tpu as pltpu
from jax.sharding import PartitionSpec as P


def halos(block, axis, dim, width):
    count = lax.axis_size(axis)
    forward = [(i, (i + 1) % count) for i in range(count)]
    backward = [((i + 1) % count, i) for i in range(count)]
    low = lax.ppermute(
        lax.slice_in_dim(block, block.shape[dim] - width, None, axis=dim), axis, forward
    )
    high = lax.ppermute(lax.slice_in_dim(block, 0, width, axis=dim), axis, backward)
    return low, high


def gather_over(values, axis):
    count = lax.axis_size(axis)
    return [values] + [
        lax.ppermute(values, axis, [(i, (i + shift) % count) for i in range(count)])
        for shift in range(1, count)
    ]


def select_chain(dist, taps_ref):
    band = jnp.zeros(dist.shape, jnp.float32)
    for offset in range(taps_ref.shape[0]):
        band = jnp.where(dist == offset, taps_ref[offset], band)
    return band.astype(jnp.bfloat16)


def build_bands(lon_taps, lat_taps, lon_cells, padded, lat_cells):
    radius = lon_taps.shape[0] - 1
    ext_cells = padded + 2 * radius
    tile = 128
    tiles = -(-lat_cells // tile)

    def kernel(lon_ref, lat_ref, blon_ref, blat_ref):
        rows = lax.broadcasted_iota(jnp.int32, (padded, ext_cells), 0)
        cols = lax.broadcasted_iota(jnp.int32, (padded, ext_cells), 1)
        source = jnp.where(
            cols < padded,
            cols,
            jnp.where(
                cols < padded + radius,
                cols - padded - radius,
                cols - padded - radius + lon_cells,
            ),
        )
        valid = (rows < lon_cells) & ((cols < lon_cells) | (cols >= padded))
        dist = jnp.where(valid, jnp.abs(source - rows), radius + 1)
        blon_ref[...] = select_chain(dist, lon_ref)

        t_rows = lax.broadcasted_iota(jnp.int32, (tile, tile), 0)
        t_cols = lax.broadcasted_iota(jnp.int32, (tile, tile), 1)
        blocks = {
            shift: select_chain(jnp.abs(t_rows - t_cols + shift * tile), lat_ref)
            for shift in (-1, 0, 1)
        }
        blat_ref[...] = jnp.zeros(blat_ref.shape, blat_ref.dtype)
        for a in range(tiles):
            for b in (a - 1, a, a + 1):
                if b < 0 or b >= tiles:
                    continue
                height = min(tile, lat_cells - a * tile)
                width = min(tile, lat_cells - b * tile)
                blat_ref[a * tile:a * tile + height, b * tile:b * tile + width] = blocks[a - b][
                    :height, :width
                ]

    smem = pl.BlockSpec(memory_space=pltpu.SMEM)
    return pl.pallas_call(
        kernel,
        in_specs=[smem, smem],
        out_shape=(
            jax.ShapeDtypeStruct((padded, ext_cells), jnp.bfloat16),
            jax.ShapeDtypeStruct((lat_cells, lat_cells), jnp.bfloat16),
        ),
    )(lon_taps.astype(jnp.float32), lat_taps.astype(jnp.float32))


def member_chunk(members):
    for size in (5, 4, 3, 2, 1):
        if members % size == 0:
            return size
    return 1


def fill_ext(ext_ref, local, low, high, lon_cells, padded):
    radius = low.shape[0]
    base = (lon_cells // 16) * 16
    ext_ref[base:padded, :] = jnp.zeros((padded - base, ext_ref.shape[1]), ext_ref.dtype)
    ext_ref[0:lon_cells, :] = local
    ext_ref[padded:padded + radius, :] = low
    ext_ref[padded + radius:padded + 2 * radius, :] = high


def split3(values):
    hi = values.astype(jnp.bfloat16)
    rest = values - hi.astype(jnp.float32)
    mid = rest.astype(jnp.bfloat16)
    lo = (rest - mid.astype(jnp.float32)).astype(jnp.bfloat16)
    return hi, mid, lo


def cell_keys(cells, padded, lat_cells):
    rows = jnp.floor((cells + 0.5) / lat_cells)
    cols = (cells - rows * lat_cells).astype(jnp.int32)
    keys = (cols // 128) * padded + rows.astype(jnp.int32)
    lane_ids = lax.broadcasted_iota(jnp.int32, (128, cells.shape[1]), 0)
    onehot = jnp.where(lane_ids == cols % 128, 1.0, 0.0).astype(jnp.bfloat16)
    return keys, onehot


def forward_pick(control, c_low, c_high, perturb, band_lon, band_lat, cells):
    members, levels, lon_cells, lat_cells = control.shape
    radius = c_low.shape[2]
    padded, ext_cells = band_lon.shape
    chunk = member_chunk(members)
    steps = members // chunk
    _, sources, slots = cells.shape
    parts = -(-lat_cells // 128)

    def kernel(ctrl_ref, low_ref, high_ref, pert_ref, blon_ref, blat_ref, cells_ref, out_ref,
               ext_ref, along_ref, acc_ref, fold_ref):
        step = pl.program_id(0)
        blon = blon_ref[...]
        for m in range(chunk):
            fill_ext(ext_ref, ctrl_ref[m], low_ref[m], high_ref[m], lon_cells, padded)
            along = jnp.dot(blon, ext_ref[...], preferred_element_type=jnp.float32)
            along_ref[m * padded:(m + 1) * padded, :] = along.astype(jnp.bfloat16)
        smoothed = jnp.dot(along_ref[...], blat_ref[...], preferred_element_type=jnp.float32)
        total = pert_ref[0].astype(jnp.float32) * smoothed[0:lon_cells]
        for m in range(1, chunk):
            total = total + pert_ref[m].astype(jnp.float32) * smoothed[
                m * padded:m * padded + lon_cells
            ]

        @pl.when(step == 0)
        def _():
            acc_ref[...] = jnp.zeros(acc_ref.shape, acc_ref.dtype)

        acc_ref[0:lon_cells, :] = acc_ref[0:lon_cells, :] + total

        @pl.when(step == steps - 1)
        def _():
            fold_ref[...] = jnp.zeros(fold_ref.shape, fold_ref.dtype)
            for part in range(parts):
                width = min(128, lat_cells - part * 128)
                fold_ref[part * padded:(part + 1) * padded, 0:width] = acc_ref[
                    :, part * 128:part * 128 + width
                ]
            pieces = split3(fold_ref[...])
            key_ids = lax.broadcasted_iota(jnp.int32, (parts * padded, slots), 0)
            for row in range(sources):
                keys, onehot = cell_keys(cells_ref[2, row:row + 1, :], padded, lat_cells)
                at_keys = jnp.dot(pieces[0], onehot, preferred_element_type=jnp.float32)
                at_keys = at_keys + jnp.dot(pieces[1], onehot, preferred_element_type=jnp.float32)
                at_keys = at_keys + jnp.dot(pieces[2], onehot, preferred_element_type=jnp.float32)
                out_ref[row:row + 1, :] = jnp.sum(
                    jnp.where(key_ids == keys, at_keys, 0.0), axis=0, keepdims=True
                )

    field = pl.BlockSpec((chunk, None, lon_cells, lat_cells), lambda g: (g, 0, 0, 0))
    halo = pl.BlockSpec((chunk, None, radius, lat_cells), lambda g: (g, 0, 0, 0))
    whole = lambda shape: pl.BlockSpec(shape, lambda g: (0,) * len(shape))
    return pl.pallas_call(
        kernel,
        grid=(steps,),
        in_specs=[
            field,
            halo,
            halo,
            field,
            whole(band_lon.shape),
            whole(band_lat.shape),
            whole(cells.shape),
        ],
        out_specs=whole((sources, slots)),
        out_shape=jax.ShapeDtypeStruct((sources, slots), jnp.float32),
        scratch_shapes=[
            pltpu.VMEM((ext_cells, lat_cells), jnp.bfloat16),
            pltpu.VMEM((chunk * padded, lat_cells), jnp.bfloat16),
            pltpu.VMEM((padded, lat_cells), jnp.float32),
            pltpu.VMEM((parts * padded, 128), jnp.float32),
        ],
        compiler_params=pltpu.CompilerParams(dimension_semantics=("arbitrary",)),
    )(control, c_low, c_high, perturb, band_lon, band_lat, cells)


def spread_misfits(partials, lists, lon_cells, lat_cells, radius, padded):
    _, sources, slots = lists.shape
    parts = -(-lat_cells // 128)

    def kernel(*refs):
        part_refs = refs[:len(partials)]
        lists_ref, spread_ref, low_ref, high_ref, fold_ref = refs[len(partials):]
        at_cells = part_refs[0][...]
        for ref in part_refs[1:]:
            at_cells = at_cells + ref[...]
        key_ids = lax.broadcasted_iota(jnp.int32, (parts * padded, slots), 0)
        folded = jnp.zeros((parts * padded, 128), jnp.float32)
        for row in range(sources):
            misfit = lists_ref[1, row:row + 1, :] * (
                at_cells[row:row + 1, :] - lists_ref[0, row:row + 1, :]
            )
            keys, onehot = cell_keys(lists_ref[2, row:row + 1, :], padded, lat_cells)
            for piece in split3(misfit):
                weighted = jnp.where(key_ids == keys, piece.astype(jnp.float32), 0.0)
                folded = folded + lax.dot_general(
                    weighted.astype(jnp.bfloat16),
                    onehot,
                    (((1,), (1,)), ((), ())),
                    preferred_element_type=jnp.float32,
                )
        for part in range(parts):
            width = min(128, lat_cells - part * 128)
            fold_ref[:, part * 128:part * 128 + width] = folded[
                part * padded:(part + 1) * padded, 0:width
            ]
        spread_ref[...] = fold_ref[0:lon_cells, :]
        low_ref[...] = fold_ref[lon_cells - radius:lon_cells, :]
        high_ref[...] = fold_ref[0:radius, :]

    return pl.pallas_call(
        kernel,
        out_shape=(
            jax.ShapeDtypeStruct((lon_cells, lat_cells), jnp.float32),
            jax.ShapeDtypeStruct((radius, lat_cells), jnp.float32),
            jax.ShapeDtypeStruct((radius, lat_cells), jnp.float32),
        ),
        scratch_shapes=[pltpu.VMEM((padded, lat_cells), jnp.float32)],
    )(*partials, lists)


def backward_grad(perturb, p_low, p_high, spread, s_low, s_high, control, band_lon, band_lat):
    members, levels, lon_cells, lat_cells = control.shape
    radius = p_low.shape[2]
    padded, ext_cells = band_lon.shape
    chunk = member_chunk(members)

    def kernel(pert_ref, plow_ref, phigh_ref, spread_ref, slow_ref, shigh_ref, ctrl_ref,
               blon_ref, blat_ref, out_ref, ext_ref, along_ref):
        blon = blon_ref[...]
        spread = spread_ref[...]
        s_lo = slow_ref[...]
        s_hi = shigh_ref[...]
        for m in range(chunk):
            fill_ext(
                ext_ref,
                (pert_ref[m].astype(jnp.float32) * spread).astype(jnp.bfloat16),
                (plow_ref[m].astype(jnp.float32) * s_lo).astype(jnp.bfloat16),
                (phigh_ref[m].astype(jnp.float32) * s_hi).astype(jnp.bfloat16),
                lon_cells,
                padded,
            )
            along = jnp.dot(blon, ext_ref[...], preferred_element_type=jnp.float32)
            along_ref[m * padded:(m + 1) * padded, :] = along.astype(jnp.bfloat16)
        smoothed = jnp.dot(along_ref[...], blat_ref[...], preferred_element_type=jnp.float32)
        for m in range(chunk):
            out_ref[m] = ctrl_ref[m].astype(jnp.float32) + smoothed[
                m * padded:m * padded + lon_cells
            ]

    field = pl.BlockSpec((chunk, None, lon_cells, lat_cells), lambda l, g: (g, l, 0, 0))
    halo = pl.BlockSpec((chunk, None, radius, lat_cells), lambda l, g: (g, l, 0, 0))
    level_field = pl.BlockSpec((None, lon_cells, lat_cells), lambda l, g: (l, 0, 0))
    level_halo = pl.BlockSpec((None, radius, lat_cells), lambda l, g: (l, 0, 0))
    out = pl.pallas_call(
        kernel,
        grid=(levels, members // chunk),
        in_specs=[
            field,
            halo,
            halo,
            level_field,
            level_halo,
            level_halo,
            field,
            pl.BlockSpec(band_lon.shape, lambda l, g: (0, 0)),
            pl.BlockSpec(band_lat.shape, lambda l, g: (0, 0)),
        ],
        out_specs=pl.BlockSpec((chunk, lon_cells, None, lat_cells), lambda l, g: (g, 0, l, 0)),
        out_shape=jax.ShapeDtypeStruct((members, lon_cells, levels, lat_cells), jnp.float32),
        scratch_shapes=[
            pltpu.VMEM((ext_cells, lat_cells), jnp.bfloat16),
            pltpu.VMEM((chunk * padded, lat_cells), jnp.bfloat16),
        ],
        compiler_params=pltpu.CompilerParams(dimension_semantics=("arbitrary", "arbitrary")),
    )(perturb, p_low, p_high, spread, s_low, s_high, control, band_lon, band_lat)
    return jnp.transpose(out, (0, 2, 1, 3))


def local(control, perturb, lon_taps, lat_taps, innov, inv_var, cell_index, counts):
    members_here, levels, lon_cells, lat_cells = control.shape
    radius = lon_taps.shape[0] - 1
    padded = -(-lon_cells // 16) * 16
    band_lon, band_lat = build_bands(lon_taps, lat_taps, lon_cells, padded, lat_cells)

    slot_ids = lax.broadcasted_iota(jnp.int32, innov.shape, 2)
    weights = jnp.where(slot_ids < counts[:, :, None], inv_var, 0.0)
    lists = jnp.concatenate([innov, weights, cell_index.astype(jnp.float32)])
    lists = lax.optimization_barrier((lists, band_lon, band_lat))[0]
    received = lax.all_to_all(lists, "tile", split_axis=1, concat_axis=1, tiled=True)

    c_low, c_high = halos(control, "tile", 2, radius)
    c_low, c_high, received = lax.optimization_barrier((c_low, c_high, received))
    late_perturb = lax.optimization_barrier((perturb, c_low, c_high))[0]
    p_low, p_high = halos(late_perturb, "tile", 2, radius)
    partial = forward_pick(
        control, c_low, c_high, perturb, band_lon, band_lat, received
    )
    partials = gather_over(partial, "mem")
    spread, low_send, high_send = spread_misfits(
        partials, received, lon_cells, lat_cells, radius, padded
    )
    count = lax.axis_size("tile")
    s_low = lax.ppermute(low_send, "tile", [(i, (i + 1) % count) for i in range(count)])
    s_high = lax.ppermute(high_send, "tile", [((i + 1) % count, i) for i in range(count)])
    return backward_grad(
        perturb,
        p_low,
        p_high,
        spread[None],
        s_low[None],
        s_high[None],
        control,
        band_lon,
        band_lat,
    )


def solution(mesh):
    return jax.shard_map(
        local,
        mesh=mesh,
        in_specs=(
            P("mem", None, "tile", None),
            P("mem", None, "tile", None),
            P(),
            P(),
            P("tile", None, None),
            P("tile", None, None),
            P("tile", None, None),
            P("tile", None),
        ),
        out_specs=P("mem", None, "tile", None),
        check_vma=False,
    )
```

```python
import math

import jax
import jax.numpy as jnp
from jax import lax
from jax.experimental import pallas as pl
from jax.experimental.pallas import tpu as pltpu
from jax.sharding import PartitionSpec as P


def halos(block, axis, dim, width):
    count = lax.axis_size(axis)
    forward = [(i, (i + 1) % count) for i in range(count)]
    backward = [((i + 1) % count, i) for i in range(count)]
    low = lax.ppermute(
        lax.slice_in_dim(block, block.shape[dim] - width, None, axis=dim), axis, forward
    )
    high = lax.ppermute(lax.slice_in_dim(block, 0, width, axis=dim), axis, backward)
    return low, high


def exchange(lists, axis):
    count = lax.axis_size(axis)
    rolled = jnp.roll(lists, -lax.axis_index(axis), axis=1)
    rows = [rolled[:, 0:1]]
    for shift in range(1, count):
        rows.append(
            lax.ppermute(
                rolled[:, shift:shift + 1], axis, [(i, (i + shift) % count) for i in range(count)]
            )
        )
    return jnp.concatenate(rows, axis=1)


def gather_over(values, axis):
    count = lax.axis_size(axis)
    return [values] + [
        lax.ppermute(values, axis, [(i, (i + shift) % count) for i in range(count)])
        for shift in range(1, count)
    ]


def select_chain(dist, taps_ref):
    band = jnp.zeros(dist.shape, jnp.float32)
    for offset in range(taps_ref.shape[0]):
        band = jnp.where(dist == offset, taps_ref[offset], band)
    return band.astype(jnp.bfloat16)


def build_bands(lon_taps, lat_taps, lon_cells, padded, lat_cells):
    radius = lon_taps.shape[0] - 1
    ext_cells = padded + 2 * radius
    tile = 128
    tiles = -(-lat_cells // tile)

    def kernel(lon_ref, lat_ref, blon_ref, blat_ref):
        rows = lax.broadcasted_iota(jnp.int32, (padded, ext_cells), 0)
        cols = lax.broadcasted_iota(jnp.int32, (padded, ext_cells), 1)
        source = jnp.where(
            cols < padded,
            cols,
            jnp.where(
                cols < padded + radius,
                cols - padded - radius,
                cols - padded - radius + lon_cells,
            ),
        )
        valid = (rows < lon_cells) & ((cols < lon_cells) | (cols >= padded))
        dist = jnp.where(valid, jnp.abs(source - rows), radius + 1)
        blon_ref[...] = select_chain(dist, lon_ref)

        t_rows = lax.broadcasted_iota(jnp.int32, (tile, tile), 0)
        t_cols = lax.broadcasted_iota(jnp.int32, (tile, tile), 1)
        blocks = {
            shift: select_chain(jnp.abs(t_rows - t_cols + shift * tile), lat_ref)
            for shift in (-1, 0, 1)
        }
        blat_ref[...] = jnp.zeros(blat_ref.shape, blat_ref.dtype)
        for a in range(tiles):
            for b in (a - 1, a, a + 1):
                if b < 0 or b >= tiles:
                    continue
                height = min(tile, lat_cells - a * tile)
                width = min(tile, lat_cells - b * tile)
                blat_ref[a * tile:a * tile + height, b * tile:b * tile + width] = blocks[a - b][
                    :height, :width
                ]

    smem = pl.BlockSpec(memory_space=pltpu.SMEM)
    return pl.pallas_call(
        kernel,
        in_specs=[smem, smem],
        out_shape=(
            jax.ShapeDtypeStruct((padded, ext_cells), jnp.bfloat16),
            jax.ShapeDtypeStruct((lat_cells, lat_cells), jnp.bfloat16),
        ),
    )(lon_taps.astype(jnp.float32), lat_taps.astype(jnp.float32))


def member_chunk(members):
    for size in (5, 4, 3, 2, 1):
        if members % size == 0:
            return size
    return 1


def fill_ext(ext_ref, local, low, high, lon_cells, padded):
    radius = low.shape[0]
    base = (lon_cells // 16) * 16
    ext_ref[base:padded, :] = jnp.zeros((padded - base, ext_ref.shape[1]), ext_ref.dtype)
    ext_ref[0:lon_cells, :] = local
    ext_ref[padded:padded + radius, :] = low
    ext_ref[padded + radius:padded + 2 * radius, :] = high


def split3(values):
    hi = values.astype(jnp.bfloat16)
    rest = values - hi.astype(jnp.float32)
    mid = rest.astype(jnp.bfloat16)
    lo = (rest - mid.astype(jnp.float32)).astype(jnp.bfloat16)
    return hi, mid, lo


def cell_keys(cells, padded, lat_cells):
    rows = jnp.floor((cells + 0.5) / lat_cells)
    cols = (cells - rows * lat_cells).astype(jnp.int32)
    keys = (cols // 128) * padded + rows.astype(jnp.int32)
    lane_ids = lax.broadcasted_iota(jnp.int32, (128, cells.shape[1]), 0)
    onehot = jnp.where(lane_ids == cols % 128, 1.0, 0.0).astype(jnp.bfloat16)
    return keys, onehot


def forward_pick(control, c_low, c_high, perturb, band_lon, band_lat, prior, cells, first):
    _, levels, lon_cells, lat_cells = control.shape
    members = c_low.shape[0]
    radius = c_low.shape[2]
    padded, ext_cells = band_lon.shape
    chunk = member_chunk(math.gcd(members, first) if first else members)
    steps = members // chunk
    base = first // chunk
    parts = -(-lat_cells // 128)
    if cells is not None:
        _, sources, slots = cells.shape

    def kernel(*refs):
        ctrl_ref, low_ref, high_ref, pert_ref, blon_ref, blat_ref = refs[:6]
        rest = list(refs[6:])
        prior_ref = rest.pop(0) if prior is not None else None
        cells_ref = rest.pop(0) if cells is not None else None
        out_ref, ext_ref, along_ref, acc_ref, fold_ref = rest
        step = pl.program_id(0)
        blon = blon_ref[...]
        for m in range(chunk):
            fill_ext(ext_ref, ctrl_ref[m], low_ref[m], high_ref[m], lon_cells, padded)
            along = jnp.dot(blon, ext_ref[...], preferred_element_type=jnp.float32)
            along_ref[m * padded:(m + 1) * padded, :] = along.astype(jnp.bfloat16)
        smoothed = jnp.dot(along_ref[...], blat_ref[...], preferred_element_type=jnp.float32)
        total = pert_ref[0].astype(jnp.float32) * smoothed[0:lon_cells]
        for m in range(1, chunk):
            total = total + pert_ref[m].astype(jnp.float32) * smoothed[
                m * padded:m * padded + lon_cells
            ]

        @pl.when(step == 0)
        def _():
            if prior_ref is None:
                acc_ref[...] = jnp.zeros(acc_ref.shape, acc_ref.dtype)
            else:
                acc_ref[...] = prior_ref[...]

        acc_ref[0:lon_cells, :] = acc_ref[0:lon_cells, :] + total

        if cells_ref is None:
            @pl.when(step == steps - 1)
            def _():
                out_ref[...] = acc_ref[...]

            return

        @pl.when(step == steps - 1)
        def _():
            fold_ref[...] = jnp.zeros(fold_ref.shape, fold_ref.dtype)
            for part in range(parts):
                width = min(128, lat_cells - part * 128)
                fold_ref[part * padded:(part + 1) * padded, 0:width] = acc_ref[
                    :, part * 128:part * 128 + width
                ]
            pieces = split3(fold_ref[...])
            key_ids = lax.broadcasted_iota(jnp.int32, (parts * padded, slots), 0)
            for row in range(sources):
                keys, onehot = cell_keys(cells_ref[2, row:row + 1, :], padded, lat_cells)
                at_keys = jnp.dot(pieces[0], onehot, preferred_element_type=jnp.float32)
                at_keys = at_keys + jnp.dot(pieces[1], onehot, preferred_element_type=jnp.float32)
                at_keys = at_keys + jnp.dot(pieces[2], onehot, preferred_element_type=jnp.float32)
                out_ref[row:row + 1, :] = jnp.sum(
                    jnp.where(key_ids == keys, at_keys, 0.0), axis=0, keepdims=True
                )

    field = pl.BlockSpec((chunk, None, lon_cells, lat_cells), lambda g: (g + base, 0, 0, 0))
    halo = pl.BlockSpec((chunk, None, radius, lat_cells), lambda g: (g, 0, 0, 0))
    whole = lambda shape: pl.BlockSpec(shape, lambda g: (0,) * len(shape))
    extra = [a for a in (prior, cells) if a is not None]
    out_shape = (sources, slots) if cells is not None else (padded, lat_cells)
    return pl.pallas_call(
        kernel,
        grid=(steps,),
        in_specs=[
            field,
            halo,
            halo,
            field,
            whole(band_lon.shape),
            whole(band_lat.shape),
        ] + [whole(a.shape) for a in extra],
        out_specs=whole(out_shape),
        out_shape=jax.ShapeDtypeStruct(out_shape, jnp.float32),
        scratch_shapes=[
            pltpu.VMEM((ext_cells, lat_cells), jnp.bfloat16),
            pltpu.VMEM((chunk * padded, lat_cells), jnp.bfloat16),
            pltpu.VMEM((padded, lat_cells), jnp.float32),
            pltpu.VMEM((parts * padded, 128), jnp.float32),
        ],
        compiler_params=pltpu.CompilerParams(dimension_semantics=("arbitrary",)),
    )(control, c_low, c_high, perturb, band_lon, band_lat, *extra)


def spread_misfits(partials, lists, lon_cells, lat_cells, radius, padded):
    _, sources, slots = lists.shape
    parts = -(-lat_cells // 128)

    def kernel(*refs):
        part_refs = refs[:len(partials)]
        lists_ref, spread_ref, low_ref, high_ref, fold_ref = refs[len(partials):]
        at_cells = part_refs[0][...]
        for ref in part_refs[1:]:
            at_cells = at_cells + ref[...]
        key_ids = lax.broadcasted_iota(jnp.int32, (parts * padded, slots), 0)
        folded = jnp.zeros((parts * padded, 128), jnp.float32)
        for row in range(sources):
            misfit = lists_ref[1, row:row + 1, :] * (
                at_cells[row:row + 1, :] - lists_ref[0, row:row + 1, :]
            )
            keys, onehot = cell_keys(lists_ref[2, row:row + 1, :], padded, lat_cells)
            for piece in split3(misfit):
                weighted = jnp.where(key_ids == keys, piece.astype(jnp.float32), 0.0)
                folded = folded + lax.dot_general(
                    weighted.astype(jnp.bfloat16),
                    onehot,
                    (((1,), (1,)), ((), ())),
                    preferred_element_type=jnp.float32,
                )
        for part in range(parts):
            width = min(128, lat_cells - part * 128)
            fold_ref[:, part * 128:part * 128 + width] = folded[
                part * padded:(part + 1) * padded, 0:width
            ]
        spread_ref[...] = fold_ref[0:lon_cells, :]
        low_ref[...] = fold_ref[lon_cells - radius:lon_cells, :]
        high_ref[...] = fold_ref[0:radius, :]

    return pl.pallas_call(
        kernel,
        out_shape=(
            jax.ShapeDtypeStruct((lon_cells, lat_cells), jnp.float32),
            jax.ShapeDtypeStruct((radius, lat_cells), jnp.float32),
            jax.ShapeDtypeStruct((radius, lat_cells), jnp.float32),
        ),
        scratch_shapes=[pltpu.VMEM((padded, lat_cells), jnp.float32)],
    )(*partials, lists)


def backward_grad(perturb, p_low, p_high, spread, s_low, s_high, control, band_lon, band_lat):
    members, levels, lon_cells, lat_cells = control.shape
    radius = p_low.shape[2]
    padded, ext_cells = band_lon.shape
    chunk = member_chunk(members)

    def kernel(pert_ref, plow_ref, phigh_ref, spread_ref, slow_ref, shigh_ref, ctrl_ref,
               blon_ref, blat_ref, out_ref, ext_ref, along_ref):
        blon = blon_ref[...]
        spread = spread_ref[...]
        s_lo = slow_ref[...]
        s_hi = shigh_ref[...]
        for m in range(chunk):
            fill_ext(
                ext_ref,
                (pert_ref[m].astype(jnp.float32) * spread).astype(jnp.bfloat16),
                (plow_ref[m].astype(jnp.float32) * s_lo).astype(jnp.bfloat16),
                (phigh_ref[m].astype(jnp.float32) * s_hi).astype(jnp.bfloat16),
                lon_cells,
                padded,
            )
            along = jnp.dot(blon, ext_ref[...], preferred_element_type=jnp.float32)
            along_ref[m * padded:(m + 1) * padded, :] = along.astype(jnp.bfloat16)
        smoothed = jnp.dot(along_ref[...], blat_ref[...], preferred_element_type=jnp.float32)
        for m in range(chunk):
            out_ref[m] = ctrl_ref[m].astype(jnp.float32) + smoothed[
                m * padded:m * padded + lon_cells
            ]

    field = pl.BlockSpec((chunk, None, lon_cells, lat_cells), lambda l, g: (g, l, 0, 0))
    halo = pl.BlockSpec((chunk, None, radius, lat_cells), lambda l, g: (g, l, 0, 0))
    level_field = pl.BlockSpec((None, lon_cells, lat_cells), lambda l, g: (l, 0, 0))
    level_halo = pl.BlockSpec((None, radius, lat_cells), lambda l, g: (l, 0, 0))
    out = pl.pallas_call(
        kernel,
        grid=(levels, members // chunk),
        in_specs=[
            field,
            halo,
            halo,
            level_field,
            level_halo,
            level_halo,
            field,
            pl.BlockSpec(band_lon.shape, lambda l, g: (0, 0)),
            pl.BlockSpec(band_lat.shape, lambda l, g: (0, 0)),
        ],
        out_specs=pl.BlockSpec((chunk, lon_cells, None, lat_cells), lambda l, g: (g, 0, l, 0)),
        out_shape=jax.ShapeDtypeStruct((members, lon_cells, levels, lat_cells), jnp.float32),
        scratch_shapes=[
            pltpu.VMEM((ext_cells, lat_cells), jnp.bfloat16),
            pltpu.VMEM((chunk * padded, lat_cells), jnp.bfloat16),
        ],
        compiler_params=pltpu.CompilerParams(dimension_semantics=("arbitrary", "arbitrary")),
    )(perturb, p_low, p_high, spread, s_low, s_high, control, band_lon, band_lat)
    return jnp.transpose(out, (0, 2, 1, 3))


def local(control, perturb, lon_taps, lat_taps, innov, inv_var, cell_index, counts):
    members_here, levels, lon_cells, lat_cells = control.shape
    radius = lon_taps.shape[0] - 1
    padded = -(-lon_cells // 16) * 16
    band_lon, band_lat = build_bands(lon_taps, lat_taps, lon_cells, padded, lat_cells)

    slot_ids = lax.broadcasted_iota(jnp.int32, innov.shape, 2)
    weights = jnp.where(slot_ids < counts[:, :, None], inv_var, 0.0)
    lists = jnp.concatenate([innov, weights, cell_index.astype(jnp.float32)])
    received = exchange(lists, "tile")

    half = members_here // 2
    a_low, a_high = halos(control[:half], "tile", 2, radius)
    a_low, a_high, band_lon, band_lat = lax.optimization_barrier(
        (a_low, a_high, band_lon, band_lat)
    )
    late_control = lax.optimization_barrier((control, a_low, a_high))[0]
    b_low, b_high = halos(late_control[half:], "tile", 2, radius)
    field = forward_pick(
        control, a_low, a_high, perturb, band_lon, band_lat, None, None, 0
    )
    b_low, b_high, field, received = lax.optimization_barrier((b_low, b_high, field, received))
    partial = forward_pick(
        control, b_low, b_high, perturb, band_lon, band_lat, field, received, half
    )
    late_perturb = lax.optimization_barrier((perturb, partial))[0]
    p_low, p_high = halos(late_perturb, "tile", 2, radius)
    partials = gather_over(partial, "mem")
    spread, low_send, high_send = spread_misfits(
        partials, received, lon_cells, lat_cells, radius, padded
    )
    count = lax.axis_size("tile")
    s_low = lax.ppermute(low_send, "tile", [(i, (i + 1) % count) for i in range(count)])
    s_high = lax.ppermute(high_send, "tile", [((i + 1) % count, i) for i in range(count)])
    return backward_grad(
        perturb,
        p_low,
        p_high,
        spread[None],
        s_low[None],
        s_high[None],
        control,
        band_lon,
        band_lat,
    )


def solution(mesh):
    return jax.shard_map(
        local,
        mesh=mesh,
        in_specs=(
            P("mem", None, "tile", None),
            P("mem", None, "tile", None),
            P(),
            P(),
            P("tile", None, None),
            P("tile", None, None),
            P("tile", None, None),
            P("tile", None),
        ),
        out_specs=P("mem", None, "tile", None),
        check_vma=False,
    )
```

```python
import math

import jax
import jax.numpy as jnp
from jax import lax
from jax.experimental import pallas as pl
from jax.experimental.pallas import tpu as pltpu
from jax.sharding import PartitionSpec as P


def halos(block, axis, dim, width):
    count = lax.axis_size(axis)
    forward = [(i, (i + 1) % count) for i in range(count)]
    backward = [((i + 1) % count, i) for i in range(count)]
    low = lax.ppermute(
        lax.slice_in_dim(block, block.shape[dim] - width, None, axis=dim), axis, forward
    )
    high = lax.ppermute(lax.slice_in_dim(block, 0, width, axis=dim), axis, backward)
    return low, high


def gather_over(values, axis):
    count = lax.axis_size(axis)
    if count & (count - 1):
        return [values] + [
            lax.ppermute(values, axis, [(i, (i + shift) % count) for i in range(count)])
            for shift in range(1, count)
        ]
    total = values
    bit = 1
    while bit < count:
        total = total + lax.ppermute(total, axis, [(i, i ^ bit) for i in range(count)])
        bit *= 2
    return [total]


def select_chain(dist, taps_ref):
    band = jnp.zeros(dist.shape, jnp.float32)
    for offset in range(taps_ref.shape[0]):
        band = jnp.where(dist == offset, taps_ref[offset], band)
    return band.astype(jnp.bfloat16)


def build_bands(lon_taps, lat_taps, lon_cells, padded, lat_cells):
    radius = lon_taps.shape[0] - 1
    ext_cells = padded + 2 * radius
    tile = 128
    tiles = -(-lat_cells // tile)

    def kernel(lon_ref, lat_ref, blon_ref, blat_ref):
        rows = lax.broadcasted_iota(jnp.int32, (padded, ext_cells), 0)
        cols = lax.broadcasted_iota(jnp.int32, (padded, ext_cells), 1)
        source = jnp.where(
            cols < padded,
            cols,
            jnp.where(
                cols < padded + radius,
                cols - padded - radius,
                cols - padded - radius + lon_cells,
            ),
        )
        valid = (rows < lon_cells) & ((cols < lon_cells) | (cols >= padded))
        dist = jnp.where(valid, jnp.abs(source - rows), radius + 1)
        blon_ref[...] = select_chain(dist, lon_ref)

        t_rows = lax.broadcasted_iota(jnp.int32, (tile, tile), 0)
        t_cols = lax.broadcasted_iota(jnp.int32, (tile, tile), 1)
        blocks = {
            shift: select_chain(jnp.abs(t_rows - t_cols + shift * tile), lat_ref)
            for shift in (-1, 0, 1)
        }
        blat_ref[...] = jnp.zeros(blat_ref.shape, blat_ref.dtype)
        for a in range(tiles):
            for b in (a - 1, a, a + 1):
                if b < 0 or b >= tiles:
                    continue
                height = min(tile, lat_cells - a * tile)
                width = min(tile, lat_cells - b * tile)
                blat_ref[a * tile:a * tile + height, b * tile:b * tile + width] = blocks[a - b][
                    :height, :width
                ]

    smem = pl.BlockSpec(memory_space=pltpu.SMEM)
    return pl.pallas_call(
        kernel,
        in_specs=[smem, smem],
        out_shape=(
            jax.ShapeDtypeStruct((padded, ext_cells), jnp.bfloat16),
            jax.ShapeDtypeStruct((lat_cells, lat_cells), jnp.bfloat16),
        ),
    )(lon_taps.astype(jnp.float32), lat_taps.astype(jnp.float32))


def member_chunk(members):
    for size in (5, 4, 3, 2, 1):
        if members % size == 0:
            return size
    return 1


def fill_ext(ext_ref, local, low, high, lon_cells, padded):
    radius = low.shape[0]
    base = (lon_cells // 16) * 16
    ext_ref[base:padded, :] = jnp.zeros((padded - base, ext_ref.shape[1]), ext_ref.dtype)
    ext_ref[0:lon_cells, :] = local
    ext_ref[padded:padded + radius, :] = low
    ext_ref[padded + radius:padded + 2 * radius, :] = high


def split3(values):
    hi = values.astype(jnp.bfloat16)
    rest = values - hi.astype(jnp.float32)
    mid = rest.astype(jnp.bfloat16)
    lo = (rest - mid.astype(jnp.float32)).astype(jnp.bfloat16)
    return hi, mid, lo


def cell_keys(cells, padded, lat_cells):
    rows = jnp.floor((cells + 0.5) / lat_cells)
    cols = (cells - rows * lat_cells).astype(jnp.int32)
    keys = (cols // 128) * padded + rows.astype(jnp.int32)
    lane_ids = lax.broadcasted_iota(jnp.int32, (128, cells.shape[1]), 0)
    onehot = jnp.where(lane_ids == cols % 128, 1.0, 0.0).astype(jnp.bfloat16)
    return keys, onehot


def forward_pick(control, c_low, c_high, perturb, band_lon, band_lat, cells):
    members, levels, lon_cells, lat_cells = control.shape
    radius = c_low.shape[2]
    padded, ext_cells = band_lon.shape
    chunk = member_chunk(members)
    steps = members // chunk
    _, sources, slots = cells.shape
    parts = -(-lat_cells // 128)

    def kernel(ctrl_ref, low_ref, high_ref, pert_ref, blon_ref, blat_ref, cells_ref, out_ref,
               ext_ref, along_ref, acc_ref, fold_ref):
        step = pl.program_id(0)
        blon = blon_ref[...]
        for m in range(chunk):
            fill_ext(ext_ref, ctrl_ref[m], low_ref[m], high_ref[m], lon_cells, padded)
            along = jnp.dot(blon, ext_ref[...], preferred_element_type=jnp.float32)
            along_ref[m * padded:(m + 1) * padded, :] = along.astype(jnp.bfloat16)
        smoothed = jnp.dot(along_ref[...], blat_ref[...], preferred_element_type=jnp.float32)
        total = pert_ref[0].astype(jnp.float32) * smoothed[0:lon_cells]
        for m in range(1, chunk):
            total = total + pert_ref[m].astype(jnp.float32) * smoothed[
                m * padded:m * padded + lon_cells
            ]

        @pl.when(step == 0)
        def _():
            acc_ref[...] = jnp.zeros(acc_ref.shape, acc_ref.dtype)

        acc_ref[0:lon_cells, :] = acc_ref[0:lon_cells, :] + total

        @pl.when(step == steps - 1)
        def _():
            fold_ref[...] = jnp.zeros(fold_ref.shape, fold_ref.dtype)
            for part in range(parts):
                width = min(128, lat_cells - part * 128)
                fold_ref[part * padded:(part + 1) * padded, 0:width] = acc_ref[
                    :, part * 128:part * 128 + width
                ]
            pieces = split3(fold_ref[...])
            key_ids = lax.broadcasted_iota(jnp.int32, (parts * padded, slots), 0)
            for row in range(sources):
                keys, onehot = cell_keys(cells_ref[2, row:row + 1, :], padded, lat_cells)
                at_keys = jnp.dot(pieces[0], onehot, preferred_element_type=jnp.float32)
                at_keys = at_keys + jnp.dot(pieces[1], onehot, preferred_element_type=jnp.float32)
                at_keys = at_keys + jnp.dot(pieces[2], onehot, preferred_element_type=jnp.float32)
                out_ref[row:row + 1, :] = jnp.sum(
                    jnp.where(key_ids == keys, at_keys, 0.0), axis=0, keepdims=True
                )

    field = pl.BlockSpec((chunk, None, lon_cells, lat_cells), lambda g: (g, 0, 0, 0))
    halo = pl.BlockSpec((chunk, None, radius, lat_cells), lambda g: (g, 0, 0, 0))
    whole = lambda shape: pl.BlockSpec(shape, lambda g: (0,) * len(shape))
    return pl.pallas_call(
        kernel,
        grid=(steps,),
        in_specs=[
            field,
            halo,
            halo,
            field,
            whole(band_lon.shape),
            whole(band_lat.shape),
            whole(cells.shape),
        ],
        out_specs=whole((sources, slots)),
        out_shape=jax.ShapeDtypeStruct((sources, slots), jnp.float32),
        scratch_shapes=[
            pltpu.VMEM((ext_cells, lat_cells), jnp.bfloat16),
            pltpu.VMEM((chunk * padded, lat_cells), jnp.bfloat16),
            pltpu.VMEM((padded, lat_cells), jnp.float32),
            pltpu.VMEM((parts * padded, 128), jnp.float32),
        ],
        compiler_params=pltpu.CompilerParams(dimension_semantics=("arbitrary",)),
    )(control, c_low, c_high, perturb, band_lon, band_lat, cells)


def spread_misfits(partials, lists, lon_cells, lat_cells, radius, padded):
    _, sources, slots = lists.shape
    parts = -(-lat_cells // 128)

    def kernel(*refs):
        part_refs = refs[:len(partials)]
        lists_ref, spread_ref, low_ref, high_ref, fold_ref = refs[len(partials):]
        at_cells = part_refs[0][...]
        for ref in part_refs[1:]:
            at_cells = at_cells + ref[...]
        key_ids = lax.broadcasted_iota(jnp.int32, (parts * padded, slots), 0)
        folded = jnp.zeros((parts * padded, 128), jnp.float32)
        for row in range(sources):
            misfit = lists_ref[1, row:row + 1, :] * (
                at_cells[row:row + 1, :] - lists_ref[0, row:row + 1, :]
            )
            keys, onehot = cell_keys(lists_ref[2, row:row + 1, :], padded, lat_cells)
            for piece in split3(misfit):
                weighted = jnp.where(key_ids == keys, piece.astype(jnp.float32), 0.0)
                folded = folded + lax.dot_general(
                    weighted.astype(jnp.bfloat16),
                    onehot,
                    (((1,), (1,)), ((), ())),
                    preferred_element_type=jnp.float32,
                )
        for part in range(parts):
            width = min(128, lat_cells - part * 128)
            fold_ref[:, part * 128:part * 128 + width] = folded[
                part * padded:(part + 1) * padded, 0:width
            ]
        spread_ref[...] = fold_ref[0:lon_cells, :]
        low_ref[...] = fold_ref[lon_cells - radius:lon_cells, :]
        high_ref[...] = fold_ref[0:radius, :]

    return pl.pallas_call(
        kernel,
        out_shape=(
            jax.ShapeDtypeStruct((lon_cells, lat_cells), jnp.float32),
            jax.ShapeDtypeStruct((radius, lat_cells), jnp.float32),
            jax.ShapeDtypeStruct((radius, lat_cells), jnp.float32),
        ),
        scratch_shapes=[pltpu.VMEM((padded, lat_cells), jnp.float32)],
    )(*partials, lists)


def backward_grad(perturb, p_low, p_high, spread, s_low, s_high, control, band_lon, band_lat):
    members, levels, lon_cells, lat_cells = control.shape
    radius = p_low.shape[2]
    padded, ext_cells = band_lon.shape
    chunk = member_chunk(members)

    def kernel(pert_ref, plow_ref, phigh_ref, spread_ref, slow_ref, shigh_ref, ctrl_ref,
               blon_ref, blat_ref, out_ref, ext_ref, along_ref):
        blon = blon_ref[...]
        spread = spread_ref[...]
        s_lo = slow_ref[...]
        s_hi = shigh_ref[...]
        for m in range(chunk):
            fill_ext(
                ext_ref,
                (pert_ref[m].astype(jnp.float32) * spread).astype(jnp.bfloat16),
                (plow_ref[m].astype(jnp.float32) * s_lo).astype(jnp.bfloat16),
                (phigh_ref[m].astype(jnp.float32) * s_hi).astype(jnp.bfloat16),
                lon_cells,
                padded,
            )
            along = jnp.dot(blon, ext_ref[...], preferred_element_type=jnp.float32)
            along_ref[m * padded:(m + 1) * padded, :] = along.astype(jnp.bfloat16)
        smoothed = jnp.dot(along_ref[...], blat_ref[...], preferred_element_type=jnp.float32)
        for m in range(chunk):
            out_ref[m] = ctrl_ref[m].astype(jnp.float32) + smoothed[
                m * padded:m * padded + lon_cells
            ]

    field = pl.BlockSpec((chunk, None, lon_cells, lat_cells), lambda l, g: (g, l, 0, 0))
    halo = pl.BlockSpec((chunk, None, radius, lat_cells), lambda l, g: (g, l, 0, 0))
    level_field = pl.BlockSpec((None, lon_cells, lat_cells), lambda l, g: (l, 0, 0))
    level_halo = pl.BlockSpec((None, radius, lat_cells), lambda l, g: (l, 0, 0))
    out = pl.pallas_call(
        kernel,
        grid=(levels, members // chunk),
        in_specs=[
            field,
            halo,
            halo,
            level_field,
            level_halo,
            level_halo,
            field,
            pl.BlockSpec(band_lon.shape, lambda l, g: (0, 0)),
            pl.BlockSpec(band_lat.shape, lambda l, g: (0, 0)),
        ],
        out_specs=pl.BlockSpec((chunk, lon_cells, None, lat_cells), lambda l, g: (g, 0, l, 0)),
        out_shape=jax.ShapeDtypeStruct((members, lon_cells, levels, lat_cells), jnp.float32),
        scratch_shapes=[
            pltpu.VMEM((ext_cells, lat_cells), jnp.bfloat16),
            pltpu.VMEM((chunk * padded, lat_cells), jnp.bfloat16),
        ],
        compiler_params=pltpu.CompilerParams(dimension_semantics=("arbitrary", "arbitrary")),
    )(perturb, p_low, p_high, spread, s_low, s_high, control, band_lon, band_lat)
    return jnp.transpose(out, (0, 2, 1, 3))


def local(control, perturb, lon_taps, lat_taps, innov, inv_var, cell_index, counts):
    members_here, levels, lon_cells, lat_cells = control.shape
    radius = lon_taps.shape[0] - 1
    padded = -(-lon_cells // 16) * 16
    band_lon, band_lat = build_bands(lon_taps, lat_taps, lon_cells, padded, lat_cells)

    slot_ids = lax.broadcasted_iota(jnp.int32, innov.shape, 2)
    weights = jnp.where(slot_ids < counts[:, :, None], inv_var, 0.0)
    lists = jnp.concatenate([innov, weights, cell_index.astype(jnp.float32)])
    lists = lax.optimization_barrier((lists, band_lon, band_lat))[0]
    received = lax.all_to_all(lists, "tile", split_axis=1, concat_axis=1, tiled=True)

    c_low, c_high = halos(control, "tile", 2, radius)
    c_low, c_high, received = lax.optimization_barrier((c_low, c_high, received))
    late_perturb = lax.optimization_barrier((perturb, c_low, c_high))[0]
    p_low, p_high = halos(late_perturb, "tile", 2, radius)
    partial = forward_pick(
        control, c_low, c_high, perturb, band_lon, band_lat, received
    )
    partials = gather_over(partial, "mem")
    spread, low_send, high_send = spread_misfits(
        partials, received, lon_cells, lat_cells, radius, padded
    )
    count = lax.axis_size("tile")
    s_low = lax.ppermute(low_send, "tile", [(i, (i + 1) % count) for i in range(count)])
    s_high = lax.ppermute(high_send, "tile", [((i + 1) % count, i) for i in range(count)])
    return backward_grad(
        perturb,
        p_low,
        p_high,
        spread[None],
        s_low[None],
        s_high[None],
        control,
        band_lon,
        band_lat,
    )


def solution(mesh):
    return jax.shard_map(
        local,
        mesh=mesh,
        in_specs=(
            P("mem", None, "tile", None),
            P("mem", None, "tile", None),
            P(),
            P(),
            P("tile", None, None),
            P("tile", None, None),
            P("tile", None, None),
            P("tile", None),
        ),
        out_specs=P("mem", None, "tile", None),
        check_vma=False,
    )
```

```python
import math

import jax
import jax.numpy as jnp
from jax import lax
from jax.experimental import pallas as pl
from jax.experimental.pallas import tpu as pltpu
from jax.sharding import PartitionSpec as P


def halos(block, axis, dim, width):
    count = lax.axis_size(axis)
    forward = [(i, (i + 1) % count) for i in range(count)]
    backward = [((i + 1) % count, i) for i in range(count)]
    low = lax.ppermute(
        lax.slice_in_dim(block, block.shape[dim] - width, None, axis=dim), axis, forward
    )
    high = lax.ppermute(lax.slice_in_dim(block, 0, width, axis=dim), axis, backward)
    return low, high


def gather_over(values, axis):
    count = lax.axis_size(axis)
    return [values] + [
        lax.ppermute(values, axis, [(i, (i + shift) % count) for i in range(count)])
        for shift in range(1, count)
    ]


def select_chain(dist, taps_ref):
    band = jnp.zeros(dist.shape, jnp.float32)
    for offset in range(taps_ref.shape[0]):
        band = jnp.where(dist == offset, taps_ref[offset], band)
    return band.astype(jnp.bfloat16)


def build_bands(lon_taps, lat_taps, lon_cells, padded, lat_cells):
    radius = lon_taps.shape[0] - 1
    ext_cells = padded + 2 * radius
    tile = 128
    tiles = -(-lat_cells // tile)

    def kernel(lon_ref, lat_ref, blon_ref, blat_ref):
        rows = lax.broadcasted_iota(jnp.int32, (padded, ext_cells), 0)
        cols = lax.broadcasted_iota(jnp.int32, (padded, ext_cells), 1)
        source = jnp.where(
            cols < padded,
            cols,
            jnp.where(
                cols < padded + radius,
                cols - padded - radius,
                cols - padded - radius + lon_cells,
            ),
        )
        valid = (rows < lon_cells) & ((cols < lon_cells) | (cols >= padded))
        dist = jnp.where(valid, jnp.abs(source - rows), radius + 1)
        blon_ref[...] = select_chain(dist, lon_ref)

        t_rows = lax.broadcasted_iota(jnp.int32, (tile, tile), 0)
        t_cols = lax.broadcasted_iota(jnp.int32, (tile, tile), 1)
        blocks = {
            shift: select_chain(jnp.abs(t_rows - t_cols + shift * tile), lat_ref)
            for shift in (-1, 0, 1)
        }
        blat_ref[...] = jnp.zeros(blat_ref.shape, blat_ref.dtype)
        for a in range(tiles):
            for b in (a - 1, a, a + 1):
                if b < 0 or b >= tiles:
                    continue
                height = min(tile, lat_cells - a * tile)
                width = min(tile, lat_cells - b * tile)
                blat_ref[a * tile:a * tile + height, b * tile:b * tile + width] = blocks[a - b][
                    :height, :width
                ]

    smem = pl.BlockSpec(memory_space=pltpu.SMEM)
    return pl.pallas_call(
        kernel,
        in_specs=[smem, smem],
        out_shape=(
            jax.ShapeDtypeStruct((padded, ext_cells), jnp.bfloat16),
            jax.ShapeDtypeStruct((lat_cells, lat_cells), jnp.bfloat16),
        ),
    )(lon_taps.astype(jnp.float32), lat_taps.astype(jnp.float32))


def member_chunk(members):
    for size in (5, 4, 3, 2, 1):
        if members % size == 0:
            return size
    return 1


def lat_conv(along_ref, blat_ref, radius):
    lat_cells = blat_ref.shape[0]
    blocks = []
    for start in range(0, lat_cells, 256):
        stop = min(lat_cells, start + 256)
        low = max(0, (start - radius) // 128 * 128)
        high = min(lat_cells, -(-(stop + radius) // 128) * 128)
        blocks.append(
            jnp.dot(
                along_ref[:, low:high],
                blat_ref[low:high, start:stop],
                preferred_element_type=jnp.float32,
            )
        )
    return jnp.concatenate(blocks, axis=1) if len(blocks) > 1 else blocks[0]


def fill_ext(ext_ref, local, low, high, lon_cells, padded):
    radius = low.shape[0]
    base = (lon_cells // 16) * 16
    ext_ref[base:padded, :] = jnp.zeros((padded - base, ext_ref.shape[1]), ext_ref.dtype)
    ext_ref[0:lon_cells, :] = local
    ext_ref[padded:padded + radius, :] = low
    ext_ref[padded + radius:padded + 2 * radius, :] = high


def split3(values):
    hi = values.astype(jnp.bfloat16)
    rest = values - hi.astype(jnp.float32)
    mid = rest.astype(jnp.bfloat16)
    lo = (rest - mid.astype(jnp.float32)).astype(jnp.bfloat16)
    return hi, mid, lo


def cell_keys(cells, padded, lat_cells):
    rows = jnp.floor((cells + 0.5) / lat_cells)
    cols = (cells - rows * lat_cells).astype(jnp.int32)
    keys = (cols // 128) * padded + rows.astype(jnp.int32)
    lane_ids = lax.broadcasted_iota(jnp.int32, (128, cells.shape[1]), 0)
    onehot = jnp.where(lane_ids == cols % 128, 1.0, 0.0).astype(jnp.bfloat16)
    return keys, onehot


def forward_pick(control, c_low, c_high, perturb, band_lon, band_lat, cells):
    members, levels, lon_cells, lat_cells = control.shape
    radius = c_low.shape[2]
    padded, ext_cells = band_lon.shape
    chunk = member_chunk(members)
    steps = members // chunk
    _, sources, slots = cells.shape
    parts = -(-lat_cells // 128)

    def kernel(ctrl_ref, low_ref, high_ref, pert_ref, blon_ref, blat_ref, cells_ref, out_ref,
               ext_ref, along_ref, acc_ref, fold_ref):
        step = pl.program_id(0)
        blon = blon_ref[...]
        for m in range(chunk):
            fill_ext(ext_ref, ctrl_ref[m], low_ref[m], high_ref[m], lon_cells, padded)
            along = jnp.dot(blon, ext_ref[...], preferred_element_type=jnp.float32)
            along_ref[m * padded:(m + 1) * padded, :] = along.astype(jnp.bfloat16)
        smoothed = lat_conv(along_ref, blat_ref, radius)
        total = pert_ref[0].astype(jnp.float32) * smoothed[0:lon_cells]
        for m in range(1, chunk):
            total = total + pert_ref[m].astype(jnp.float32) * smoothed[
                m * padded:m * padded + lon_cells
            ]

        @pl.when(step == 0)
        def _():
            acc_ref[...] = jnp.zeros(acc_ref.shape, acc_ref.dtype)

        acc_ref[0:lon_cells, :] = acc_ref[0:lon_cells, :] + total

        @pl.when(step == steps - 1)
        def _():
            fold_ref[...] = jnp.zeros(fold_ref.shape, fold_ref.dtype)
            for part in range(parts):
                width = min(128, lat_cells - part * 128)
                fold_ref[part * padded:(part + 1) * padded, 0:width] = acc_ref[
                    :, part * 128:part * 128 + width
                ]
            pieces = split3(fold_ref[...])
            key_ids = lax.broadcasted_iota(jnp.int32, (parts * padded, slots), 0)
            for row in range(sources):
                keys, onehot = cell_keys(cells_ref[2, row:row + 1, :], padded, lat_cells)
                at_keys = jnp.dot(pieces[0], onehot, preferred_element_type=jnp.float32)
                at_keys = at_keys + jnp.dot(pieces[1], onehot, preferred_element_type=jnp.float32)
                at_keys = at_keys + jnp.dot(pieces[2], onehot, preferred_element_type=jnp.float32)
                out_ref[row:row + 1, :] = jnp.sum(
                    jnp.where(key_ids == keys, at_keys, 0.0), axis=0, keepdims=True
                )

    field = pl.BlockSpec((chunk, None, lon_cells, lat_cells), lambda g: (g, 0, 0, 0))
    halo = pl.BlockSpec((chunk, None, radius, lat_cells), lambda g: (g, 0, 0, 0))
    whole = lambda shape: pl.BlockSpec(shape, lambda g: (0,) * len(shape))
    return pl.pallas_call(
        kernel,
        grid=(steps,),
        in_specs=[
            field,
            halo,
            halo,
            field,
            whole(band_lon.shape),
            whole(band_lat.shape),
            whole(cells.shape),
        ],
        out_specs=whole((sources, slots)),
        out_shape=jax.ShapeDtypeStruct((sources, slots), jnp.float32),
        scratch_shapes=[
            pltpu.VMEM((ext_cells, lat_cells), jnp.bfloat16),
            pltpu.VMEM((chunk * padded, lat_cells), jnp.bfloat16),
            pltpu.VMEM((padded, lat_cells), jnp.float32),
            pltpu.VMEM((parts * padded, 128), jnp.float32),
        ],
        compiler_params=pltpu.CompilerParams(dimension_semantics=("arbitrary",)),
    )(control, c_low, c_high, perturb, band_lon, band_lat, cells)


def spread_misfits(partials, lists, lon_cells, lat_cells, radius, padded):
    _, sources, slots = lists.shape
    parts = -(-lat_cells // 128)

    def kernel(*refs):
        part_refs = refs[:len(partials)]
        lists_ref, spread_ref, low_ref, high_ref, fold_ref = refs[len(partials):]
        at_cells = part_refs[0][...]
        for ref in part_refs[1:]:
            at_cells = at_cells + ref[...]
        key_ids = lax.broadcasted_iota(jnp.int32, (parts * padded, slots), 0)
        folded = jnp.zeros((parts * padded, 128), jnp.float32)
        for row in range(sources):
            misfit = lists_ref[1, row:row + 1, :] * (
                at_cells[row:row + 1, :] - lists_ref[0, row:row + 1, :]
            )
            keys, onehot = cell_keys(lists_ref[2, row:row + 1, :], padded, lat_cells)
            for piece in split3(misfit):
                weighted = jnp.where(key_ids == keys, piece.astype(jnp.float32), 0.0)
                folded = folded + lax.dot_general(
                    weighted.astype(jnp.bfloat16),
                    onehot,
                    (((1,), (1,)), ((), ())),
                    preferred_element_type=jnp.float32,
                )
        for part in range(parts):
            width = min(128, lat_cells - part * 128)
            fold_ref[:, part * 128:part * 128 + width] = folded[
                part * padded:(part + 1) * padded, 0:width
            ]
        spread_ref[...] = fold_ref[0:lon_cells, :]
        low_ref[...] = fold_ref[lon_cells - radius:lon_cells, :]
        high_ref[...] = fold_ref[0:radius, :]

    return pl.pallas_call(
        kernel,
        out_shape=(
            jax.ShapeDtypeStruct((lon_cells, lat_cells), jnp.float32),
            jax.ShapeDtypeStruct((radius, lat_cells), jnp.float32),
            jax.ShapeDtypeStruct((radius, lat_cells), jnp.float32),
        ),
        scratch_shapes=[pltpu.VMEM((padded, lat_cells), jnp.float32)],
    )(*partials, lists)


def backward_grad(perturb, p_low, p_high, spread, s_low, s_high, control, band_lon, band_lat):
    members, levels, lon_cells, lat_cells = control.shape
    radius = p_low.shape[2]
    padded, ext_cells = band_lon.shape
    chunk = member_chunk(members)

    def kernel(pert_ref, plow_ref, phigh_ref, spread_ref, slow_ref, shigh_ref, ctrl_ref,
               blon_ref, blat_ref, out_ref, ext_ref, along_ref):
        blon = blon_ref[...]
        spread = spread_ref[...]
        s_lo = slow_ref[...]
        s_hi = shigh_ref[...]
        for m in range(chunk):
            fill_ext(
                ext_ref,
                (pert_ref[m].astype(jnp.float32) * spread).astype(jnp.bfloat16),
                (plow_ref[m].astype(jnp.float32) * s_lo).astype(jnp.bfloat16),
                (phigh_ref[m].astype(jnp.float32) * s_hi).astype(jnp.bfloat16),
                lon_cells,
                padded,
            )
            along = jnp.dot(blon, ext_ref[...], preferred_element_type=jnp.float32)
            along_ref[m * padded:(m + 1) * padded, :] = along.astype(jnp.bfloat16)
        smoothed = lat_conv(along_ref, blat_ref, radius)
        for m in range(chunk):
            out_ref[m] = ctrl_ref[m].astype(jnp.float32) + smoothed[
                m * padded:m * padded + lon_cells
            ]

    field = pl.BlockSpec((chunk, None, lon_cells, lat_cells), lambda l, g: (g, l, 0, 0))
    halo = pl.BlockSpec((chunk, None, radius, lat_cells), lambda l, g: (g, l, 0, 0))
    level_field = pl.BlockSpec((None, lon_cells, lat_cells), lambda l, g: (l, 0, 0))
    level_halo = pl.BlockSpec((None, radius, lat_cells), lambda l, g: (l, 0, 0))
    out = pl.pallas_call(
        kernel,
        grid=(levels, members // chunk),
        in_specs=[
            field,
            halo,
            halo,
            level_field,
            level_halo,
            level_halo,
            field,
            pl.BlockSpec(band_lon.shape, lambda l, g: (0, 0)),
            pl.BlockSpec(band_lat.shape, lambda l, g: (0, 0)),
        ],
        out_specs=pl.BlockSpec((chunk, lon_cells, None, lat_cells), lambda l, g: (g, 0, l, 0)),
        out_shape=jax.ShapeDtypeStruct((members, lon_cells, levels, lat_cells), jnp.float32),
        scratch_shapes=[
            pltpu.VMEM((ext_cells, lat_cells), jnp.bfloat16),
            pltpu.VMEM((chunk * padded, lat_cells), jnp.bfloat16),
        ],
        compiler_params=pltpu.CompilerParams(dimension_semantics=("arbitrary", "arbitrary")),
    )(perturb, p_low, p_high, spread, s_low, s_high, control, band_lon, band_lat)
    return jnp.transpose(out, (0, 2, 1, 3))


def local(control, perturb, lon_taps, lat_taps, innov, inv_var, cell_index, counts):
    members_here, levels, lon_cells, lat_cells = control.shape
    radius = lon_taps.shape[0] - 1
    padded = -(-lon_cells // 16) * 16
    band_lon, band_lat = build_bands(lon_taps, lat_taps, lon_cells, padded, lat_cells)

    slot_ids = lax.broadcasted_iota(jnp.int32, innov.shape, 2)
    weights = jnp.where(slot_ids < counts[:, :, None], inv_var, 0.0)
    lists = jnp.concatenate([innov, weights, cell_index.astype(jnp.float32)])
    lists = lax.optimization_barrier((lists, band_lon, band_lat))[0]
    received = lax.all_to_all(lists, "tile", split_axis=1, concat_axis=1, tiled=True)

    c_low, c_high = halos(control, "tile", 2, radius)
    c_low, c_high, received = lax.optimization_barrier((c_low, c_high, received))
    late_perturb = lax.optimization_barrier((perturb, c_low, c_high))[0]
    p_low, p_high = halos(late_perturb, "tile", 2, radius)
    partial = forward_pick(
        control, c_low, c_high, perturb, band_lon, band_lat, received
    )
    partials = gather_over(partial, "mem")
    spread, low_send, high_send = spread_misfits(
        partials, received, lon_cells, lat_cells, radius, padded
    )
    count = lax.axis_size("tile")
    s_low = lax.ppermute(low_send, "tile", [(i, (i + 1) % count) for i in range(count)])
    s_high = lax.ppermute(high_send, "tile", [((i + 1) % count, i) for i in range(count)])
    return backward_grad(
        perturb,
        p_low,
        p_high,
        spread[None],
        s_low[None],
        s_high[None],
        control,
        band_lon,
        band_lat,
    )


def solution(mesh):
    return jax.shard_map(
        local,
        mesh=mesh,
        in_specs=(
            P("mem", None, "tile", None),
            P("mem", None, "tile", None),
            P(),
            P(),
            P("tile", None, None),
            P("tile", None, None),
            P("tile", None, None),
            P("tile", None),
        ),
        out_specs=P("mem", None, "tile", None),
        check_vma=False,
    )
```

```python
import math

import jax
import jax.numpy as jnp
from jax import lax
from jax.experimental import pallas as pl
from jax.experimental.pallas import tpu as pltpu
from jax.sharding import PartitionSpec as P


def halos(block, axis, dim, width):
    count = lax.axis_size(axis)
    forward = [(i, (i + 1) % count) for i in range(count)]
    backward = [((i + 1) % count, i) for i in range(count)]
    low = lax.ppermute(
        lax.slice_in_dim(block, block.shape[dim] - width, None, axis=dim), axis, forward
    )
    high = lax.ppermute(lax.slice_in_dim(block, 0, width, axis=dim), axis, backward)
    return low, high


def gather_over(values, axis):
    count = lax.axis_size(axis)
    return [values] + [
        lax.ppermute(values, axis, [(i, (i + shift) % count) for i in range(count)])
        for shift in range(1, count)
    ]


def select_chain(dist, taps_ref):
    band = jnp.zeros(dist.shape, jnp.float32)
    for offset in range(taps_ref.shape[0]):
        band = jnp.where(dist == offset, taps_ref[offset], band)
    return band.astype(jnp.bfloat16)


def build_bands(lon_taps, lat_taps, lon_cells, padded, lat_cells):
    radius = lon_taps.shape[0] - 1
    ext_cells = padded + 2 * radius
    tile = 128
    tiles = -(-lat_cells // tile)

    def kernel(lon_ref, lat_ref, blon_ref, blat_ref):
        rows = lax.broadcasted_iota(jnp.int32, (padded, ext_cells), 0)
        cols = lax.broadcasted_iota(jnp.int32, (padded, ext_cells), 1)
        source = jnp.where(
            cols < padded,
            cols,
            jnp.where(
                cols < padded + radius,
                cols - padded - radius,
                cols - padded - radius + lon_cells,
            ),
        )
        valid = (rows < lon_cells) & ((cols < lon_cells) | (cols >= padded))
        dist = jnp.where(valid, jnp.abs(source - rows), radius + 1)
        blon_ref[...] = select_chain(dist, lon_ref)

        t_rows = lax.broadcasted_iota(jnp.int32, (tile, tile), 0)
        t_cols = lax.broadcasted_iota(jnp.int32, (tile, tile), 1)
        blocks = {
            shift: select_chain(jnp.abs(t_rows - t_cols + shift * tile), lat_ref)
            for shift in (-1, 0, 1)
        }
        blat_ref[...] = jnp.zeros(blat_ref.shape, blat_ref.dtype)
        for a in range(tiles):
            for b in (a - 1, a, a + 1):
                if b < 0 or b >= tiles:
                    continue
                height = min(tile, lat_cells - a * tile)
                width = min(tile, lat_cells - b * tile)
                blat_ref[a * tile:a * tile + height, b * tile:b * tile + width] = blocks[a - b][
                    :height, :width
                ]

    smem = pl.BlockSpec(memory_space=pltpu.SMEM)
    return pl.pallas_call(
        kernel,
        in_specs=[smem, smem],
        out_shape=(
            jax.ShapeDtypeStruct((padded, ext_cells), jnp.bfloat16),
            jax.ShapeDtypeStruct((lat_cells, lat_cells), jnp.bfloat16),
        ),
    )(lon_taps.astype(jnp.float32), lat_taps.astype(jnp.float32))


def member_chunk(members):
    for size in (10, 8, 5, 4, 3, 2, 1):
        if members % size == 0:
            return size
    return 1


def lat_conv(along_ref, blat_ref, radius):
    lat_cells = blat_ref.shape[0]
    blocks = []
    for start in range(0, lat_cells, 256):
        stop = min(lat_cells, start + 256)
        low = max(0, (start - radius) // 128 * 128)
        high = min(lat_cells, -(-(stop + radius) // 128) * 128)
        blocks.append(
            jnp.dot(
                along_ref[:, low:high],
                blat_ref[low:high, start:stop],
                preferred_element_type=jnp.float32,
            )
        )
    return jnp.concatenate(blocks, axis=1) if len(blocks) > 1 else blocks[0]


def fill_ext(ext_ref, local, low, high, lon_cells, padded):
    radius = low.shape[0]
    base = (lon_cells // 16) * 16
    ext_ref[base:padded, :] = jnp.zeros((padded - base, ext_ref.shape[1]), ext_ref.dtype)
    ext_ref[0:lon_cells, :] = local
    ext_ref[padded:padded + radius, :] = low
    ext_ref[padded + radius:padded + 2 * radius, :] = high


def split3(values):
    hi = values.astype(jnp.bfloat16)
    rest = values - hi.astype(jnp.float32)
    mid = rest.astype(jnp.bfloat16)
    lo = (rest - mid.astype(jnp.float32)).astype(jnp.bfloat16)
    return hi, mid, lo


def cell_keys(cells, padded, lat_cells):
    rows = jnp.floor((cells + 0.5) / lat_cells)
    cols = (cells - rows * lat_cells).astype(jnp.int32)
    keys = (cols // 128) * padded + rows.astype(jnp.int32)
    lane_ids = lax.broadcasted_iota(jnp.int32, (128, cells.shape[1]), 0)
    onehot = jnp.where(lane_ids == cols % 128, 1.0, 0.0).astype(jnp.bfloat16)
    return keys, onehot


def forward_pick(control, c_low, c_high, perturb, band_lon, band_lat, cells):
    members, levels, lon_cells, lat_cells = control.shape
    radius = c_low.shape[2]
    padded, ext_cells = band_lon.shape
    chunk = member_chunk(members)
    steps = members // chunk
    _, sources, slots = cells.shape
    parts = -(-lat_cells // 128)

    def kernel(ctrl_ref, low_ref, high_ref, pert_ref, blon_ref, blat_ref, cells_ref, out_ref,
               ext_ref, along_ref, acc_ref, fold_ref):
        step = pl.program_id(0)
        blon = blon_ref[...]
        for m in range(chunk):
            fill_ext(ext_ref, ctrl_ref[m], low_ref[m], high_ref[m], lon_cells, padded)
            along = jnp.dot(blon, ext_ref[...], preferred_element_type=jnp.float32)
            along_ref[m * padded:(m + 1) * padded, :] = along.astype(jnp.bfloat16)
        smoothed = lat_conv(along_ref, blat_ref, radius)
        total = pert_ref[0].astype(jnp.float32) * smoothed[0:lon_cells]
        for m in range(1, chunk):
            total = total + pert_ref[m].astype(jnp.float32) * smoothed[
                m * padded:m * padded + lon_cells
            ]

        @pl.when(step == 0)
        def _():
            acc_ref[...] = jnp.zeros(acc_ref.shape, acc_ref.dtype)

        acc_ref[0:lon_cells, :] = acc_ref[0:lon_cells, :] + total

        @pl.when(step == steps - 1)
        def _():
            fold_ref[...] = jnp.zeros(fold_ref.shape, fold_ref.dtype)
            for part in range(parts):
                width = min(128, lat_cells - part * 128)
                fold_ref[part * padded:(part + 1) * padded, 0:width] = acc_ref[
                    :, part * 128:part * 128 + width
                ]
            pieces = split3(fold_ref[...])
            key_ids = lax.broadcasted_iota(jnp.int32, (parts * padded, slots), 0)
            for row in range(sources):
                keys, onehot = cell_keys(cells_ref[2, row:row + 1, :], padded, lat_cells)
                at_keys = jnp.dot(pieces[0], onehot, preferred_element_type=jnp.float32)
                at_keys = at_keys + jnp.dot(pieces[1], onehot, preferred_element_type=jnp.float32)
                at_keys = at_keys + jnp.dot(pieces[2], onehot, preferred_element_type=jnp.float32)
                out_ref[row:row + 1, :] = jnp.sum(
                    jnp.where(key_ids == keys, at_keys, 0.0), axis=0, keepdims=True
                )

    field = pl.BlockSpec((chunk, None, lon_cells, lat_cells), lambda g: (g, 0, 0, 0))
    halo = pl.BlockSpec((chunk, None, radius, lat_cells), lambda g: (g, 0, 0, 0))
    whole = lambda shape: pl.BlockSpec(shape, lambda g: (0,) * len(shape))
    return pl.pallas_call(
        kernel,
        grid=(steps,),
        in_specs=[
            field,
            halo,
            halo,
            field,
            whole(band_lon.shape),
            whole(band_lat.shape),
            whole(cells.shape),
        ],
        out_specs=whole((sources, slots)),
        out_shape=jax.ShapeDtypeStruct((sources, slots), jnp.float32),
        scratch_shapes=[
            pltpu.VMEM((ext_cells, lat_cells), jnp.bfloat16),
            pltpu.VMEM((chunk * padded, lat_cells), jnp.bfloat16),
            pltpu.VMEM((padded, lat_cells), jnp.float32),
            pltpu.VMEM((parts * padded, 128), jnp.float32),
        ],
        compiler_params=pltpu.CompilerParams(dimension_semantics=("arbitrary",)),
    )(control, c_low, c_high, perturb, band_lon, band_lat, cells)


def spread_misfits(partials, lists, lon_cells, lat_cells, radius, padded):
    _, sources, slots = lists.shape
    parts = -(-lat_cells // 128)

    def kernel(*refs):
        part_refs = refs[:len(partials)]
        lists_ref, spread_ref, low_ref, high_ref, fold_ref = refs[len(partials):]
        at_cells = part_refs[0][...]
        for ref in part_refs[1:]:
            at_cells = at_cells + ref[...]
        key_ids = lax.broadcasted_iota(jnp.int32, (parts * padded, slots), 0)
        folded = jnp.zeros((parts * padded, 128), jnp.float32)
        for row in range(sources):
            misfit = lists_ref[1, row:row + 1, :] * (
                at_cells[row:row + 1, :] - lists_ref[0, row:row + 1, :]
            )
            keys, onehot = cell_keys(lists_ref[2, row:row + 1, :], padded, lat_cells)
            for piece in split3(misfit):
                weighted = jnp.where(key_ids == keys, piece.astype(jnp.float32), 0.0)
                folded = folded + lax.dot_general(
                    weighted.astype(jnp.bfloat16),
                    onehot,
                    (((1,), (1,)), ((), ())),
                    preferred_element_type=jnp.float32,
                )
        for part in range(parts):
            width = min(128, lat_cells - part * 128)
            fold_ref[:, part * 128:part * 128 + width] = folded[
                part * padded:(part + 1) * padded, 0:width
            ]
        spread_ref[...] = fold_ref[0:lon_cells, :]
        low_ref[...] = fold_ref[lon_cells - radius:lon_cells, :]
        high_ref[...] = fold_ref[0:radius, :]

    return pl.pallas_call(
        kernel,
        out_shape=(
            jax.ShapeDtypeStruct((lon_cells, lat_cells), jnp.float32),
            jax.ShapeDtypeStruct((radius, lat_cells), jnp.float32),
            jax.ShapeDtypeStruct((radius, lat_cells), jnp.float32),
        ),
        scratch_shapes=[pltpu.VMEM((padded, lat_cells), jnp.float32)],
    )(*partials, lists)


def backward_grad(perturb, p_low, p_high, spread, s_low, s_high, control, band_lon, band_lat):
    members, levels, lon_cells, lat_cells = control.shape
    radius = p_low.shape[2]
    padded, ext_cells = band_lon.shape
    chunk = member_chunk(members)

    def kernel(pert_ref, plow_ref, phigh_ref, spread_ref, slow_ref, shigh_ref, ctrl_ref,
               blon_ref, blat_ref, out_ref, ext_ref, along_ref):
        blon = blon_ref[...]
        spread = spread_ref[...]
        s_lo = slow_ref[...]
        s_hi = shigh_ref[...]
        for m in range(chunk):
            fill_ext(
                ext_ref,
                (pert_ref[m].astype(jnp.float32) * spread).astype(jnp.bfloat16),
                (plow_ref[m].astype(jnp.float32) * s_lo).astype(jnp.bfloat16),
                (phigh_ref[m].astype(jnp.float32) * s_hi).astype(jnp.bfloat16),
                lon_cells,
                padded,
            )
            along = jnp.dot(blon, ext_ref[...], preferred_element_type=jnp.float32)
            along_ref[m * padded:(m + 1) * padded, :] = along.astype(jnp.bfloat16)
        smoothed = lat_conv(along_ref, blat_ref, radius)
        for m in range(chunk):
            out_ref[m] = ctrl_ref[m].astype(jnp.float32) + smoothed[
                m * padded:m * padded + lon_cells
            ]

    field = pl.BlockSpec((chunk, None, lon_cells, lat_cells), lambda l, g: (g, l, 0, 0))
    halo = pl.BlockSpec((chunk, None, radius, lat_cells), lambda l, g: (g, l, 0, 0))
    level_field = pl.BlockSpec((None, lon_cells, lat_cells), lambda l, g: (l, 0, 0))
    level_halo = pl.BlockSpec((None, radius, lat_cells), lambda l, g: (l, 0, 0))
    out = pl.pallas_call(
        kernel,
        grid=(levels, members // chunk),
        in_specs=[
            field,
            halo,
            halo,
            level_field,
            level_halo,
            level_halo,
            field,
            pl.BlockSpec(band_lon.shape, lambda l, g: (0, 0)),
            pl.BlockSpec(band_lat.shape, lambda l, g: (0, 0)),
        ],
        out_specs=pl.BlockSpec((chunk, lon_cells, None, lat_cells), lambda l, g: (g, 0, l, 0)),
        out_shape=jax.ShapeDtypeStruct((members, lon_cells, levels, lat_cells), jnp.float32),
        scratch_shapes=[
            pltpu.VMEM((ext_cells, lat_cells), jnp.bfloat16),
            pltpu.VMEM((chunk * padded, lat_cells), jnp.bfloat16),
        ],
        compiler_params=pltpu.CompilerParams(dimension_semantics=("arbitrary", "arbitrary")),
    )(perturb, p_low, p_high, spread, s_low, s_high, control, band_lon, band_lat)
    return jnp.transpose(out, (0, 2, 1, 3))


def local(control, perturb, lon_taps, lat_taps, innov, inv_var, cell_index, counts):
    members_here, levels, lon_cells, lat_cells = control.shape
    radius = lon_taps.shape[0] - 1
    padded = -(-lon_cells // 16) * 16
    band_lon, band_lat = build_bands(lon_taps, lat_taps, lon_cells, padded, lat_cells)

    slot_ids = lax.broadcasted_iota(jnp.int32, innov.shape, 2)
    weights = jnp.where(slot_ids < counts[:, :, None], inv_var, 0.0)
    lists = jnp.concatenate([innov, weights, cell_index.astype(jnp.float32)])
    lists = lax.optimization_barrier((lists, band_lon, band_lat))[0]
    received = lax.all_to_all(lists, "tile", split_axis=1, concat_axis=1, tiled=True)

    c_low, c_high = halos(control, "tile", 2, radius)
    c_low, c_high, received = lax.optimization_barrier((c_low, c_high, received))
    late_perturb = lax.optimization_barrier((perturb, c_low, c_high))[0]
    p_low, p_high = halos(late_perturb, "tile", 2, radius)
    partial = forward_pick(
        control, c_low, c_high, perturb, band_lon, band_lat, received
    )
    partials = gather_over(partial, "mem")
    spread, low_send, high_send = spread_misfits(
        partials, received, lon_cells, lat_cells, radius, padded
    )
    count = lax.axis_size("tile")
    s_low = lax.ppermute(low_send, "tile", [(i, (i + 1) % count) for i in range(count)])
    s_high = lax.ppermute(high_send, "tile", [((i + 1) % count, i) for i in range(count)])
    return backward_grad(
        perturb,
        p_low,
        p_high,
        spread[None],
        s_low[None],
        s_high[None],
        control,
        band_lon,
        band_lat,
    )


def solution(mesh):
    return jax.shard_map(
        local,
        mesh=mesh,
        in_specs=(
            P("mem", None, "tile", None),
            P("mem", None, "tile", None),
            P(),
            P(),
            P("tile", None, None),
            P("tile", None, None),
            P("tile", None, None),
            P("tile", None),
        ),
        out_specs=P("mem", None, "tile", None),
        check_vma=False,
    )
```

```python
import math

import jax
import jax.numpy as jnp
from jax import lax
from jax.experimental import pallas as pl
from jax.experimental.pallas import tpu as pltpu
from jax.sharding import PartitionSpec as P


def halos(block, axis, dim, width):
    count = lax.axis_size(axis)
    forward = [(i, (i + 1) % count) for i in range(count)]
    backward = [((i + 1) % count, i) for i in range(count)]
    low = lax.ppermute(
        lax.slice_in_dim(block, block.shape[dim] - width, None, axis=dim), axis, forward
    )
    high = lax.ppermute(lax.slice_in_dim(block, 0, width, axis=dim), axis, backward)
    return low, high


def gather_over(values, axis):
    count = lax.axis_size(axis)
    return [values] + [
        lax.ppermute(values, axis, [(i, (i + shift) % count) for i in range(count)])
        for shift in range(1, count)
    ]


def select_chain(dist, taps_ref):
    band = jnp.zeros(dist.shape, jnp.float32)
    for offset in range(taps_ref.shape[0]):
        band = jnp.where(dist == offset, taps_ref[offset], band)
    return band.astype(jnp.bfloat16)


def build_bands(lon_taps, lat_taps, lon_cells, padded, lat_cells):
    radius = lon_taps.shape[0] - 1
    ext_cells = padded + 2 * radius
    tile = 128
    tiles = -(-lat_cells // tile)

    def kernel(lon_ref, lat_ref, blon_ref, blat_ref):
        rows = lax.broadcasted_iota(jnp.int32, (padded, ext_cells), 0)
        cols = lax.broadcasted_iota(jnp.int32, (padded, ext_cells), 1)
        source = jnp.where(
            cols < padded,
            cols,
            jnp.where(
                cols < padded + radius,
                cols - padded - radius,
                cols - padded - radius + lon_cells,
            ),
        )
        valid = (rows < lon_cells) & ((cols < lon_cells) | (cols >= padded))
        dist = jnp.where(valid, jnp.abs(source - rows), radius + 1)
        blon_ref[...] = select_chain(dist, lon_ref)

        t_rows = lax.broadcasted_iota(jnp.int32, (tile, tile), 0)
        t_cols = lax.broadcasted_iota(jnp.int32, (tile, tile), 1)
        blocks = {
            shift: select_chain(jnp.abs(t_rows - t_cols + shift * tile), lat_ref)
            for shift in (-1, 0, 1)
        }
        blat_ref[...] = jnp.zeros(blat_ref.shape, blat_ref.dtype)
        for a in range(tiles):
            for b in (a - 1, a, a + 1):
                if b < 0 or b >= tiles:
                    continue
                height = min(tile, lat_cells - a * tile)
                width = min(tile, lat_cells - b * tile)
                blat_ref[a * tile:a * tile + height, b * tile:b * tile + width] = blocks[a - b][
                    :height, :width
                ]

    smem = pl.BlockSpec(memory_space=pltpu.SMEM)
    return pl.pallas_call(
        kernel,
        in_specs=[smem, smem],
        out_shape=(
            jax.ShapeDtypeStruct((padded, ext_cells), jnp.bfloat16),
            jax.ShapeDtypeStruct((lat_cells, lat_cells), jnp.bfloat16),
        ),
    )(lon_taps.astype(jnp.float32), lat_taps.astype(jnp.float32))


def member_chunk(members):
    for size in (10, 8, 5, 4, 3, 2, 1):
        if members % size == 0:
            return size
    return 1


def lat_conv(along_ref, blat_ref, radius):
    lat_cells = blat_ref.shape[0]
    blocks = []
    for start in range(0, lat_cells, 256):
        stop = min(lat_cells, start + 256)
        low = max(0, (start - radius) // 128 * 128)
        high = min(lat_cells, -(-(stop + radius) // 128) * 128)
        blocks.append(
            jnp.dot(
                along_ref[:, low:high],
                blat_ref[low:high, start:stop],
                preferred_element_type=jnp.float32,
            )
        )
    return jnp.concatenate(blocks, axis=1) if len(blocks) > 1 else blocks[0]


def fill_ext(ext_ref, local, low, high, lon_cells, padded):
    radius = low.shape[0]
    base = (lon_cells // 16) * 16
    ext_ref[base:padded, :] = jnp.zeros((padded - base, ext_ref.shape[1]), ext_ref.dtype)
    ext_ref[0:lon_cells, :] = local
    ext_ref[padded:padded + radius, :] = low
    ext_ref[padded + radius:padded + 2 * radius, :] = high


def split3(values):
    hi = values.astype(jnp.bfloat16)
    rest = values - hi.astype(jnp.float32)
    mid = rest.astype(jnp.bfloat16)
    lo = (rest - mid.astype(jnp.float32)).astype(jnp.bfloat16)
    return hi, mid, lo


def cell_keys(cells, padded, lat_cells):
    rows = jnp.floor((cells + 0.5) / lat_cells)
    cols = (cells - rows * lat_cells).astype(jnp.int32)
    keys = (cols // 128) * padded + rows.astype(jnp.int32)
    lane_ids = lax.broadcasted_iota(jnp.int32, (128, cells.shape[1]), 0)
    onehot = jnp.where(lane_ids == cols % 128, 1.0, 0.0).astype(jnp.bfloat16)
    return keys, onehot


def forward_pick(control, c_low, c_high, perturb, band_lon, band_lat, cells):
    members, levels, lon_cells, lat_cells = control.shape
    radius = c_low.shape[2]
    padded, ext_cells = band_lon.shape
    chunk = members
    steps = 1
    _, sources, slots = cells.shape
    parts = -(-lat_cells // 128)

    def kernel(ctrl_ref, low_ref, high_ref, pert_ref, blon_ref, blat_ref, cells_ref, out_ref,
               ext_ref, along_ref, acc_ref, fold_ref):
        step = pl.program_id(0)
        blon = blon_ref[...]
        for m in range(chunk):
            fill_ext(ext_ref, ctrl_ref[m], low_ref[m], high_ref[m], lon_cells, padded)
            along = jnp.dot(blon, ext_ref[...], preferred_element_type=jnp.float32)
            along_ref[m * padded:(m + 1) * padded, :] = along.astype(jnp.bfloat16)
        smoothed = lat_conv(along_ref, blat_ref, radius)
        total = pert_ref[0].astype(jnp.float32) * smoothed[0:lon_cells]
        for m in range(1, chunk):
            total = total + pert_ref[m].astype(jnp.float32) * smoothed[
                m * padded:m * padded + lon_cells
            ]

        @pl.when(step == 0)
        def _():
            acc_ref[...] = jnp.zeros(acc_ref.shape, acc_ref.dtype)

        acc_ref[0:lon_cells, :] = acc_ref[0:lon_cells, :] + total

        @pl.when(step == steps - 1)
        def _():
            fold_ref[...] = jnp.zeros(fold_ref.shape, fold_ref.dtype)
            for part in range(parts):
                width = min(128, lat_cells - part * 128)
                fold_ref[part * padded:(part + 1) * padded, 0:width] = acc_ref[
                    :, part * 128:part * 128 + width
                ]
            pieces = split3(fold_ref[...])
            key_ids = lax.broadcasted_iota(jnp.int32, (parts * padded, slots), 0)
            for row in range(sources):
                keys, onehot = cell_keys(cells_ref[2, row:row + 1, :], padded, lat_cells)
                at_keys = jnp.dot(pieces[0], onehot, preferred_element_type=jnp.float32)
                at_keys = at_keys + jnp.dot(pieces[1], onehot, preferred_element_type=jnp.float32)
                at_keys = at_keys + jnp.dot(pieces[2], onehot, preferred_element_type=jnp.float32)
                out_ref[row:row + 1, :] = jnp.sum(
                    jnp.where(key_ids == keys, at_keys, 0.0), axis=0, keepdims=True
                )

    field = pl.BlockSpec((chunk, None, lon_cells, lat_cells), lambda g: (g, 0, 0, 0))
    halo = pl.BlockSpec((chunk, None, radius, lat_cells), lambda g: (g, 0, 0, 0))
    whole = lambda shape: pl.BlockSpec(shape, lambda g: (0,) * len(shape))
    return pl.pallas_call(
        kernel,
        grid=(steps,),
        in_specs=[
            field,
            halo,
            halo,
            field,
            whole(band_lon.shape),
            whole(band_lat.shape),
            whole(cells.shape),
        ],
        out_specs=whole((sources, slots)),
        out_shape=jax.ShapeDtypeStruct((sources, slots), jnp.float32),
        scratch_shapes=[
            pltpu.VMEM((ext_cells, lat_cells), jnp.bfloat16),
            pltpu.VMEM((chunk * padded, lat_cells), jnp.bfloat16),
            pltpu.VMEM((padded, lat_cells), jnp.float32),
            pltpu.VMEM((parts * padded, 128), jnp.float32),
        ],
        compiler_params=pltpu.CompilerParams(dimension_semantics=("arbitrary",)),
    )(control, c_low, c_high, perturb, band_lon, band_lat, cells)


def spread_misfits(partials, lists, lon_cells, lat_cells, radius, padded):
    _, sources, slots = lists.shape
    parts = -(-lat_cells // 128)

    def kernel(*refs):
        part_refs = refs[:len(partials)]
        lists_ref, spread_ref, low_ref, high_ref, fold_ref = refs[len(partials):]
        at_cells = part_refs[0][...]
        for ref in part_refs[1:]:
            at_cells = at_cells + ref[...]
        key_ids = lax.broadcasted_iota(jnp.int32, (parts * padded, slots), 0)
        folded = jnp.zeros((parts * padded, 128), jnp.float32)
        for row in range(sources):
            misfit = lists_ref[1, row:row + 1, :] * (
                at_cells[row:row + 1, :] - lists_ref[0, row:row + 1, :]
            )
            keys, onehot = cell_keys(lists_ref[2, row:row + 1, :], padded, lat_cells)
            for piece in split3(misfit):
                weighted = jnp.where(key_ids == keys, piece.astype(jnp.float32), 0.0)
                folded = folded + lax.dot_general(
                    weighted.astype(jnp.bfloat16),
                    onehot,
                    (((1,), (1,)), ((), ())),
                    preferred_element_type=jnp.float32,
                )
        for part in range(parts):
            width = min(128, lat_cells - part * 128)
            fold_ref[:, part * 128:part * 128 + width] = folded[
                part * padded:(part + 1) * padded, 0:width
            ]
        spread_ref[...] = fold_ref[0:lon_cells, :]
        low_ref[...] = fold_ref[lon_cells - radius:lon_cells, :]
        high_ref[...] = fold_ref[0:radius, :]

    return pl.pallas_call(
        kernel,
        out_shape=(
            jax.ShapeDtypeStruct((lon_cells, lat_cells), jnp.float32),
            jax.ShapeDtypeStruct((radius, lat_cells), jnp.float32),
            jax.ShapeDtypeStruct((radius, lat_cells), jnp.float32),
        ),
        scratch_shapes=[pltpu.VMEM((padded, lat_cells), jnp.float32)],
    )(*partials, lists)


def backward_grad(perturb, p_low, p_high, spread, s_low, s_high, control, band_lon, band_lat):
    members, levels, lon_cells, lat_cells = control.shape
    radius = p_low.shape[2]
    padded, ext_cells = band_lon.shape
    chunk = member_chunk(members)

    def kernel(pert_ref, plow_ref, phigh_ref, spread_ref, slow_ref, shigh_ref, ctrl_ref,
               blon_ref, blat_ref, out_ref, ext_ref, along_ref):
        blon = blon_ref[...]
        spread = spread_ref[...]
        s_lo = slow_ref[...]
        s_hi = shigh_ref[...]
        for m in range(chunk):
            fill_ext(
                ext_ref,
                (pert_ref[m].astype(jnp.float32) * spread).astype(jnp.bfloat16),
                (plow_ref[m].astype(jnp.float32) * s_lo).astype(jnp.bfloat16),
                (phigh_ref[m].astype(jnp.float32) * s_hi).astype(jnp.bfloat16),
                lon_cells,
                padded,
            )
            along = jnp.dot(blon, ext_ref[...], preferred_element_type=jnp.float32)
            along_ref[m * padded:(m + 1) * padded, :] = along.astype(jnp.bfloat16)
        smoothed = lat_conv(along_ref, blat_ref, radius)
        for m in range(chunk):
            out_ref[m] = ctrl_ref[m].astype(jnp.float32) + smoothed[
                m * padded:m * padded + lon_cells
            ]

    field = pl.BlockSpec((chunk, None, lon_cells, lat_cells), lambda l, g: (g, l, 0, 0))
    halo = pl.BlockSpec((chunk, None, radius, lat_cells), lambda l, g: (g, l, 0, 0))
    level_field = pl.BlockSpec((None, lon_cells, lat_cells), lambda l, g: (l, 0, 0))
    level_halo = pl.BlockSpec((None, radius, lat_cells), lambda l, g: (l, 0, 0))
    out = pl.pallas_call(
        kernel,
        grid=(levels, members // chunk),
        in_specs=[
            field,
            halo,
            halo,
            level_field,
            level_halo,
            level_halo,
            field,
            pl.BlockSpec(band_lon.shape, lambda l, g: (0, 0)),
            pl.BlockSpec(band_lat.shape, lambda l, g: (0, 0)),
        ],
        out_specs=pl.BlockSpec((chunk, lon_cells, None, lat_cells), lambda l, g: (g, 0, l, 0)),
        out_shape=jax.ShapeDtypeStruct((members, lon_cells, levels, lat_cells), jnp.float32),
        scratch_shapes=[
            pltpu.VMEM((ext_cells, lat_cells), jnp.bfloat16),
            pltpu.VMEM((chunk * padded, lat_cells), jnp.bfloat16),
        ],
        compiler_params=pltpu.CompilerParams(dimension_semantics=("arbitrary", "arbitrary")),
    )(perturb, p_low, p_high, spread, s_low, s_high, control, band_lon, band_lat)
    return jnp.transpose(out, (0, 2, 1, 3))


def local(control, perturb, lon_taps, lat_taps, innov, inv_var, cell_index, counts):
    members_here, levels, lon_cells, lat_cells = control.shape
    radius = lon_taps.shape[0] - 1
    padded = -(-lon_cells // 16) * 16
    band_lon, band_lat = build_bands(lon_taps, lat_taps, lon_cells, padded, lat_cells)

    slot_ids = lax.broadcasted_iota(jnp.int32, innov.shape, 2)
    weights = jnp.where(slot_ids < counts[:, :, None], inv_var, 0.0)
    lists = jnp.concatenate([innov, weights, cell_index.astype(jnp.float32)])
    lists = lax.optimization_barrier((lists, band_lon, band_lat))[0]
    received = lax.all_to_all(lists, "tile", split_axis=1, concat_axis=1, tiled=True)

    c_low, c_high = halos(control, "tile", 2, radius)
    c_low, c_high, received = lax.optimization_barrier((c_low, c_high, received))
    late_perturb = lax.optimization_barrier((perturb, c_low, c_high))[0]
    p_low, p_high = halos(late_perturb, "tile", 2, radius)
    partial = forward_pick(
        control, c_low, c_high, perturb, band_lon, band_lat, received
    )
    partials = gather_over(partial, "mem")
    spread, low_send, high_send = spread_misfits(
        partials, received, lon_cells, lat_cells, radius, padded
    )
    count = lax.axis_size("tile")
    s_low = lax.ppermute(low_send, "tile", [(i, (i + 1) % count) for i in range(count)])
    s_high = lax.ppermute(high_send, "tile", [((i + 1) % count, i) for i in range(count)])
    return backward_grad(
        perturb,
        p_low,
        p_high,
        spread[None],
        s_low[None],
        s_high[None],
        control,
        band_lon,
        band_lat,
    )


def solution(mesh):
    return jax.shard_map(
        local,
        mesh=mesh,
        in_specs=(
            P("mem", None, "tile", None),
            P("mem", None, "tile", None),
            P(),
            P(),
            P("tile", None, None),
            P("tile", None, None),
            P("tile", None, None),
            P("tile", None),
        ),
        out_specs=P("mem", None, "tile", None),
        check_vma=False,
    )
```

```python
import math

import jax
import jax.numpy as jnp
from jax import lax
from jax.experimental import pallas as pl
from jax.experimental.pallas import tpu as pltpu
from jax.sharding import PartitionSpec as P


def halos(block, axis, dim, width):
    count = lax.axis_size(axis)
    forward = [(i, (i + 1) % count) for i in range(count)]
    backward = [((i + 1) % count, i) for i in range(count)]
    low = lax.ppermute(
        lax.slice_in_dim(block, block.shape[dim] - width, None, axis=dim), axis, forward
    )
    high = lax.ppermute(lax.slice_in_dim(block, 0, width, axis=dim), axis, backward)
    return low, high


def gather_over(values, axis):
    count = lax.axis_size(axis)
    return [values] + [
        lax.ppermute(values, axis, [(i, (i + shift) % count) for i in range(count)])
        for shift in range(1, count)
    ]


def select_chain(dist, taps_ref):
    band = jnp.zeros(dist.shape, jnp.float32)
    for offset in range(taps_ref.shape[0]):
        band = jnp.where(dist == offset, taps_ref[offset], band)
    return band.astype(jnp.bfloat16)


def build_bands(lon_taps, lat_taps, lon_cells, padded, lat_cells):
    radius = lon_taps.shape[0] - 1
    ext_cells = padded + 2 * radius
    tile = 128
    tiles = -(-lat_cells // tile)

    def kernel(lon_ref, lat_ref, blon_ref, blat_ref):
        rows = lax.broadcasted_iota(jnp.int32, (padded, ext_cells), 0)
        cols = lax.broadcasted_iota(jnp.int32, (padded, ext_cells), 1)
        source = jnp.where(
            cols < padded,
            cols,
            jnp.where(
                cols < padded + radius,
                cols - padded - radius,
                cols - padded - radius + lon_cells,
            ),
        )
        valid = (rows < lon_cells) & ((cols < lon_cells) | (cols >= padded))
        dist = jnp.where(valid, jnp.abs(source - rows), radius + 1)
        blon_ref[...] = select_chain(dist, lon_ref)

        t_rows = lax.broadcasted_iota(jnp.int32, (tile, tile), 0)
        t_cols = lax.broadcasted_iota(jnp.int32, (tile, tile), 1)
        blocks = {
            shift: select_chain(jnp.abs(t_rows - t_cols + shift * tile), lat_ref)
            for shift in (-1, 0, 1)
        }
        blat_ref[...] = jnp.zeros(blat_ref.shape, blat_ref.dtype)
        for a in range(tiles):
            for b in (a - 1, a, a + 1):
                if b < 0 or b >= tiles:
                    continue
                height = min(tile, lat_cells - a * tile)
                width = min(tile, lat_cells - b * tile)
                blat_ref[a * tile:a * tile + height, b * tile:b * tile + width] = blocks[a - b][
                    :height, :width
                ]

    smem = pl.BlockSpec(memory_space=pltpu.SMEM)
    return pl.pallas_call(
        kernel,
        in_specs=[smem, smem],
        out_shape=(
            jax.ShapeDtypeStruct((padded, ext_cells), jnp.bfloat16),
            jax.ShapeDtypeStruct((lat_cells, lat_cells), jnp.bfloat16),
        ),
    )(lon_taps.astype(jnp.float32), lat_taps.astype(jnp.float32))


def member_chunk(members):
    for size in (10, 8, 5, 4, 3, 2, 1):
        if members % size == 0:
            return size
    return 1


def lat_conv(along_ref, blat_ref, radius):
    lat_cells = blat_ref.shape[0]
    blocks = []
    for start in range(0, lat_cells, 256):
        stop = min(lat_cells, start + 256)
        low = max(0, (start - radius) // 128 * 128)
        high = min(lat_cells, -(-(stop + radius) // 128) * 128)
        blocks.append(
            jnp.dot(
                along_ref[:, low:high],
                blat_ref[low:high, start:stop],
                preferred_element_type=jnp.float32,
            )
        )
    return jnp.concatenate(blocks, axis=1) if len(blocks) > 1 else blocks[0]


def fill_ext(ext_ref, local, low, high, lon_cells, padded):
    radius = low.shape[0]
    base = (lon_cells // 16) * 16
    ext_ref[base:padded, :] = jnp.zeros((padded - base, ext_ref.shape[1]), ext_ref.dtype)
    ext_ref[0:lon_cells, :] = local
    ext_ref[padded:padded + radius, :] = low
    ext_ref[padded + radius:padded + 2 * radius, :] = high


def split3(values):
    hi = values.astype(jnp.bfloat16)
    rest = values - hi.astype(jnp.float32)
    mid = rest.astype(jnp.bfloat16)
    lo = (rest - mid.astype(jnp.float32)).astype(jnp.bfloat16)
    return hi, mid, lo


def cell_keys(cells, padded, lat_cells):
    rows = jnp.floor((cells + 0.5) / lat_cells)
    cols = (cells - rows * lat_cells).astype(jnp.int32)
    keys = (cols // 128) * padded + rows.astype(jnp.int32)
    lane_ids = lax.broadcasted_iota(jnp.int32, (128, cells.shape[1]), 0)
    onehot = jnp.where(lane_ids == cols % 128, 1.0, 0.0).astype(jnp.bfloat16)
    return keys, onehot


def forward_pick(control, c_low, c_high, perturb, band_lon, band_lat, cells):
    members, levels, lon_cells, lat_cells = control.shape
    radius = c_low.shape[2]
    padded, ext_cells = band_lon.shape
    chunk = member_chunk(members)
    steps = members // chunk
    _, sources, slots = cells.shape
    parts = -(-lat_cells // 128)

    def kernel(ctrl_ref, low_ref, high_ref, pert_ref, blon_ref, blat_ref, cells_ref, out_ref,
               ext_ref, along_ref, acc_ref, fold_ref):
        step = pl.program_id(0)
        blon = blon_ref[...]
        for m in range(chunk):
            fill_ext(ext_ref, ctrl_ref[m], low_ref[m], high_ref[m], lon_cells, padded)
            along = jnp.dot(blon, ext_ref[...], preferred_element_type=jnp.float32)
            along_ref[m * padded:(m + 1) * padded, :] = along.astype(jnp.bfloat16)
        smoothed = lat_conv(along_ref, blat_ref, radius)
        total = pert_ref[0].astype(jnp.float32) * smoothed[0:lon_cells]
        for m in range(1, chunk):
            total = total + pert_ref[m].astype(jnp.float32) * smoothed[
                m * padded:m * padded + lon_cells
            ]

        @pl.when(step == 0)
        def _():
            acc_ref[...] = jnp.zeros(acc_ref.shape, acc_ref.dtype)

        acc_ref[0:lon_cells, :] = acc_ref[0:lon_cells, :] + total

        @pl.when(step == steps - 1)
        def _():
            fold_ref[...] = jnp.zeros(fold_ref.shape, fold_ref.dtype)
            for part in range(parts):
                width = min(128, lat_cells - part * 128)
                fold_ref[part * padded:(part + 1) * padded, 0:width] = acc_ref[
                    :, part * 128:part * 128 + width
                ]
            pieces = split3(fold_ref[...])
            key_ids = lax.broadcasted_iota(jnp.int32, (parts * padded, slots), 0)
            for row in range(sources):
                keys, onehot = cell_keys(cells_ref[2, row:row + 1, :], padded, lat_cells)
                at_keys = jnp.dot(pieces[0], onehot, preferred_element_type=jnp.float32)
                at_keys = at_keys + jnp.dot(pieces[1], onehot, preferred_element_type=jnp.float32)
                at_keys = at_keys + jnp.dot(pieces[2], onehot, preferred_element_type=jnp.float32)
                out_ref[row:row + 1, :] = jnp.sum(
                    jnp.where(key_ids == keys, at_keys, 0.0), axis=0, keepdims=True
                )

    field = pl.BlockSpec((chunk, None, lon_cells, lat_cells), lambda g: (g, 0, 0, 0))
    halo = pl.BlockSpec((chunk, None, radius, lat_cells), lambda g: (g, 0, 0, 0))
    whole = lambda shape: pl.BlockSpec(shape, lambda g: (0,) * len(shape))
    return pl.pallas_call(
        kernel,
        grid=(steps,),
        in_specs=[
            field,
            halo,
            halo,
            field,
            whole(band_lon.shape),
            whole(band_lat.shape),
            whole(cells.shape),
        ],
        out_specs=whole((sources, slots)),
        out_shape=jax.ShapeDtypeStruct((sources, slots), jnp.float32),
        scratch_shapes=[
            pltpu.VMEM((ext_cells, lat_cells), jnp.bfloat16),
            pltpu.VMEM((chunk * padded, lat_cells), jnp.bfloat16),
            pltpu.VMEM((padded, lat_cells), jnp.float32),
            pltpu.VMEM((parts * padded, 128), jnp.float32),
        ],
        compiler_params=pltpu.CompilerParams(dimension_semantics=("arbitrary",)),
    )(control, c_low, c_high, perturb, band_lon, band_lat, cells)


def spread_misfits(partials, lists, lon_cells, lat_cells, radius, padded):
    _, sources, slots = lists.shape
    parts = -(-lat_cells // 128)

    def kernel(*refs):
        part_refs = refs[:len(partials)]
        lists_ref, spread_ref, low_ref, high_ref, fold_ref = refs[len(partials):]
        at_cells = part_refs[0][...]
        for ref in part_refs[1:]:
            at_cells = at_cells + ref[...]
        key_ids = lax.broadcasted_iota(jnp.int32, (parts * padded, slots), 0)
        folded = jnp.zeros((parts * padded, 128), jnp.float32)
        for row in range(sources):
            misfit = lists_ref[1, row:row + 1, :] * (
                at_cells[row:row + 1, :] - lists_ref[0, row:row + 1, :]
            )
            keys, _ = cell_keys(lists_ref[2, row:row + 1, :], padded, lat_cells)
            cells_col = jnp.transpose(
                jnp.broadcast_to(lists_ref[2, row:row + 1, :], (8, slots))
            )[:, 0:1]
            rows_col = jnp.floor((cells_col + 0.5) / lat_cells)
            lanes_col = (cells_col - rows_col * lat_cells).astype(jnp.int32) % 128
            lane_ids = lax.broadcasted_iota(jnp.int32, (slots, 128), 1)
            onehot_t = jnp.where(lane_ids == lanes_col, 1.0, 0.0).astype(jnp.bfloat16)
            weighted = jnp.concatenate(
                [
                    jnp.where(key_ids == keys, piece.astype(jnp.float32), 0.0).astype(
                        jnp.bfloat16
                    )
                    for piece in split3(misfit)
                ],
                axis=1,
            )
            stacked = jnp.concatenate([onehot_t, onehot_t, onehot_t], axis=0)
            folded = folded + jnp.dot(weighted, stacked, preferred_element_type=jnp.float32)
        for part in range(parts):
            width = min(128, lat_cells - part * 128)
            fold_ref[:, part * 128:part * 128 + width] = folded[
                part * padded:(part + 1) * padded, 0:width
            ]
        spread_ref[...] = fold_ref[0:lon_cells, :]
        low_ref[...] = fold_ref[lon_cells - radius:lon_cells, :]
        high_ref[...] = fold_ref[0:radius, :]

    return pl.pallas_call(
        kernel,
        out_shape=(
            jax.ShapeDtypeStruct((lon_cells, lat_cells), jnp.float32),
            jax.ShapeDtypeStruct((radius, lat_cells), jnp.float32),
            jax.ShapeDtypeStruct((radius, lat_cells), jnp.float32),
        ),
        scratch_shapes=[pltpu.VMEM((padded, lat_cells), jnp.float32)],
    )(*partials, lists)


def backward_grad(perturb, p_low, p_high, spread, s_low, s_high, control, band_lon, band_lat):
    members, levels, lon_cells, lat_cells = control.shape
    radius = p_low.shape[2]
    padded, ext_cells = band_lon.shape
    chunk = member_chunk(members)

    def kernel(pert_ref, plow_ref, phigh_ref, spread_ref, slow_ref, shigh_ref, ctrl_ref,
               blon_ref, blat_ref, out_ref, ext_ref, along_ref):
        blon = blon_ref[...]
        spread = spread_ref[...]
        s_lo = slow_ref[...]
        s_hi = shigh_ref[...]
        for m in range(chunk):
            fill_ext(
                ext_ref,
                (pert_ref[m].astype(jnp.float32) * spread).astype(jnp.bfloat16),
                (plow_ref[m].astype(jnp.float32) * s_lo).astype(jnp.bfloat16),
                (phigh_ref[m].astype(jnp.float32) * s_hi).astype(jnp.bfloat16),
                lon_cells,
                padded,
            )
            along = jnp.dot(blon, ext_ref[...], preferred_element_type=jnp.float32)
            along_ref[m * padded:(m + 1) * padded, :] = along.astype(jnp.bfloat16)
        smoothed = lat_conv(along_ref, blat_ref, radius)
        for m in range(chunk):
            out_ref[m] = ctrl_ref[m].astype(jnp.float32) + smoothed[
                m * padded:m * padded + lon_cells
            ]

    field = pl.BlockSpec((chunk, None, lon_cells, lat_cells), lambda l, g: (g, l, 0, 0))
    halo = pl.BlockSpec((chunk, None, radius, lat_cells), lambda l, g: (g, l, 0, 0))
    level_field = pl.BlockSpec((None, lon_cells, lat_cells), lambda l, g: (l, 0, 0))
    level_halo = pl.BlockSpec((None, radius, lat_cells), lambda l, g: (l, 0, 0))
    out = pl.pallas_call(
        kernel,
        grid=(levels, members // chunk),
        in_specs=[
            field,
            halo,
            halo,
            level_field,
            level_halo,
            level_halo,
            field,
            pl.BlockSpec(band_lon.shape, lambda l, g: (0, 0)),
            pl.BlockSpec(band_lat.shape, lambda l, g: (0, 0)),
        ],
        out_specs=pl.BlockSpec((chunk, lon_cells, None, lat_cells), lambda l, g: (g, 0, l, 0)),
        out_shape=jax.ShapeDtypeStruct((members, lon_cells, levels, lat_cells), jnp.float32),
        scratch_shapes=[
            pltpu.VMEM((ext_cells, lat_cells), jnp.bfloat16),
            pltpu.VMEM((chunk * padded, lat_cells), jnp.bfloat16),
        ],
        compiler_params=pltpu.CompilerParams(dimension_semantics=("arbitrary", "arbitrary")),
    )(perturb, p_low, p_high, spread, s_low, s_high, control, band_lon, band_lat)
    return jnp.transpose(out, (0, 2, 1, 3))


def local(control, perturb, lon_taps, lat_taps, innov, inv_var, cell_index, counts):
    members_here, levels, lon_cells, lat_cells = control.shape
    radius = lon_taps.shape[0] - 1
    padded = -(-lon_cells // 16) * 16
    band_lon, band_lat = build_bands(lon_taps, lat_taps, lon_cells, padded, lat_cells)

    slot_ids = lax.broadcasted_iota(jnp.int32, innov.shape, 2)
    weights = jnp.where(slot_ids < counts[:, :, None], inv_var, 0.0)
    lists = jnp.concatenate([innov, weights, cell_index.astype(jnp.float32)])
    lists = lax.optimization_barrier((lists, band_lon, band_lat))[0]
    received = lax.all_to_all(lists, "tile", split_axis=1, concat_axis=1, tiled=True)

    c_low, c_high = halos(control, "tile", 2, radius)
    c_low, c_high, received = lax.optimization_barrier((c_low, c_high, received))
    late_perturb = lax.optimization_barrier((perturb, c_low, c_high))[0]
    p_low, p_high = halos(late_perturb, "tile", 2, radius)
    partial = forward_pick(
        control, c_low, c_high, perturb, band_lon, band_lat, received
    )
    partials = gather_over(partial, "mem")
    spread, low_send, high_send = spread_misfits(
        partials, received, lon_cells, lat_cells, radius, padded
    )
    count = lax.axis_size("tile")
    s_low = lax.ppermute(low_send, "tile", [(i, (i + 1) % count) for i in range(count)])
    s_high = lax.ppermute(high_send, "tile", [((i + 1) % count, i) for i in range(count)])
    return backward_grad(
        perturb,
        p_low,
        p_high,
        spread[None],
        s_low[None],
        s_high[None],
        control,
        band_lon,
        band_lat,
    )


def solution(mesh):
    return jax.shard_map(
        local,
        mesh=mesh,
        in_specs=(
            P("mem", None, "tile", None),
            P("mem", None, "tile", None),
            P(),
            P(),
            P("tile", None, None),
            P("tile", None, None),
            P("tile", None, None),
            P("tile", None),
        ),
        out_specs=P("mem", None, "tile", None),
        check_vma=False,
    )
```

```python
import math

import jax
import jax.numpy as jnp
from jax import lax
from jax.experimental import pallas as pl
from jax.experimental.pallas import tpu as pltpu
from jax.sharding import PartitionSpec as P


def halos(block, axis, dim, width):
    count = lax.axis_size(axis)
    forward = [(i, (i + 1) % count) for i in range(count)]
    backward = [((i + 1) % count, i) for i in range(count)]
    low = lax.ppermute(
        lax.slice_in_dim(block, block.shape[dim] - width, None, axis=dim), axis, forward
    )
    high = lax.ppermute(lax.slice_in_dim(block, 0, width, axis=dim), axis, backward)
    return low, high


def gather_over(values, axis):
    count = lax.axis_size(axis)
    return [values] + [
        lax.ppermute(values, axis, [(i, (i + shift) % count) for i in range(count)])
        for shift in range(1, count)
    ]


def select_chain(dist, taps_ref):
    band = jnp.zeros(dist.shape, jnp.float32)
    for offset in range(taps_ref.shape[0]):
        band = jnp.where(dist == offset, taps_ref[offset], band)
    return band.astype(jnp.bfloat16)


def build_bands(lon_taps, lat_taps, lon_cells, padded, lat_cells):
    radius = lon_taps.shape[0] - 1
    ext_cells = padded + 2 * radius
    tile = 128
    tiles = -(-lat_cells // tile)

    def kernel(lon_ref, lat_ref, blon_ref, blat_ref):
        rows = lax.broadcasted_iota(jnp.int32, (padded, ext_cells), 0)
        cols = lax.broadcasted_iota(jnp.int32, (padded, ext_cells), 1)
        source = jnp.where(
            cols < padded,
            cols,
            jnp.where(
                cols < padded + radius,
                cols - padded - radius,
                cols - padded - radius + lon_cells,
            ),
        )
        valid = (rows < lon_cells) & ((cols < lon_cells) | (cols >= padded))
        dist = jnp.where(valid, jnp.abs(source - rows), radius + 1)
        blon_ref[...] = select_chain(dist, lon_ref)

        t_rows = lax.broadcasted_iota(jnp.int32, (tile, tile), 0)
        t_cols = lax.broadcasted_iota(jnp.int32, (tile, tile), 1)
        blocks = {
            shift: select_chain(jnp.abs(t_rows - t_cols + shift * tile), lat_ref)
            for shift in (-1, 0, 1)
        }
        blat_ref[...] = jnp.zeros(blat_ref.shape, blat_ref.dtype)
        for a in range(tiles):
            for b in (a - 1, a, a + 1):
                if b < 0 or b >= tiles:
                    continue
                height = min(tile, lat_cells - a * tile)
                width = min(tile, lat_cells - b * tile)
                blat_ref[a * tile:a * tile + height, b * tile:b * tile + width] = blocks[a - b][
                    :height, :width
                ]

    smem = pl.BlockSpec(memory_space=pltpu.SMEM)
    return pl.pallas_call(
        kernel,
        in_specs=[smem, smem],
        out_shape=(
            jax.ShapeDtypeStruct((padded, ext_cells), jnp.bfloat16),
            jax.ShapeDtypeStruct((lat_cells, lat_cells), jnp.bfloat16),
        ),
    )(lon_taps.astype(jnp.float32), lat_taps.astype(jnp.float32))


def member_chunk(members):
    for size in (10, 8, 5, 4, 3, 2, 1):
        if members % size == 0:
            return size
    return 1


def lat_conv(along_ref, blat_ref, radius):
    lat_cells = blat_ref.shape[0]
    blocks = []
    for start in range(0, lat_cells, 256):
        stop = min(lat_cells, start + 256)
        low = max(0, (start - radius) // 128 * 128)
        high = min(lat_cells, -(-(stop + radius) // 128) * 128)
        blocks.append(
            jnp.dot(
                along_ref[:, low:high],
                blat_ref[low:high, start:stop],
                preferred_element_type=jnp.float32,
            )
        )
    return jnp.concatenate(blocks, axis=1) if len(blocks) > 1 else blocks[0]


def fill_ext(ext_ref, local, low, high, lon_cells, padded):
    radius = low.shape[0]
    base = (lon_cells // 16) * 16
    ext_ref[base:padded, :] = jnp.zeros((padded - base, ext_ref.shape[1]), ext_ref.dtype)
    ext_ref[0:lon_cells, :] = local
    ext_ref[padded:padded + radius, :] = low
    ext_ref[padded + radius:padded + 2 * radius, :] = high


def split3(values):
    hi = values.astype(jnp.bfloat16)
    rest = values - hi.astype(jnp.float32)
    mid = rest.astype(jnp.bfloat16)
    lo = (rest - mid.astype(jnp.float32)).astype(jnp.bfloat16)
    return hi, mid, lo


def cell_keys(cells, padded, lat_cells):
    rows = jnp.floor((cells + 0.5) / lat_cells)
    cols = (cells - rows * lat_cells).astype(jnp.int32)
    keys = (cols // 128) * padded + rows.astype(jnp.int32)
    lane_ids = lax.broadcasted_iota(jnp.int32, (128, cells.shape[1]), 0)
    onehot = jnp.where(lane_ids == cols % 128, 1.0, 0.0).astype(jnp.bfloat16)
    return keys, onehot


def forward_pick(control, c_low, c_high, perturb, band_lon, band_lat, cells):
    members, levels, lon_cells, lat_cells = control.shape
    radius = c_low.shape[2]
    padded, ext_cells = band_lon.shape
    chunk = member_chunk(members)
    steps = members // chunk
    sources, _, slots = cells.shape
    parts = -(-lat_cells // 128)

    def kernel(ctrl_ref, low_ref, high_ref, pert_ref, blon_ref, blat_ref, cells_ref, out_ref,
               ext_ref, along_ref, acc_ref, fold_ref):
        step = pl.program_id(0)
        blon = blon_ref[...]
        for m in range(chunk):
            fill_ext(ext_ref, ctrl_ref[m], low_ref[m], high_ref[m], lon_cells, padded)
            along = jnp.dot(blon, ext_ref[...], preferred_element_type=jnp.float32)
            along_ref[m * padded:(m + 1) * padded, :] = along.astype(jnp.bfloat16)
        smoothed = lat_conv(along_ref, blat_ref, radius)
        total = pert_ref[0].astype(jnp.float32) * smoothed[0:lon_cells]
        for m in range(1, chunk):
            total = total + pert_ref[m].astype(jnp.float32) * smoothed[
                m * padded:m * padded + lon_cells
            ]

        @pl.when(step == 0)
        def _():
            acc_ref[...] = jnp.zeros(acc_ref.shape, acc_ref.dtype)

        acc_ref[0:lon_cells, :] = acc_ref[0:lon_cells, :] + total

        @pl.when(step == steps - 1)
        def _():
            fold_ref[...] = jnp.zeros(fold_ref.shape, fold_ref.dtype)
            for part in range(parts):
                width = min(128, lat_cells - part * 128)
                fold_ref[part * padded:(part + 1) * padded, 0:width] = acc_ref[
                    :, part * 128:part * 128 + width
                ]
            pieces = split3(fold_ref[...])
            key_ids = lax.broadcasted_iota(jnp.int32, (parts * padded, slots), 0)
            for row in range(sources):
                keys, onehot = cell_keys(cells_ref[row, 2:3, :], padded, lat_cells)
                at_keys = jnp.dot(pieces[0], onehot, preferred_element_type=jnp.float32)
                at_keys = at_keys + jnp.dot(pieces[1], onehot, preferred_element_type=jnp.float32)
                at_keys = at_keys + jnp.dot(pieces[2], onehot, preferred_element_type=jnp.float32)
                out_ref[row:row + 1, :] = jnp.sum(
                    jnp.where(key_ids == keys, at_keys, 0.0), axis=0, keepdims=True
                )

    field = pl.BlockSpec((chunk, None, lon_cells, lat_cells), lambda g: (g, 0, 0, 0))
    halo = pl.BlockSpec((chunk, None, radius, lat_cells), lambda g: (g, 0, 0, 0))
    whole = lambda shape: pl.BlockSpec(shape, lambda g: (0,) * len(shape))
    return pl.pallas_call(
        kernel,
        grid=(steps,),
        in_specs=[
            field,
            halo,
            halo,
            field,
            whole(band_lon.shape),
            whole(band_lat.shape),
            whole(cells.shape),
        ],
        out_specs=whole((sources, slots)),
        out_shape=jax.ShapeDtypeStruct((sources, slots), jnp.float32),
        scratch_shapes=[
            pltpu.VMEM((ext_cells, lat_cells), jnp.bfloat16),
            pltpu.VMEM((chunk * padded, lat_cells), jnp.bfloat16),
            pltpu.VMEM((padded, lat_cells), jnp.float32),
            pltpu.VMEM((parts * padded, 128), jnp.float32),
        ],
        compiler_params=pltpu.CompilerParams(dimension_semantics=("arbitrary",)),
    )(control, c_low, c_high, perturb, band_lon, band_lat, cells)


def spread_misfits(partials, lists, lon_cells, lat_cells, radius, padded):
    sources, _, slots = lists.shape
    parts = -(-lat_cells // 128)

    def kernel(*refs):
        part_refs = refs[:len(partials)]
        lists_ref, spread_ref, low_ref, high_ref, fold_ref = refs[len(partials):]
        at_cells = part_refs[0][...]
        for ref in part_refs[1:]:
            at_cells = at_cells + ref[...]
        key_ids = lax.broadcasted_iota(jnp.int32, (parts * padded, slots), 0)
        folded = jnp.zeros((parts * padded, 128), jnp.float32)
        for row in range(sources):
            misfit = lists_ref[row, 1:2, :] * (
                at_cells[row:row + 1, :] - lists_ref[row, 0:1, :]
            )
            keys, onehot = cell_keys(lists_ref[row, 2:3, :], padded, lat_cells)
            for piece in split3(misfit):
                weighted = jnp.where(key_ids == keys, piece.astype(jnp.float32), 0.0)
                folded = folded + lax.dot_general(
                    weighted.astype(jnp.bfloat16),
                    onehot,
                    (((1,), (1,)), ((), ())),
                    preferred_element_type=jnp.float32,
                )
        for part in range(parts):
            width = min(128, lat_cells - part * 128)
            fold_ref[:, part * 128:part * 128 + width] = folded[
                part * padded:(part + 1) * padded, 0:width
            ]
        spread_ref[...] = fold_ref[0:lon_cells, :]
        low_ref[...] = fold_ref[lon_cells - radius:lon_cells, :]
        high_ref[...] = fold_ref[0:radius, :]

    return pl.pallas_call(
        kernel,
        out_shape=(
            jax.ShapeDtypeStruct((lon_cells, lat_cells), jnp.float32),
            jax.ShapeDtypeStruct((radius, lat_cells), jnp.float32),
            jax.ShapeDtypeStruct((radius, lat_cells), jnp.float32),
        ),
        scratch_shapes=[pltpu.VMEM((padded, lat_cells), jnp.float32)],
    )(*partials, lists)


def backward_grad(perturb, p_low, p_high, spread, s_low, s_high, control, band_lon, band_lat):
    members, levels, lon_cells, lat_cells = control.shape
    radius = p_low.shape[2]
    padded, ext_cells = band_lon.shape
    chunk = member_chunk(members)

    def kernel(pert_ref, plow_ref, phigh_ref, spread_ref, slow_ref, shigh_ref, ctrl_ref,
               blon_ref, blat_ref, out_ref, ext_ref, along_ref):
        blon = blon_ref[...]
        spread = spread_ref[...]
        s_lo = slow_ref[...]
        s_hi = shigh_ref[...]
        for m in range(chunk):
            fill_ext(
                ext_ref,
                (pert_ref[m].astype(jnp.float32) * spread).astype(jnp.bfloat16),
                (plow_ref[m].astype(jnp.float32) * s_lo).astype(jnp.bfloat16),
                (phigh_ref[m].astype(jnp.float32) * s_hi).astype(jnp.bfloat16),
                lon_cells,
                padded,
            )
            along = jnp.dot(blon, ext_ref[...], preferred_element_type=jnp.float32)
            along_ref[m * padded:(m + 1) * padded, :] = along.astype(jnp.bfloat16)
        smoothed = lat_conv(along_ref, blat_ref, radius)
        for m in range(chunk):
            out_ref[m] = ctrl_ref[m].astype(jnp.float32) + smoothed[
                m * padded:m * padded + lon_cells
            ]

    field = pl.BlockSpec((chunk, None, lon_cells, lat_cells), lambda l, g: (g, l, 0, 0))
    halo = pl.BlockSpec((chunk, None, radius, lat_cells), lambda l, g: (g, l, 0, 0))
    level_field = pl.BlockSpec((None, lon_cells, lat_cells), lambda l, g: (l, 0, 0))
    level_halo = pl.BlockSpec((None, radius, lat_cells), lambda l, g: (l, 0, 0))
    out = pl.pallas_call(
        kernel,
        grid=(levels, members // chunk),
        in_specs=[
            field,
            halo,
            halo,
            level_field,
            level_halo,
            level_halo,
            field,
            pl.BlockSpec(band_lon.shape, lambda l, g: (0, 0)),
            pl.BlockSpec(band_lat.shape, lambda l, g: (0, 0)),
        ],
        out_specs=pl.BlockSpec((chunk, lon_cells, None, lat_cells), lambda l, g: (g, 0, l, 0)),
        out_shape=jax.ShapeDtypeStruct((members, lon_cells, levels, lat_cells), jnp.float32),
        scratch_shapes=[
            pltpu.VMEM((ext_cells, lat_cells), jnp.bfloat16),
            pltpu.VMEM((chunk * padded, lat_cells), jnp.bfloat16),
        ],
        compiler_params=pltpu.CompilerParams(dimension_semantics=("arbitrary", "arbitrary")),
    )(perturb, p_low, p_high, spread, s_low, s_high, control, band_lon, band_lat)
    return jnp.transpose(out, (0, 2, 1, 3))


def local(control, perturb, lon_taps, lat_taps, innov, inv_var, cell_index, counts):
    members_here, levels, lon_cells, lat_cells = control.shape
    radius = lon_taps.shape[0] - 1
    padded = -(-lon_cells // 16) * 16
    band_lon, band_lat = build_bands(lon_taps, lat_taps, lon_cells, padded, lat_cells)

    slot_ids = lax.broadcasted_iota(jnp.int32, innov.shape, 2)
    weights = jnp.where(slot_ids < counts[:, :, None], inv_var, 0.0)
    lists = jnp.stack([innov[0], weights[0], cell_index[0].astype(jnp.float32)], axis=1)
    lists = lax.optimization_barrier((lists, band_lon, band_lat))[0]
    received = lax.all_to_all(lists, "tile", split_axis=0, concat_axis=0, tiled=True)

    c_low, c_high = halos(control, "tile", 2, radius)
    c_low, c_high, received = lax.optimization_barrier((c_low, c_high, received))
    late_perturb = lax.optimization_barrier((perturb, c_low, c_high))[0]
    p_low, p_high = halos(late_perturb, "tile", 2, radius)
    partial = forward_pick(
        control, c_low, c_high, perturb, band_lon, band_lat, received
    )
    partials = gather_over(partial, "mem")
    spread, low_send, high_send = spread_misfits(
        partials, received, lon_cells, lat_cells, radius, padded
    )
    count = lax.axis_size("tile")
    s_low = lax.ppermute(low_send, "tile", [(i, (i + 1) % count) for i in range(count)])
    s_high = lax.ppermute(high_send, "tile", [((i + 1) % count, i) for i in range(count)])
    return backward_grad(
        perturb,
        p_low,
        p_high,
        spread[None],
        s_low[None],
        s_high[None],
        control,
        band_lon,
        band_lat,
    )


def solution(mesh):
    return jax.shard_map(
        local,
        mesh=mesh,
        in_specs=(
            P("mem", None, "tile", None),
            P("mem", None, "tile", None),
            P(),
            P(),
            P("tile", None, None),
            P("tile", None, None),
            P("tile", None, None),
            P("tile", None),
        ),
        out_specs=P("mem", None, "tile", None),
        check_vma=False,
    )
```

```python
import jax
import jax.numpy as jnp
from jax import lax
from jax.experimental import pallas as pl
from jax.experimental.pallas import tpu as pltpu
from jax.sharding import PartitionSpec as P


def halos(block, axis, dim, width):
    count = lax.axis_size(axis)
    forward = [(i, (i + 1) % count) for i in range(count)]
    backward = [((i + 1) % count, i) for i in range(count)]
    low = lax.ppermute(
        lax.slice_in_dim(block, block.shape[dim] - width, None, axis=dim), axis, forward
    )
    high = lax.ppermute(lax.slice_in_dim(block, 0, width, axis=dim), axis, backward)
    return low, high


def gather_over(values, axis):
    count = lax.axis_size(axis)
    return [values] + [
        lax.ppermute(values, axis, [(i, (i + shift) % count) for i in range(count)])
        for shift in range(1, count)
    ]


def select_chain(dist, taps_ref):
    band = jnp.zeros(dist.shape, jnp.float32)
    for offset in range(taps_ref.shape[0]):
        band = jnp.where(dist == offset, taps_ref[offset], band)
    return band.astype(jnp.bfloat16)


def build_bands(lon_taps, lat_taps, lon_cells, padded, lat_cells):
    radius = lon_taps.shape[0] - 1
    ext_cells = padded + 2 * radius
    tile = 128
    tiles = -(-lat_cells // tile)

    def kernel(lon_ref, lat_ref, blon_ref, blat_ref):
        rows = lax.broadcasted_iota(jnp.int32, (padded, ext_cells), 0)
        cols = lax.broadcasted_iota(jnp.int32, (padded, ext_cells), 1)
        source = jnp.where(
            cols < padded,
            cols,
            jnp.where(
                cols < padded + radius,
                cols - padded - radius,
                cols - padded - radius + lon_cells,
            ),
        )
        valid = (rows < lon_cells) & ((cols < lon_cells) | (cols >= padded))
        dist = jnp.where(valid, jnp.abs(source - rows), radius + 1)
        blon_ref[...] = select_chain(dist, lon_ref)

        t_rows = lax.broadcasted_iota(jnp.int32, (tile, tile), 0)
        t_cols = lax.broadcasted_iota(jnp.int32, (tile, tile), 1)
        blocks = {
            shift: select_chain(jnp.abs(t_rows - t_cols + shift * tile), lat_ref)
            for shift in (-1, 0, 1)
        }
        blat_ref[...] = jnp.zeros(blat_ref.shape, blat_ref.dtype)
        for a in range(tiles):
            for b in (a - 1, a, a + 1):
                if b < 0 or b >= tiles:
                    continue
                height = min(tile, lat_cells - a * tile)
                width = min(tile, lat_cells - b * tile)
                blat_ref[a * tile:a * tile + height, b * tile:b * tile + width] = blocks[a - b][
                    :height, :width
                ]

    smem = pl.BlockSpec(memory_space=pltpu.SMEM)
    return pl.pallas_call(
        kernel,
        in_specs=[smem, smem],
        out_shape=(
            jax.ShapeDtypeStruct((padded, ext_cells), jnp.bfloat16),
            jax.ShapeDtypeStruct((lat_cells, lat_cells), jnp.bfloat16),
        ),
    )(lon_taps.astype(jnp.float32), lat_taps.astype(jnp.float32))


def member_chunk(members):
    for size in (10, 8, 5, 4, 3, 2, 1):
        if members % size == 0:
            return size
    return 1


def lat_conv(along_ref, blat_ref, radius):
    lat_cells = blat_ref.shape[0]
    blocks = []
    for start in range(0, lat_cells, 256):
        stop = min(lat_cells, start + 256)
        low = max(0, (start - radius) // 128 * 128)
        high = min(lat_cells, -(-(stop + radius) // 128) * 128)
        blocks.append(
            jnp.dot(
                along_ref[:, low:high],
                blat_ref[low:high, start:stop],
                preferred_element_type=jnp.float32,
            )
        )
    return jnp.concatenate(blocks, axis=1) if len(blocks) > 1 else blocks[0]


def fill_ext(ext_ref, local, low, high, lon_cells, padded):
    radius = low.shape[0]
    base = (lon_cells // 16) * 16
    ext_ref[base:padded, :] = jnp.zeros((padded - base, ext_ref.shape[1]), ext_ref.dtype)
    ext_ref[0:lon_cells, :] = local
    ext_ref[padded:padded + radius, :] = low
    ext_ref[padded + radius:padded + 2 * radius, :] = high


def split3(values):
    hi = values.astype(jnp.bfloat16)
    rest = values - hi.astype(jnp.float32)
    mid = rest.astype(jnp.bfloat16)
    lo = (rest - mid.astype(jnp.float32)).astype(jnp.bfloat16)
    return hi, mid, lo


def cell_keys(cells, padded, lat_cells):
    rows = jnp.floor((cells + 0.5) / lat_cells)
    cols = (cells - rows * lat_cells).astype(jnp.int32)
    keys = (cols // 128) * padded + rows.astype(jnp.int32)
    lane_ids = lax.broadcasted_iota(jnp.int32, (128, cells.shape[1]), 0)
    onehot = jnp.where(lane_ids == cols % 128, 1.0, 0.0).astype(jnp.bfloat16)
    return keys, onehot


def forward_pick(control, c_low, c_high, perturb, band_lon, band_lat, cells):
    members, _, lon_cells, lat_cells = control.shape
    radius = c_low.shape[2]
    padded, ext_cells = band_lon.shape
    chunk = member_chunk(members)
    steps = members // chunk
    sources, _, slots = cells.shape
    parts = -(-lat_cells // 128)

    def kernel(ctrl_ref, low_ref, high_ref, pert_ref, blon_ref, blat_ref, cells_ref, out_ref,
               ext_ref, along_ref, acc_ref, fold_ref):
        step = pl.program_id(0)
        blon = blon_ref[...]
        for m in range(chunk):
            fill_ext(ext_ref, ctrl_ref[m], low_ref[m], high_ref[m], lon_cells, padded)
            along = jnp.dot(blon, ext_ref[...], preferred_element_type=jnp.float32)
            along_ref[m * padded:(m + 1) * padded, :] = along.astype(jnp.bfloat16)
        smoothed = lat_conv(along_ref, blat_ref, radius)
        total = pert_ref[0].astype(jnp.float32) * smoothed[0:lon_cells]
        for m in range(1, chunk):
            total = total + pert_ref[m].astype(jnp.float32) * smoothed[
                m * padded:m * padded + lon_cells
            ]

        @pl.when(step == 0)
        def _():
            acc_ref[...] = jnp.zeros(acc_ref.shape, acc_ref.dtype)

        acc_ref[0:lon_cells, :] = acc_ref[0:lon_cells, :] + total

        @pl.when(step == steps - 1)
        def _():
            fold_ref[...] = jnp.zeros(fold_ref.shape, fold_ref.dtype)
            for part in range(parts):
                width = min(128, lat_cells - part * 128)
                fold_ref[part * padded:(part + 1) * padded, 0:width] = acc_ref[
                    :, part * 128:part * 128 + width
                ]
            pieces = split3(fold_ref[...])
            key_ids = lax.broadcasted_iota(jnp.int32, (parts * padded, slots), 0)
            for row in range(sources):
                keys, onehot = cell_keys(cells_ref[row, 2:3, :], padded, lat_cells)
                at_keys = jnp.dot(pieces[0], onehot, preferred_element_type=jnp.float32)
                at_keys = at_keys + jnp.dot(pieces[1], onehot, preferred_element_type=jnp.float32)
                at_keys = at_keys + jnp.dot(pieces[2], onehot, preferred_element_type=jnp.float32)
                out_ref[row:row + 1, :] = jnp.sum(
                    jnp.where(key_ids == keys, at_keys, 0.0), axis=0, keepdims=True
                )

    field = pl.BlockSpec((chunk, None, lon_cells, lat_cells), lambda g: (g, 0, 0, 0))
    halo = pl.BlockSpec((chunk, None, radius, lat_cells), lambda g: (g, 0, 0, 0))
    whole = lambda shape: pl.BlockSpec(shape, lambda g: (0,) * len(shape))
    return pl.pallas_call(
        kernel,
        grid=(steps,),
        in_specs=[
            field,
            halo,
            halo,
            field,
            whole(band_lon.shape),
            whole(band_lat.shape),
            whole(cells.shape),
        ],
        out_specs=whole((sources, slots)),
        out_shape=jax.ShapeDtypeStruct((sources, slots), jnp.float32),
        scratch_shapes=[
            pltpu.VMEM((ext_cells, lat_cells), jnp.bfloat16),
            pltpu.VMEM((chunk * padded, lat_cells), jnp.bfloat16),
            pltpu.VMEM((padded, lat_cells), jnp.float32),
            pltpu.VMEM((parts * padded, 128), jnp.float32),
        ],
        compiler_params=pltpu.CompilerParams(dimension_semantics=("arbitrary",)),
    )(control, c_low, c_high, perturb, band_lon, band_lat, cells)


def spread_misfits(partials, lists, lon_cells, lat_cells, radius, padded):
    sources, _, slots = lists.shape
    parts = -(-lat_cells // 128)

    def kernel(*refs):
        part_refs = refs[:len(partials)]
        lists_ref, spread_ref, low_ref, high_ref, fold_ref = refs[len(partials):]
        at_cells = part_refs[0][...]
        for ref in part_refs[1:]:
            at_cells = at_cells + ref[...]
        key_ids = lax.broadcasted_iota(jnp.int32, (parts * padded, slots), 0)
        folded = jnp.zeros((parts * padded, 128), jnp.float32)
        for row in range(sources):
            misfit = lists_ref[row, 1:2, :] * (
                at_cells[row:row + 1, :] - lists_ref[row, 0:1, :]
            )
            keys, onehot = cell_keys(lists_ref[row, 2:3, :], padded, lat_cells)
            for piece in split3(misfit):
                weighted = jnp.where(key_ids == keys, piece.astype(jnp.float32), 0.0)
                folded = folded + lax.dot_general(
                    weighted.astype(jnp.bfloat16),
                    onehot,
                    (((1,), (1,)), ((), ())),
                    preferred_element_type=jnp.float32,
                )
        for part in range(parts):
            width = min(128, lat_cells - part * 128)
            fold_ref[:, part * 128:part * 128 + width] = folded[
                part * padded:(part + 1) * padded, 0:width
            ]
        spread_ref[...] = fold_ref[0:lon_cells, :]
        low_ref[...] = fold_ref[lon_cells - radius:lon_cells, :]
        high_ref[...] = fold_ref[0:radius, :]

    return pl.pallas_call(
        kernel,
        out_shape=(
            jax.ShapeDtypeStruct((lon_cells, lat_cells), jnp.float32),
            jax.ShapeDtypeStruct((radius, lat_cells), jnp.float32),
            jax.ShapeDtypeStruct((radius, lat_cells), jnp.float32),
        ),
        scratch_shapes=[pltpu.VMEM((padded, lat_cells), jnp.float32)],
    )(*partials, lists)


def backward_grad(perturb, p_low, p_high, spread, s_low, s_high, control, band_lon, band_lat):
    members, levels, lon_cells, lat_cells = control.shape
    radius = p_low.shape[2]
    padded, ext_cells = band_lon.shape
    chunk = member_chunk(members)

    def kernel(pert_ref, plow_ref, phigh_ref, spread_ref, slow_ref, shigh_ref, ctrl_ref,
               blon_ref, blat_ref, out_ref, ext_ref, along_ref):
        blon = blon_ref[...]
        spread = spread_ref[...]
        s_lo = slow_ref[...]
        s_hi = shigh_ref[...]
        for m in range(chunk):
            fill_ext(
                ext_ref,
                (pert_ref[m].astype(jnp.float32) * spread).astype(jnp.bfloat16),
                (plow_ref[m].astype(jnp.float32) * s_lo).astype(jnp.bfloat16),
                (phigh_ref[m].astype(jnp.float32) * s_hi).astype(jnp.bfloat16),
                lon_cells,
                padded,
            )
            along = jnp.dot(blon, ext_ref[...], preferred_element_type=jnp.float32)
            along_ref[m * padded:(m + 1) * padded, :] = along.astype(jnp.bfloat16)
        smoothed = lat_conv(along_ref, blat_ref, radius)
        for m in range(chunk):
            out_ref[m] = ctrl_ref[m].astype(jnp.float32) + smoothed[
                m * padded:m * padded + lon_cells
            ]

    field = pl.BlockSpec((chunk, None, lon_cells, lat_cells), lambda l, g: (g, l, 0, 0))
    halo = pl.BlockSpec((chunk, None, radius, lat_cells), lambda l, g: (g, l, 0, 0))
    level_field = pl.BlockSpec((None, lon_cells, lat_cells), lambda l, g: (l, 0, 0))
    level_halo = pl.BlockSpec((None, radius, lat_cells), lambda l, g: (l, 0, 0))
    out = pl.pallas_call(
        kernel,
        grid=(levels, members // chunk),
        in_specs=[
            field,
            halo,
            halo,
            level_field,
            level_halo,
            level_halo,
            field,
            pl.BlockSpec(band_lon.shape, lambda l, g: (0, 0)),
            pl.BlockSpec(band_lat.shape, lambda l, g: (0, 0)),
        ],
        out_specs=pl.BlockSpec((chunk, lon_cells, None, lat_cells), lambda l, g: (g, 0, l, 0)),
        out_shape=jax.ShapeDtypeStruct((members, lon_cells, levels, lat_cells), jnp.float32),
        scratch_shapes=[
            pltpu.VMEM((ext_cells, lat_cells), jnp.bfloat16),
            pltpu.VMEM((chunk * padded, lat_cells), jnp.bfloat16),
        ],
        compiler_params=pltpu.CompilerParams(dimension_semantics=("arbitrary", "arbitrary")),
    )(perturb, p_low, p_high, spread, s_low, s_high, control, band_lon, band_lat)
    return jnp.transpose(out, (0, 2, 1, 3))


def local_body(control, perturb, lon_taps, lat_taps, innov, inv_var, cell_index, counts):
    _, _, lon_cells, lat_cells = control.shape
    radius = lon_taps.shape[0] - 1
    padded = -(-lon_cells // 16) * 16
    band_lon, band_lat = build_bands(lon_taps, lat_taps, lon_cells, padded, lat_cells)

    slot_ids = lax.broadcasted_iota(jnp.int32, innov.shape, 2)
    weights = jnp.where(slot_ids < counts[:, :, None], inv_var, 0.0)
    lists = jnp.stack([innov[0], weights[0], cell_index[0].astype(jnp.float32)], axis=1)
    lists = lax.optimization_barrier((lists, band_lon, band_lat))[0]
    received = lax.all_to_all(lists, "tile", split_axis=0, concat_axis=0, tiled=True)

    c_low, c_high = halos(control, "tile", 2, radius)
    c_low, c_high, received = lax.optimization_barrier((c_low, c_high, received))
    partial = forward_pick(
        control, c_low, c_high, perturb, band_lon, band_lat, received
    )
    partials = gather_over(partial, "mem")
    late_perturb = lax.optimization_barrier((perturb, partial))[0]
    p_low, p_high = halos(late_perturb, "tile", 2, radius)
    spread, low_send, high_send = spread_misfits(
        partials, received, lon_cells, lat_cells, radius, padded
    )
    count = lax.axis_size("tile")
    s_low = lax.ppermute(low_send, "tile", [(i, (i + 1) % count) for i in range(count)])
    s_high = lax.ppermute(high_send, "tile", [((i + 1) % count, i) for i in range(count)])
    return backward_grad(
        perturb,
        p_low,
        p_high,
        spread[None],
        s_low[None],
        s_high[None],
        control,
        band_lon,
        band_lat,
    )


def solution(mesh):
    return jax.shard_map(
        local_body,
        mesh=mesh,
        in_specs=(
            P("mem", None, "tile", None),
            P("mem", None, "tile", None),
            P(),
            P(),
            P("tile", None, None),
            P("tile", None, None),
            P("tile", None, None),
            P("tile", None),
        ),
        out_specs=P("mem", None, "tile", None),
        check_vma=False,
    )
```

```python
import math

import jax
import jax.numpy as jnp
from jax import lax
from jax.experimental import pallas as pl
from jax.experimental.pallas import tpu as pltpu
from jax.sharding import PartitionSpec as P


def halos(block, axis, dim, width):
    count = lax.axis_size(axis)
    forward = [(i, (i + 1) % count) for i in range(count)]
    backward = [((i + 1) % count, i) for i in range(count)]
    low = lax.ppermute(
        lax.slice_in_dim(block, block.shape[dim] - width, None, axis=dim), axis, forward
    )
    high = lax.ppermute(lax.slice_in_dim(block, 0, width, axis=dim), axis, backward)
    return low, high


def gather_over(values, axis):
    count = lax.axis_size(axis)
    return [values] + [
        lax.ppermute(values, axis, [(i, (i + shift) % count) for i in range(count)])
        for shift in range(1, count)
    ]


def select_chain(dist, taps_ref):
    band = jnp.zeros(dist.shape, jnp.float32)
    for offset in range(taps_ref.shape[0]):
        band = jnp.where(dist == offset, taps_ref[offset], band)
    return band.astype(jnp.bfloat16)


def build_bands(lon_taps, lat_taps, lon_cells, padded, lat_cells):
    radius = lon_taps.shape[0] - 1
    ext_cells = padded + 2 * radius
    tile = 128
    tiles = -(-lat_cells // tile)

    def kernel(lon_ref, lat_ref, blon_ref, blat_ref):
        rows = lax.broadcasted_iota(jnp.int32, (padded, ext_cells), 0)
        cols = lax.broadcasted_iota(jnp.int32, (padded, ext_cells), 1)
        source = jnp.where(
            cols < padded,
            cols,
            jnp.where(
                cols < padded + radius,
                cols - padded - radius,
                cols - padded - radius + lon_cells,
            ),
        )
        valid = (rows < lon_cells) & ((cols < lon_cells) | (cols >= padded))
        dist = jnp.where(valid, jnp.abs(source - rows), radius + 1)
        blon_ref[...] = select_chain(dist, lon_ref)

        t_rows = lax.broadcasted_iota(jnp.int32, (tile, tile), 0)
        t_cols = lax.broadcasted_iota(jnp.int32, (tile, tile), 1)
        blocks = {
            shift: select_chain(jnp.abs(t_rows - t_cols + shift * tile), lat_ref)
            for shift in (-1, 0, 1)
        }
        blat_ref[...] = jnp.zeros(blat_ref.shape, blat_ref.dtype)
        for a in range(tiles):
            for b in (a - 1, a, a + 1):
                if b < 0 or b >= tiles:
                    continue
                height = min(tile, lat_cells - a * tile)
                width = min(tile, lat_cells - b * tile)
                blat_ref[a * tile:a * tile + height, b * tile:b * tile + width] = blocks[a - b][
                    :height, :width
                ]

    smem = pl.BlockSpec(memory_space=pltpu.SMEM)
    return pl.pallas_call(
        kernel,
        in_specs=[smem, smem],
        out_shape=(
            jax.ShapeDtypeStruct((padded, ext_cells), jnp.bfloat16),
            jax.ShapeDtypeStruct((lat_cells, lat_cells), jnp.bfloat16),
        ),
    )(lon_taps.astype(jnp.float32), lat_taps.astype(jnp.float32))


def member_chunk(members):
    for size in (10, 8, 5, 4, 3, 2, 1):
        if members % size == 0:
            return size
    return 1


def lat_conv(along_ref, blat_ref, radius):
    lat_cells = blat_ref.shape[0]
    blocks = []
    for start in range(0, lat_cells, 256):
        stop = min(lat_cells, start + 256)
        low = max(0, (start - radius) // 128 * 128)
        high = min(lat_cells, -(-(stop + radius) // 128) * 128)
        blocks.append(
            jnp.dot(
                along_ref[:, low:high],
                blat_ref[low:high, start:stop],
                preferred_element_type=jnp.float32,
            )
        )
    return jnp.concatenate(blocks, axis=1) if len(blocks) > 1 else blocks[0]


def fill_ext(ext_ref, local, low, high, lon_cells, padded):
    radius = low.shape[0]
    base = (lon_cells // 16) * 16
    ext_ref[base:padded, :] = jnp.zeros((padded - base, ext_ref.shape[1]), ext_ref.dtype)
    ext_ref[0:lon_cells, :] = local
    ext_ref[padded:padded + radius, :] = low
    ext_ref[padded + radius:padded + 2 * radius, :] = high


def split3(values):
    hi = values.astype(jnp.bfloat16)
    rest = values - hi.astype(jnp.float32)
    mid = rest.astype(jnp.bfloat16)
    lo = (rest - mid.astype(jnp.float32)).astype(jnp.bfloat16)
    return hi, mid, lo


def cell_keys(cells, padded, lat_cells):
    rows = jnp.floor((cells + 0.5) / lat_cells)
    cols = (cells - rows * lat_cells).astype(jnp.int32)
    keys = (cols // 128) * padded + rows.astype(jnp.int32)
    lane_ids = lax.broadcasted_iota(jnp.int32, (128, cells.shape[1]), 0)
    onehot = jnp.where(lane_ids == cols % 128, 1.0, 0.0).astype(jnp.bfloat16)
    return keys, onehot


def forward_pick(control, c_low, c_high, perturb, band_lon, band_lat, cells):
    members, levels, lon_cells, lat_cells = control.shape
    radius = c_low.shape[2]
    padded, ext_cells = band_lon.shape
    chunk = member_chunk(members)
    steps = members // chunk
    sources, _, slots = cells.shape
    parts = -(-lat_cells // 128)

    def kernel(ctrl_ref, low_ref, high_ref, pert_ref, blon_ref, blat_ref, cells_ref, out_ref,
               ext_ref, along_ref, acc_ref, fold_ref):
        step = pl.program_id(0)
        blon = blon_ref[...]
        for m in range(chunk):
            fill_ext(ext_ref, ctrl_ref[m], low_ref[m], high_ref[m], lon_cells, padded)
            along = jnp.dot(blon, ext_ref[...], preferred_element_type=jnp.float32)
            along_ref[m * padded:(m + 1) * padded, :] = along.astype(jnp.bfloat16)
        smoothed = lat_conv(along_ref, blat_ref, radius)
        total = pert_ref[0].astype(jnp.float32) * smoothed[0:lon_cells]
        for m in range(1, chunk):
            total = total + pert_ref[m].astype(jnp.float32) * smoothed[
                m * padded:m * padded + lon_cells
            ]

        @pl.when(step == 0)
        def _():
            acc_ref[...] = jnp.zeros(acc_ref.shape, acc_ref.dtype)

        acc_ref[0:lon_cells, :] = acc_ref[0:lon_cells, :] + total

        @pl.when(step == steps - 1)
        def _():
            fold_ref[...] = jnp.zeros(fold_ref.shape, fold_ref.dtype)
            for part in range(parts):
                width = min(128, lat_cells - part * 128)
                fold_ref[part * padded:(part + 1) * padded, 0:width] = acc_ref[
                    :, part * 128:part * 128 + width
                ]
            pieces = jnp.concatenate(split3(fold_ref[...]), axis=1)
            key_ids = lax.broadcasted_iota(jnp.int32, (parts * padded, slots), 0)
            for row in range(sources):
                keys, onehot = cell_keys(cells_ref[row, 2:3, :], padded, lat_cells)
                at_keys = jnp.dot(
                    pieces,
                    jnp.concatenate([onehot, onehot, onehot], axis=0),
                    preferred_element_type=jnp.float32,
                )
                out_ref[row:row + 1, :] = jnp.sum(
                    jnp.where(key_ids == keys, at_keys, 0.0), axis=0, keepdims=True
                )

    field = pl.BlockSpec((chunk, None, lon_cells, lat_cells), lambda g: (g, 0, 0, 0))
    halo = pl.BlockSpec((chunk, None, radius, lat_cells), lambda g: (g, 0, 0, 0))
    whole = lambda shape: pl.BlockSpec(shape, lambda g: (0,) * len(shape))
    return pl.pallas_call(
        kernel,
        grid=(steps,),
        in_specs=[
            field,
            halo,
            halo,
            field,
            whole(band_lon.shape),
            whole(band_lat.shape),
            whole(cells.shape),
        ],
        out_specs=whole((sources, slots)),
        out_shape=jax.ShapeDtypeStruct((sources, slots), jnp.float32),
        scratch_shapes=[
            pltpu.VMEM((ext_cells, lat_cells), jnp.bfloat16),
            pltpu.VMEM((chunk * padded, lat_cells), jnp.bfloat16),
            pltpu.VMEM((padded, lat_cells), jnp.float32),
            pltpu.VMEM((parts * padded, 128), jnp.float32),
        ],
        compiler_params=pltpu.CompilerParams(dimension_semantics=("arbitrary",)),
    )(control, c_low, c_high, perturb, band_lon, band_lat, cells)


def spread_misfits(partials, lists, lon_cells, lat_cells, radius, padded):
    sources, _, slots = lists.shape
    parts = -(-lat_cells // 128)

    def kernel(*refs):
        part_refs = refs[:len(partials)]
        lists_ref, spread_ref, low_ref, high_ref, fold_ref = refs[len(partials):]
        at_cells = part_refs[0][...]
        for ref in part_refs[1:]:
            at_cells = at_cells + ref[...]
        key_ids = lax.broadcasted_iota(jnp.int32, (parts * padded, slots), 0)
        folded = jnp.zeros((parts * padded, 128), jnp.float32)
        for row in range(sources):
            misfit = lists_ref[row, 1:2, :] * (
                at_cells[row:row + 1, :] - lists_ref[row, 0:1, :]
            )
            keys, onehot = cell_keys(lists_ref[row, 2:3, :], padded, lat_cells)
            hits = key_ids == keys
            weighted = jnp.concatenate(
                [
                    jnp.where(hits, piece.astype(jnp.float32), 0.0).astype(jnp.bfloat16)
                    for piece in split3(misfit)
                ],
                axis=0,
            )
            summed = lax.dot_general(
                weighted, onehot, (((1,), (1,)), ((), ())), preferred_element_type=jnp.float32
            )
            rows_here = parts * padded
            folded = folded + (
                summed[0:rows_here] + summed[rows_here:2 * rows_here]
            ) + summed[2 * rows_here:3 * rows_here]
        for part in range(parts):
            width = min(128, lat_cells - part * 128)
            fold_ref[:, part * 128:part * 128 + width] = folded[
                part * padded:(part + 1) * padded, 0:width
            ]
        spread_ref[...] = fold_ref[0:lon_cells, :]
        low_ref[...] = fold_ref[lon_cells - radius:lon_cells, :]
        high_ref[...] = fold_ref[0:radius, :]

    return pl.pallas_call(
        kernel,
        out_shape=(
            jax.ShapeDtypeStruct((lon_cells, lat_cells), jnp.float32),
            jax.ShapeDtypeStruct((radius, lat_cells), jnp.float32),
            jax.ShapeDtypeStruct((radius, lat_cells), jnp.float32),
        ),
        scratch_shapes=[pltpu.VMEM((padded, lat_cells), jnp.float32)],
    )(*partials, lists)


def backward_grad(perturb, p_low, p_high, spread, s_low, s_high, control, band_lon, band_lat):
    members, levels, lon_cells, lat_cells = control.shape
    radius = p_low.shape[2]
    padded, ext_cells = band_lon.shape
    chunk = member_chunk(members)

    def kernel(pert_ref, plow_ref, phigh_ref, spread_ref, slow_ref, shigh_ref, ctrl_ref,
               blon_ref, blat_ref, out_ref, ext_ref, along_ref):
        blon = blon_ref[...]
        spread = spread_ref[...]
        s_lo = slow_ref[...]
        s_hi = shigh_ref[...]
        for m in range(chunk):
            fill_ext(
                ext_ref,
                (pert_ref[m].astype(jnp.float32) * spread).astype(jnp.bfloat16),
                (plow_ref[m].astype(jnp.float32) * s_lo).astype(jnp.bfloat16),
                (phigh_ref[m].astype(jnp.float32) * s_hi).astype(jnp.bfloat16),
                lon_cells,
                padded,
            )
            along = jnp.dot(blon, ext_ref[...], preferred_element_type=jnp.float32)
            along_ref[m * padded:(m + 1) * padded, :] = along.astype(jnp.bfloat16)
        smoothed = lat_conv(along_ref, blat_ref, radius)
        for m in range(chunk):
            out_ref[m] = ctrl_ref[m].astype(jnp.float32) + smoothed[
                m * padded:m * padded + lon_cells
            ]

    field = pl.BlockSpec((chunk, None, lon_cells, lat_cells), lambda l, g: (g, l, 0, 0))
    halo = pl.BlockSpec((chunk, None, radius, lat_cells), lambda l, g: (g, l, 0, 0))
    level_field = pl.BlockSpec((None, lon_cells, lat_cells), lambda l, g: (l, 0, 0))
    level_halo = pl.BlockSpec((None, radius, lat_cells), lambda l, g: (l, 0, 0))
    out = pl.pallas_call(
        kernel,
        grid=(levels, members // chunk),
        in_specs=[
            field,
            halo,
            halo,
            level_field,
            level_halo,
            level_halo,
            field,
            pl.BlockSpec(band_lon.shape, lambda l, g: (0, 0)),
            pl.BlockSpec(band_lat.shape, lambda l, g: (0, 0)),
        ],
        out_specs=pl.BlockSpec((chunk, lon_cells, None, lat_cells), lambda l, g: (g, 0, l, 0)),
        out_shape=jax.ShapeDtypeStruct((members, lon_cells, levels, lat_cells), jnp.float32),
        scratch_shapes=[
            pltpu.VMEM((ext_cells, lat_cells), jnp.bfloat16),
            pltpu.VMEM((chunk * padded, lat_cells), jnp.bfloat16),
        ],
        compiler_params=pltpu.CompilerParams(dimension_semantics=("arbitrary", "arbitrary")),
    )(perturb, p_low, p_high, spread, s_low, s_high, control, band_lon, band_lat)
    return jnp.transpose(out, (0, 2, 1, 3))


def local(control, perturb, lon_taps, lat_taps, innov, inv_var, cell_index, counts):
    members_here, levels, lon_cells, lat_cells = control.shape
    radius = lon_taps.shape[0] - 1
    padded = -(-lon_cells // 16) * 16
    band_lon, band_lat = build_bands(lon_taps, lat_taps, lon_cells, padded, lat_cells)

    slot_ids = lax.broadcasted_iota(jnp.int32, innov.shape, 2)
    weights = jnp.where(slot_ids < counts[:, :, None], inv_var, 0.0)
    lists = jnp.stack([innov[0], weights[0], cell_index[0].astype(jnp.float32)], axis=1)
    lists = lax.optimization_barrier((lists, band_lon, band_lat))[0]
    received = lax.all_to_all(lists, "tile", split_axis=0, concat_axis=0, tiled=True)

    c_low, c_high = halos(control, "tile", 2, radius)
    c_low, c_high, received = lax.optimization_barrier((c_low, c_high, received))
    late_perturb = lax.optimization_barrier((perturb, c_low, c_high))[0]
    p_low, p_high = halos(late_perturb, "tile", 2, radius)
    partial = forward_pick(
        control, c_low, c_high, perturb, band_lon, band_lat, received
    )
    partials = gather_over(partial, "mem")
    spread, low_send, high_send = spread_misfits(
        partials, received, lon_cells, lat_cells, radius, padded
    )
    count = lax.axis_size("tile")
    s_low = lax.ppermute(low_send, "tile", [(i, (i + 1) % count) for i in range(count)])
    s_high = lax.ppermute(high_send, "tile", [((i + 1) % count, i) for i in range(count)])
    return backward_grad(
        perturb,
        p_low,
        p_high,
        spread[None],
        s_low[None],
        s_high[None],
        control,
        band_lon,
        band_lat,
    )


def solution(mesh):
    return jax.shard_map(
        local,
        mesh=mesh,
        in_specs=(
            P("mem", None, "tile", None),
            P("mem", None, "tile", None),
            P(),
            P(),
            P("tile", None, None),
            P("tile", None, None),
            P("tile", None, None),
            P("tile", None),
        ),
        out_specs=P("mem", None, "tile", None),
        check_vma=False,
    )
```

```python
import math

import jax
import jax.numpy as jnp
from jax import lax
from jax.experimental import pallas as pl
from jax.experimental.pallas import tpu as pltpu
from jax.sharding import PartitionSpec as P


def halos(block, axis, dim, width):
    count = lax.axis_size(axis)
    forward = [(i, (i + 1) % count) for i in range(count)]
    backward = [((i + 1) % count, i) for i in range(count)]
    low = lax.ppermute(
        lax.slice_in_dim(block, block.shape[dim] - width, None, axis=dim), axis, forward
    )
    high = lax.ppermute(lax.slice_in_dim(block, 0, width, axis=dim), axis, backward)
    return low, high


def gather_over(values, axis):
    count = lax.axis_size(axis)
    return [values] + [
        lax.ppermute(values, axis, [(i, (i + shift) % count) for i in range(count)])
        for shift in range(1, count)
    ]


def select_chain(dist, taps_ref):
    band = jnp.zeros(dist.shape, jnp.float32)
    for offset in range(taps_ref.shape[0]):
        band = jnp.where(dist == offset, taps_ref[offset], band)
    return band.astype(jnp.bfloat16)


def build_bands(lon_taps, lat_taps, lon_cells, padded, lat_cells):
    radius = lon_taps.shape[0] - 1
    ext_cells = padded + 2 * radius
    tile = 128
    tiles = -(-lat_cells // tile)

    def kernel(lon_ref, lat_ref, blon_ref, blat_ref):
        rows = lax.broadcasted_iota(jnp.int32, (padded, ext_cells), 0)
        cols = lax.broadcasted_iota(jnp.int32, (padded, ext_cells), 1)
        source = jnp.where(
            cols < padded,
            cols,
            jnp.where(
                cols < padded + radius,
                cols - padded - radius,
                cols - padded - radius + lon_cells,
            ),
        )
        valid = (rows < lon_cells) & ((cols < lon_cells) | (cols >= padded))
        dist = jnp.where(valid, jnp.abs(source - rows), radius + 1)
        blon_ref[...] = select_chain(dist, lon_ref)

        t_rows = lax.broadcasted_iota(jnp.int32, (tile, tile), 0)
        t_cols = lax.broadcasted_iota(jnp.int32, (tile, tile), 1)
        blocks = {
            shift: select_chain(jnp.abs(t_rows - t_cols + shift * tile), lat_ref)
            for shift in (-1, 0, 1)
        }
        blat_ref[...] = jnp.zeros(blat_ref.shape, blat_ref.dtype)
        for a in range(tiles):
            for b in (a - 1, a, a + 1):
                if b < 0 or b >= tiles:
                    continue
                height = min(tile, lat_cells - a * tile)
                width = min(tile, lat_cells - b * tile)
                blat_ref[a * tile:a * tile + height, b * tile:b * tile + width] = blocks[a - b][
                    :height, :width
                ]

    smem = pl.BlockSpec(memory_space=pltpu.SMEM)
    return pl.pallas_call(
        kernel,
        in_specs=[smem, smem],
        out_shape=(
            jax.ShapeDtypeStruct((padded, ext_cells), jnp.bfloat16),
            jax.ShapeDtypeStruct((lat_cells, lat_cells), jnp.bfloat16),
        ),
    )(lon_taps.astype(jnp.float32), lat_taps.astype(jnp.float32))


def member_chunk(members):
    for size in (10, 8, 5, 4, 3, 2, 1):
        if members % size == 0:
            return size
    return 1


def lat_conv(along_ref, blat_ref, radius):
    lat_cells = blat_ref.shape[0]
    blocks = []
    for start in range(0, lat_cells, 256):
        stop = min(lat_cells, start + 256)
        low = max(0, (start - radius) // 128 * 128)
        high = min(lat_cells, -(-(stop + radius) // 128) * 128)
        blocks.append(
            jnp.dot(
                along_ref[:, low:high],
                blat_ref[low:high, start:stop],
                preferred_element_type=jnp.float32,
            )
        )
    return jnp.concatenate(blocks, axis=1) if len(blocks) > 1 else blocks[0]


def fill_ext(ext_ref, local, low, high, lon_cells, padded):
    radius = low.shape[0]
    base = (lon_cells // 16) * 16
    ext_ref[base:padded, :] = jnp.zeros((padded - base, ext_ref.shape[1]), ext_ref.dtype)
    ext_ref[0:lon_cells, :] = local
    ext_ref[padded:padded + radius, :] = low
    ext_ref[padded + radius:padded + 2 * radius, :] = high


def split3(values):
    hi = values.astype(jnp.bfloat16)
    rest = values - hi.astype(jnp.float32)
    mid = rest.astype(jnp.bfloat16)
    lo = (rest - mid.astype(jnp.float32)).astype(jnp.bfloat16)
    return hi, mid, lo


def cell_keys(cells, padded, lat_cells):
    rows = jnp.floor((cells + 0.5) / lat_cells)
    cols = (cells - rows * lat_cells).astype(jnp.int32)
    keys = (cols // 128) * padded + rows.astype(jnp.int32)
    lane_ids = lax.broadcasted_iota(jnp.int32, (128, cells.shape[1]), 0)
    onehot = jnp.where(lane_ids == cols % 128, 1.0, 0.0).astype(jnp.bfloat16)
    return keys, onehot


def forward_pick(control, c_low, c_high, perturb, band_lon, band_lat, cells):
    members, levels, lon_cells, lat_cells = control.shape
    radius = c_low.shape[2]
    padded, ext_cells = band_lon.shape
    chunk = member_chunk(members)
    steps = members // chunk
    sources, _, slots = cells.shape
    parts = -(-lat_cells // 128)

    def kernel(ctrl_ref, low_ref, high_ref, pert_ref, blon_ref, blat_ref, cells_ref, out_ref,
               ext_ref, along_ref, acc_ref, fold_ref):
        step = pl.program_id(0)
        blon = blon_ref[...]
        for m in range(chunk):
            fill_ext(ext_ref, ctrl_ref[m], low_ref[m], high_ref[m], lon_cells, padded)
            along = jnp.dot(blon, ext_ref[...], preferred_element_type=jnp.float32)
            along_ref[m * padded:(m + 1) * padded, :] = along.astype(jnp.bfloat16)
        smoothed = lat_conv(along_ref, blat_ref, radius)
        total = pert_ref[0].astype(jnp.float32) * smoothed[0:lon_cells]
        for m in range(1, chunk):
            total = total + pert_ref[m].astype(jnp.float32) * smoothed[
                m * padded:m * padded + lon_cells
            ]

        @pl.when(step == 0)
        def _():
            acc_ref[...] = jnp.zeros(acc_ref.shape, acc_ref.dtype)

        acc_ref[0:lon_cells, :] = acc_ref[0:lon_cells, :] + total

        @pl.when(step == steps - 1)
        def _():
            fold_ref[...] = jnp.zeros(fold_ref.shape, fold_ref.dtype)
            for part in range(parts):
                width = min(128, lat_cells - part * 128)
                fold_ref[part * padded:(part + 1) * padded, 0:width] = acc_ref[
                    :, part * 128:part * 128 + width
                ]
            pieces = split3(fold_ref[...])
            key_ids = lax.broadcasted_iota(jnp.int32, (parts * padded, slots), 0)
            for row in range(sources):
                keys, onehot = cell_keys(cells_ref[row, 2:3, :], padded, lat_cells)
                at_keys = jnp.dot(pieces[0], onehot, preferred_element_type=jnp.float32)
                at_keys = at_keys + jnp.dot(pieces[1], onehot, preferred_element_type=jnp.float32)
                at_keys = at_keys + jnp.dot(pieces[2], onehot, preferred_element_type=jnp.float32)
                out_ref[row:row + 1, :] = jnp.sum(
                    jnp.where(key_ids == keys, at_keys, 0.0), axis=0, keepdims=True
                )

    field = pl.BlockSpec((chunk, None, lon_cells, lat_cells), lambda g: (g, 0, 0, 0))
    halo = pl.BlockSpec((chunk, None, radius, lat_cells), lambda g: (g, 0, 0, 0))
    whole = lambda shape: pl.BlockSpec(shape, lambda g: (0,) * len(shape))
    return pl.pallas_call(
        kernel,
        grid=(steps,),
        in_specs=[
            field,
            halo,
            halo,
            field,
            whole(band_lon.shape),
            whole(band_lat.shape),
            whole(cells.shape),
        ],
        out_specs=whole((sources, slots)),
        out_shape=jax.ShapeDtypeStruct((sources, slots), jnp.float32),
        scratch_shapes=[
            pltpu.VMEM((ext_cells, lat_cells), jnp.bfloat16),
            pltpu.VMEM((chunk * padded, lat_cells), jnp.bfloat16),
            pltpu.VMEM((padded, lat_cells), jnp.float32),
            pltpu.VMEM((parts * padded, 128), jnp.float32),
        ],
        compiler_params=pltpu.CompilerParams(dimension_semantics=("arbitrary",)),
    )(control, c_low, c_high, perturb, band_lon, band_lat, cells)


def spread_misfits(partials, lists, lon_cells, lat_cells, radius, padded):
    sources, _, slots = lists.shape
    parts = -(-lat_cells // 128)

    def kernel(*refs):
        part_refs = refs[:len(partials)]
        lists_ref, spread_ref, low_ref, high_ref, fold_ref = refs[len(partials):]
        at_cells = part_refs[0][...]
        for ref in part_refs[1:]:
            at_cells = at_cells + ref[...]
        key_ids = lax.broadcasted_iota(jnp.int32, (parts * padded, slots), 0)
        folded = jnp.zeros((parts * padded, 128), jnp.float32)
        for row in range(sources):
            misfit = lists_ref[row, 1:2, :] * (
                at_cells[row:row + 1, :] - lists_ref[row, 0:1, :]
            )
            keys, onehot = cell_keys(lists_ref[row, 2:3, :], padded, lat_cells)
            for piece in split3(misfit):
                weighted = jnp.where(key_ids == keys, piece.astype(jnp.float32), 0.0)
                folded = folded + lax.dot_general(
                    weighted.astype(jnp.bfloat16),
                    onehot,
                    (((1,), (1,)), ((), ())),
                    preferred_element_type=jnp.float32,
                )
        for part in range(parts):
            width = min(128, lat_cells - part * 128)
            fold_ref[:, part * 128:part * 128 + width] = folded[
                part * padded:(part + 1) * padded, 0:width
            ]
        spread_ref[...] = fold_ref[0:lon_cells, :]
        low_ref[...] = fold_ref[lon_cells - radius:lon_cells, :]
        high_ref[...] = fold_ref[0:radius, :]

    return pl.pallas_call(
        kernel,
        out_shape=(
            jax.ShapeDtypeStruct((lon_cells, lat_cells), jnp.float32),
            jax.ShapeDtypeStruct((radius, lat_cells), jnp.float32),
            jax.ShapeDtypeStruct((radius, lat_cells), jnp.float32),
        ),
        scratch_shapes=[pltpu.VMEM((padded, lat_cells), jnp.float32)],
    )(*partials, lists)


def backward_grad(perturb, p_low, p_high, spread, s_low, s_high, control, band_lon, band_lat):
    members, levels, lon_cells, lat_cells = control.shape
    radius = p_low.shape[2]
    padded, ext_cells = band_lon.shape
    chunk = members

    def kernel(pert_ref, plow_ref, phigh_ref, spread_ref, slow_ref, shigh_ref, ctrl_ref,
               blon_ref, blat_ref, out_ref, ext_ref, along_ref):
        blon = blon_ref[...]
        spread = spread_ref[...]
        s_lo = slow_ref[...]
        s_hi = shigh_ref[...]
        for m in range(chunk):
            fill_ext(
                ext_ref,
                (pert_ref[m].astype(jnp.float32) * spread).astype(jnp.bfloat16),
                (plow_ref[m].astype(jnp.float32) * s_lo).astype(jnp.bfloat16),
                (phigh_ref[m].astype(jnp.float32) * s_hi).astype(jnp.bfloat16),
                lon_cells,
                padded,
            )
            along = jnp.dot(blon, ext_ref[...], preferred_element_type=jnp.float32)
            along_ref[m * padded:(m + 1) * padded, :] = along.astype(jnp.bfloat16)
        smoothed = lat_conv(along_ref, blat_ref, radius)
        for m in range(chunk):
            out_ref[m] = ctrl_ref[m].astype(jnp.float32) + smoothed[
                m * padded:m * padded + lon_cells
            ]

    field = pl.BlockSpec((chunk, None, lon_cells, lat_cells), lambda l, g: (g, l, 0, 0))
    halo = pl.BlockSpec((chunk, None, radius, lat_cells), lambda l, g: (g, l, 0, 0))
    level_field = pl.BlockSpec((None, lon_cells, lat_cells), lambda l, g: (l, 0, 0))
    level_halo = pl.BlockSpec((None, radius, lat_cells), lambda l, g: (l, 0, 0))
    out = pl.pallas_call(
        kernel,
        grid=(levels, members // chunk),
        in_specs=[
            field,
            halo,
            halo,
            level_field,
            level_halo,
            level_halo,
            field,
            pl.BlockSpec(band_lon.shape, lambda l, g: (0, 0)),
            pl.BlockSpec(band_lat.shape, lambda l, g: (0, 0)),
        ],
        out_specs=pl.BlockSpec((chunk, lon_cells, None, lat_cells), lambda l, g: (g, 0, l, 0)),
        out_shape=jax.ShapeDtypeStruct((members, lon_cells, levels, lat_cells), jnp.float32),
        scratch_shapes=[
            pltpu.VMEM((ext_cells, lat_cells), jnp.bfloat16),
            pltpu.VMEM((chunk * padded, lat_cells), jnp.bfloat16),
        ],
        compiler_params=pltpu.CompilerParams(dimension_semantics=("arbitrary", "arbitrary")),
    )(perturb, p_low, p_high, spread, s_low, s_high, control, band_lon, band_lat)
    return jnp.transpose(out, (0, 2, 1, 3))


def local(control, perturb, lon_taps, lat_taps, innov, inv_var, cell_index, counts):
    members_here, levels, lon_cells, lat_cells = control.shape
    radius = lon_taps.shape[0] - 1
    padded = -(-lon_cells // 16) * 16
    band_lon, band_lat = build_bands(lon_taps, lat_taps, lon_cells, padded, lat_cells)

    slot_ids = lax.broadcasted_iota(jnp.int32, innov.shape, 2)
    weights = jnp.where(slot_ids < counts[:, :, None], inv_var, 0.0)
    lists = jnp.stack([innov[0], weights[0], cell_index[0].astype(jnp.float32)], axis=1)
    lists = lax.optimization_barrier((lists, band_lon, band_lat))[0]
    received = lax.all_to_all(lists, "tile", split_axis=0, concat_axis=0, tiled=True)

    c_low, c_high = halos(control, "tile", 2, radius)
    c_low, c_high, received = lax.optimization_barrier((c_low, c_high, received))
    late_perturb = lax.optimization_barrier((perturb, c_low, c_high))[0]
    p_low, p_high = halos(late_perturb, "tile", 2, radius)
    partial = forward_pick(
        control, c_low, c_high, perturb, band_lon, band_lat, received
    )
    partials = gather_over(partial, "mem")
    spread, low_send, high_send = spread_misfits(
        partials, received, lon_cells, lat_cells, radius, padded
    )
    count = lax.axis_size("tile")
    s_low = lax.ppermute(low_send, "tile", [(i, (i + 1) % count) for i in range(count)])
    s_high = lax.ppermute(high_send, "tile", [((i + 1) % count, i) for i in range(count)])
    return backward_grad(
        perturb,
        p_low,
        p_high,
        spread[None],
        s_low[None],
        s_high[None],
        control,
        band_lon,
        band_lat,
    )


def solution(mesh):
    return jax.shard_map(
        local,
        mesh=mesh,
        in_specs=(
            P("mem", None, "tile", None),
            P("mem", None, "tile", None),
            P(),
            P(),
            P("tile", None, None),
            P("tile", None, None),
            P("tile", None, None),
            P("tile", None),
        ),
        out_specs=P("mem", None, "tile", None),
        check_vma=False,
    )
```

```python
import math

import jax
import jax.numpy as jnp
from jax import lax
from jax.experimental import pallas as pl
from jax.experimental.pallas import tpu as pltpu
from jax.sharding import PartitionSpec as P


def halos(block, axis, dim, width):
    count = lax.axis_size(axis)
    forward = [(i, (i + 1) % count) for i in range(count)]
    backward = [((i + 1) % count, i) for i in range(count)]
    low = lax.ppermute(
        lax.slice_in_dim(block, block.shape[dim] - width, None, axis=dim), axis, forward
    )
    high = lax.ppermute(lax.slice_in_dim(block, 0, width, axis=dim), axis, backward)
    return low, high


def gather_over(values, axis):
    count = lax.axis_size(axis)
    return [values] + [
        lax.ppermute(values, axis, [(i, (i + shift) % count) for i in range(count)])
        for shift in range(1, count)
    ]


def select_chain(dist, taps_ref):
    band = jnp.zeros(dist.shape, jnp.float32)
    for offset in range(taps_ref.shape[0]):
        band = jnp.where(dist == offset, taps_ref[offset], band)
    return band.astype(jnp.bfloat16)


def build_bands(lon_taps, lat_taps, lon_cells, padded, lat_cells):
    radius = lon_taps.shape[0] - 1
    ext_cells = padded + 2 * radius
    tile = 128
    tiles = -(-lat_cells // tile)

    def kernel(lon_ref, lat_ref, blon_ref, blat_ref):
        rows = lax.broadcasted_iota(jnp.int32, (padded, ext_cells), 0)
        cols = lax.broadcasted_iota(jnp.int32, (padded, ext_cells), 1)
        source = jnp.where(
            cols < padded,
            cols,
            jnp.where(
                cols < padded + radius,
                cols - padded - radius,
                cols - padded - radius + lon_cells,
            ),
        )
        valid = (rows < lon_cells) & ((cols < lon_cells) | (cols >= padded))
        dist = jnp.where(valid, jnp.abs(source - rows), radius + 1)
        blon_ref[...] = select_chain(dist, lon_ref)

        t_rows = lax.broadcasted_iota(jnp.int32, (tile, tile), 0)
        t_cols = lax.broadcasted_iota(jnp.int32, (tile, tile), 1)
        blocks = {
            shift: select_chain(jnp.abs(t_rows - t_cols + shift * tile), lat_ref)
            for shift in (-1, 0, 1)
        }
        blat_ref[...] = jnp.zeros(blat_ref.shape, blat_ref.dtype)
        for a in range(tiles):
            for b in (a - 1, a, a + 1):
                if b < 0 or b >= tiles:
                    continue
                height = min(tile, lat_cells - a * tile)
                width = min(tile, lat_cells - b * tile)
                blat_ref[a * tile:a * tile + height, b * tile:b * tile + width] = blocks[a - b][
                    :height, :width
                ]

    smem = pl.BlockSpec(memory_space=pltpu.SMEM)
    band_lon, band_lat = pl.pallas_call(
        kernel,
        in_specs=[smem, smem],
        out_shape=(
            jax.ShapeDtypeStruct((padded, ext_cells), jnp.bfloat16),
            jax.ShapeDtypeStruct((lat_cells, lat_cells), jnp.bfloat16),
        ),
    )(lon_taps.astype(jnp.float32), lat_taps.astype(jnp.float32))
    windows = tuple(
        band_lat[low:high, start:stop] for start, stop, low, high in lat_windows(lat_cells, radius)
    )
    return band_lon, windows


def lat_windows(lat_cells, radius):
    out = []
    for start in range(0, lat_cells, 256):
        stop = min(lat_cells, start + 256)
        low = max(0, (start - radius) // 128 * 128)
        high = min(lat_cells, -(-(stop + radius) // 128) * 128)
        out.append((start, stop, low, high))
    return out


def member_chunk(members):
    for size in (10, 8, 5, 4, 3, 2, 1):
        if members % size == 0:
            return size
    return 1


def lat_conv(along_ref, window_refs, radius):
    lat_cells = along_ref.shape[1]
    blocks = [
        jnp.dot(along_ref[:, low:high], ref[...], preferred_element_type=jnp.float32)
        for (start, stop, low, high), ref in zip(lat_windows(lat_cells, radius), window_refs)
    ]
    return jnp.concatenate(blocks, axis=1) if len(blocks) > 1 else blocks[0]


def fill_ext(ext_ref, local, low, high, lon_cells, padded):
    radius = low.shape[0]
    base = (lon_cells // 16) * 16
    ext_ref[base:padded, :] = jnp.zeros((padded - base, ext_ref.shape[1]), ext_ref.dtype)
    ext_ref[0:lon_cells, :] = local
    ext_ref[padded:padded + radius, :] = low
    ext_ref[padded + radius:padded + 2 * radius, :] = high


def split3(values):
    hi = values.astype(jnp.bfloat16)
    rest = values - hi.astype(jnp.float32)
    mid = rest.astype(jnp.bfloat16)
    lo = (rest - mid.astype(jnp.float32)).astype(jnp.bfloat16)
    return hi, mid, lo


def cell_keys(cells, padded, lat_cells):
    rows = jnp.floor((cells + 0.5) / lat_cells)
    cols = (cells - rows * lat_cells).astype(jnp.int32)
    keys = (cols // 128) * padded + rows.astype(jnp.int32)
    lane_ids = lax.broadcasted_iota(jnp.int32, (128, cells.shape[1]), 0)
    onehot = jnp.where(lane_ids == cols % 128, 1.0, 0.0).astype(jnp.bfloat16)
    return keys, onehot


def forward_pick(control, c_low, c_high, perturb, band_lon, band_lat, cells):
    members, levels, lon_cells, lat_cells = control.shape
    radius = c_low.shape[2]
    padded, ext_cells = band_lon.shape
    chunk = member_chunk(members)
    steps = members // chunk
    sources, _, slots = cells.shape
    parts = -(-lat_cells // 128)

    count = len(band_lat)

    def kernel(ctrl_ref, low_ref, high_ref, pert_ref, blon_ref, *refs):
        blat_refs = refs[:count]
        cells_ref, out_ref, ext_ref, along_ref, acc_ref, fold_ref = refs[count:]
        step = pl.program_id(0)
        blon = blon_ref[...]
        for m in range(chunk):
            fill_ext(ext_ref, ctrl_ref[m], low_ref[m], high_ref[m], lon_cells, padded)
            along = jnp.dot(blon, ext_ref[...], preferred_element_type=jnp.float32)
            along_ref[m * padded:(m + 1) * padded, :] = along.astype(jnp.bfloat16)
        smoothed = lat_conv(along_ref, blat_refs, radius)
        total = pert_ref[0].astype(jnp.float32) * smoothed[0:lon_cells]
        for m in range(1, chunk):
            total = total + pert_ref[m].astype(jnp.float32) * smoothed[
                m * padded:m * padded + lon_cells
            ]

        @pl.when(step == 0)
        def _():
            acc_ref[...] = jnp.zeros(acc_ref.shape, acc_ref.dtype)

        acc_ref[0:lon_cells, :] = acc_ref[0:lon_cells, :] + total

        @pl.when(step == steps - 1)
        def _():
            fold_ref[...] = jnp.zeros(fold_ref.shape, fold_ref.dtype)
            for part in range(parts):
                width = min(128, lat_cells - part * 128)
                fold_ref[part * padded:(part + 1) * padded, 0:width] = acc_ref[
                    :, part * 128:part * 128 + width
                ]
            pieces = split3(fold_ref[...])
            key_ids = lax.broadcasted_iota(jnp.int32, (parts * padded, slots), 0)
            for row in range(sources):
                keys, onehot = cell_keys(cells_ref[row, 2:3, :], padded, lat_cells)
                at_keys = jnp.dot(pieces[0], onehot, preferred_element_type=jnp.float32)
                at_keys = at_keys + jnp.dot(pieces[1], onehot, preferred_element_type=jnp.float32)
                at_keys = at_keys + jnp.dot(pieces[2], onehot, preferred_element_type=jnp.float32)
                out_ref[row:row + 1, :] = jnp.sum(
                    jnp.where(key_ids == keys, at_keys, 0.0), axis=0, keepdims=True
                )

    field = pl.BlockSpec((chunk, None, lon_cells, lat_cells), lambda g: (g, 0, 0, 0))
    halo = pl.BlockSpec((chunk, None, radius, lat_cells), lambda g: (g, 0, 0, 0))
    whole = lambda shape: pl.BlockSpec(shape, lambda g: (0,) * len(shape))
    return pl.pallas_call(
        kernel,
        grid=(steps,),
        in_specs=[
            field,
            halo,
            halo,
            field,
            whole(band_lon.shape),
        ] + [whole(w.shape) for w in band_lat] + [

            whole(cells.shape),
        ],
        out_specs=whole((sources, slots)),
        out_shape=jax.ShapeDtypeStruct((sources, slots), jnp.float32),
        scratch_shapes=[
            pltpu.VMEM((ext_cells, lat_cells), jnp.bfloat16),
            pltpu.VMEM((chunk * padded, lat_cells), jnp.bfloat16),
            pltpu.VMEM((padded, lat_cells), jnp.float32),
            pltpu.VMEM((parts * padded, 128), jnp.float32),
        ],
        compiler_params=pltpu.CompilerParams(dimension_semantics=("arbitrary",)),
    )(control, c_low, c_high, perturb, band_lon, *band_lat, cells)


def spread_misfits(partials, lists, lon_cells, lat_cells, radius, padded):
    sources, _, slots = lists.shape
    parts = -(-lat_cells // 128)

    def kernel(*refs):
        part_refs = refs[:len(partials)]
        lists_ref, spread_ref, low_ref, high_ref, fold_ref = refs[len(partials):]
        at_cells = part_refs[0][...]
        for ref in part_refs[1:]:
            at_cells = at_cells + ref[...]
        key_ids = lax.broadcasted_iota(jnp.int32, (parts * padded, slots), 0)
        folded = jnp.zeros((parts * padded, 128), jnp.float32)
        for row in range(sources):
            misfit = lists_ref[row, 1:2, :] * (
                at_cells[row:row + 1, :] - lists_ref[row, 0:1, :]
            )
            keys, onehot = cell_keys(lists_ref[row, 2:3, :], padded, lat_cells)
            for piece in split3(misfit):
                weighted = jnp.where(key_ids == keys, piece.astype(jnp.float32), 0.0)
                folded = folded + lax.dot_general(
                    weighted.astype(jnp.bfloat16),
                    onehot,
                    (((1,), (1,)), ((), ())),
                    preferred_element_type=jnp.float32,
                )
        for part in range(parts):
            width = min(128, lat_cells - part * 128)
            fold_ref[:, part * 128:part * 128 + width] = folded[
                part * padded:(part + 1) * padded, 0:width
            ]
        spread_ref[...] = fold_ref[0:lon_cells, :]
        low_ref[...] = fold_ref[lon_cells - radius:lon_cells, :]
        high_ref[...] = fold_ref[0:radius, :]

    return pl.pallas_call(
        kernel,
        out_shape=(
            jax.ShapeDtypeStruct((lon_cells, lat_cells), jnp.float32),
            jax.ShapeDtypeStruct((radius, lat_cells), jnp.float32),
            jax.ShapeDtypeStruct((radius, lat_cells), jnp.float32),
        ),
        scratch_shapes=[pltpu.VMEM((padded, lat_cells), jnp.float32)],
    )(*partials, lists)


def backward_grad(perturb, p_low, p_high, spread, s_low, s_high, control, band_lon, band_lat):
    members, levels, lon_cells, lat_cells = control.shape
    radius = p_low.shape[2]
    padded, ext_cells = band_lon.shape
    chunk = member_chunk(members)

    count = len(band_lat)

    def kernel(pert_ref, plow_ref, phigh_ref, spread_ref, slow_ref, shigh_ref, ctrl_ref,
               blon_ref, *refs):
        blat_refs = refs[:count]
        out_ref, ext_ref, along_ref = refs[count:]
        blon = blon_ref[...]
        spread = spread_ref[...]
        s_lo = slow_ref[...]
        s_hi = shigh_ref[...]
        for m in range(chunk):
            fill_ext(
                ext_ref,
                (pert_ref[m].astype(jnp.float32) * spread).astype(jnp.bfloat16),
                (plow_ref[m].astype(jnp.float32) * s_lo).astype(jnp.bfloat16),
                (phigh_ref[m].astype(jnp.float32) * s_hi).astype(jnp.bfloat16),
                lon_cells,
                padded,
            )
            along = jnp.dot(blon, ext_ref[...], preferred_element_type=jnp.float32)
            along_ref[m * padded:(m + 1) * padded, :] = along.astype(jnp.bfloat16)
        smoothed = lat_conv(along_ref, blat_refs, radius)
        for m in range(chunk):
            out_ref[m] = ctrl_ref[m].astype(jnp.float32) + smoothed[
                m * padded:m * padded + lon_cells
            ]

    field = pl.BlockSpec((chunk, None, lon_cells, lat_cells), lambda l, g: (g, l, 0, 0))
    halo = pl.BlockSpec((chunk, None, radius, lat_cells), lambda l, g: (g, l, 0, 0))
    level_field = pl.BlockSpec((None, lon_cells, lat_cells), lambda l, g: (l, 0, 0))
    level_halo = pl.BlockSpec((None, radius, lat_cells), lambda l, g: (l, 0, 0))
    out = pl.pallas_call(
        kernel,
        grid=(levels, members // chunk),
        in_specs=[
            field,
            halo,
            halo,
            level_field,
            level_halo,
            level_halo,
            field,
            pl.BlockSpec(band_lon.shape, lambda l, g: (0, 0)),
        ] + [pl.BlockSpec(w.shape, lambda l, g: (0, 0)) for w in band_lat] + [
        ],
        out_specs=pl.BlockSpec((chunk, lon_cells, None, lat_cells), lambda l, g: (g, 0, l, 0)),
        out_shape=jax.ShapeDtypeStruct((members, lon_cells, levels, lat_cells), jnp.float32),
        scratch_shapes=[
            pltpu.VMEM((ext_cells, lat_cells), jnp.bfloat16),
            pltpu.VMEM((chunk * padded, lat_cells), jnp.bfloat16),
        ],
        compiler_params=pltpu.CompilerParams(dimension_semantics=("arbitrary", "arbitrary")),
    )(perturb, p_low, p_high, spread, s_low, s_high, control, band_lon, *band_lat)
    return jnp.transpose(out, (0, 2, 1, 3))


def local(control, perturb, lon_taps, lat_taps, innov, inv_var, cell_index, counts):
    members_here, levels, lon_cells, lat_cells = control.shape
    radius = lon_taps.shape[0] - 1
    padded = -(-lon_cells // 16) * 16
    band_lon, band_lat = build_bands(lon_taps, lat_taps, lon_cells, padded, lat_cells)

    slot_ids = lax.broadcasted_iota(jnp.int32, innov.shape, 2)
    weights = jnp.where(slot_ids < counts[:, :, None], inv_var, 0.0)
    lists = jnp.stack([innov[0], weights[0], cell_index[0].astype(jnp.float32)], axis=1)
    lists = lax.optimization_barrier((lists, band_lon, band_lat))[0]
    received = lax.all_to_all(lists, "tile", split_axis=0, concat_axis=0, tiled=True)

    c_low, c_high = halos(control, "tile", 2, radius)
    c_low, c_high, received = lax.optimization_barrier((c_low, c_high, received))
    late_perturb = lax.optimization_barrier((perturb, c_low, c_high))[0]
    p_low, p_high = halos(late_perturb, "tile", 2, radius)
    partial = forward_pick(
        control, c_low, c_high, perturb, band_lon, band_lat, received
    )
    partials = gather_over(partial, "mem")
    spread, low_send, high_send = spread_misfits(
        partials, received, lon_cells, lat_cells, radius, padded
    )
    count = lax.axis_size("tile")
    s_low = lax.ppermute(low_send, "tile", [(i, (i + 1) % count) for i in range(count)])
    s_high = lax.ppermute(high_send, "tile", [((i + 1) % count, i) for i in range(count)])
    return backward_grad(
        perturb,
        p_low,
        p_high,
        spread[None],
        s_low[None],
        s_high[None],
        control,
        band_lon,
        band_lat,
    )


def solution(mesh):
    return jax.shard_map(
        local,
        mesh=mesh,
        in_specs=(
            P("mem", None, "tile", None),
            P("mem", None, "tile", None),
            P(),
            P(),
            P("tile", None, None),
            P("tile", None, None),
            P("tile", None, None),
            P("tile", None),
        ),
        out_specs=P("mem", None, "tile", None),
        check_vma=False,
    )
```
